32 devices in a mesh: parts: 2 (over x), wide: 16 (over z, y, core).
Axes of the slice: x: 2, y: 2, z: 4, core: 2. Of those that a mesh axis runs over, the one named last changes fastest.
Arguments:
- frames: float32 [65536, 80], P(('parts', 'wide')), parts along dimension 0, may hold values from -6 to 6
- seg_start: int32 [2048], P(('parts', 'wide')), parts along dimension 0, may hold values from 1 to 1983
- seg_dest: int32 [2048], P(('parts', 'wide')), parts along dimension 0, may hold values from -1 to 15, as said below
- rec_id: int32 [2048], P(('parts', 'wide')), parts along dimension 0, may hold values from 0 to 63
- conv_weight: float32 [240, 1024], replicated, may hold values from -0.375 to 0.375
- conv_bias: float32 [1024], replicated, may hold values from -0.5 to 0.5
- proj_weight: float32 [2048, 192], replicated, may hold values from -0.125 to 0.125
- smooth_kernel: float32 [3, 3], replicated, may hold values from 0.2 to 1
Outputs:
- smoothed: float32 [1024, 512], P(('parts', 'wide')), parts along dimension 0
The draws below stay inside these ranges and needn't reach their ends.
There are 2 independent parts, one for each index of `parts`. The reference program is written for one: setup_inputs(seed, part) draws one part's arguments, and reference() takes and returns one part's arrays. A program takes and returns all parts, laid end to end along the dimension named above; an argument that names none is the same for every part. Nothing has to cross between parts.
Inputs may be any that keep to these rules, and one draw needn't show every extreme that they name: `seg_dest`: -1 marks an unused slot; on each device the used slots come first; at most 4 segments of one device go to one device, and some device reaches this; every device is assigned exactly 32 segments.
All inputs are finite; a program needn't handle non-finite values.
Results may differ from the reference program's by a relative error of at most 0.001.
Values may be sent and summed in bfloat16 or wider, within the bound.
No kernel may reach another device: no remote copies, remote signals or barrier semaphores. Data moves between devices by JAX's collectives and lax.ppermute only.
A program may use at most 64 MiB of HBM per device.

```python
import math
import jax
import jax.numpy as jnp
from jax import lax

FEAT = 80
CH = 1024
EMB = 192
SEGLEN = 64
SEG_DEV = 32
F_DEV = 2048
SEG_CAP = 64
TOTAL = 512
SLOTS = 1024
FRAMES = 32768
RECS = 64
N_WIDE = 16


def draw_seg_dest(key, part):
    half_count = N_WIDE // 2
    shuffle = jax.random.permutation(jax.random.fold_in(key, 101), N_WIDE).astype(jnp.int32)
    swings = jax.random.randint(jax.random.fold_in(key, 102), (half_count,), 0, SEG_DEV + 1).astype(jnp.int32)
    swings = swings.at[0].set(SEG_DEV)
    seg_counts = jnp.zeros((N_WIDE,), jnp.int32)
    seg_counts = seg_counts.at[shuffle[:half_count]].set(SEG_DEV + swings)
    seg_counts = seg_counts.at[shuffle[half_count:]].set(SEG_DEV - swings)
    offsets = jnp.cumsum(seg_counts) - seg_counts
    slot_pos = jnp.arange(SEG_CAP, dtype=jnp.int32)
    global_pos = offsets[:, None] + slot_pos[None, :]
    targets = jax.random.permutation(jax.random.fold_in(key, 103), N_WIDE).astype(jnp.int32)
    rotation = jax.random.randint(jax.random.fold_in(key, 104), (), 0, N_WIDE).astype(jnp.int32)
    destined = targets[(global_pos + rotation) % N_WIDE]
    marked = jnp.where(slot_pos[None, :] < seg_counts[:, None], destined, -1)
    return marked.reshape(N_WIDE * SEG_CAP).astype(jnp.int32)


def touch_ends(values, key, low, largest):
    longest = values.shape.index(max(values.shape))
    spots = []
    for shift in (0, 1):
        where = [jax.random.randint(jax.random.fold_in(key, axis), (), 0, length) for axis, length in enumerate(values.shape)]
        where[longest] = (where[longest] + shift) % values.shape[longest]
        spots.append(tuple(where))
    return values.at[spots[0]].set(low).at[spots[1]].set(largest)


def level_of(rng, shape, cuts, smallest, high):
    factor_of = 1.0
    for dim, parts in cuts:
        steps = jax.random.uniform(jax.random.fold_in(jax.random.fold_in(rng, 6), dim), (parts,), jnp.float32, smallest / len(cuts), high / len(cuts))
        factor_of = factor_of * jnp.repeat(jnp.exp(steps), shape[dim] // parts).reshape((-1,) + (1,) * (len(shape) - 1 - dim))
    return factor_of


def normal_values(own_key, dims, scale, most, pieces=(), kind=jnp.bfloat16):
    drawn = jax.random.normal(own_key, dims, jnp.float32) * scale
    if len(pieces) > 0:
        drawn = level_of(own_key, dims, pieces, -0.22, 0.18) * drawn
    return jnp.clip(drawn, min=-most, max=most).astype(kind)


def setup_inputs(seed: int = 0, part: int = 0) -> dict:
    arg_keys = jax.random.split(jax.random.key(seed), 9)
    part_splits = jax.random.split(jax.random.fold_in(arg_keys[8], part), 9)
    frames = normal_values(part_splits[0], (FRAMES, FEAT), 1.0, 6.0, ((0, 16),), jnp.float32)
    seg_start = touch_ends(jax.random.randint(part_splits[1], (SLOTS,), 1, F_DEV - SEGLEN), jax.random.fold_in(part_splits[1], 1), 1, (F_DEV - SEGLEN) - 1).astype(jnp.int32)
    seg_dest = draw_seg_dest(jax.random.fold_in(jax.random.fold_in(arg_keys[8], part), 71), part)
    rec_id = touch_ends(jax.random.randint(part_splits[3], (SLOTS,), 0, RECS), jax.random.fold_in(part_splits[3], 1), 0, RECS - 1).astype(jnp.int32)
    conv_weight = normal_values(arg_keys[4], (3 * FEAT, CH), (3 * FEAT) ** -0.5, 0.375, (), jnp.float32)
    conv_bias = jnp.clip(jax.random.uniform(arg_keys[5], (CH,), jnp.float32, -0.5, 0.5), -0.5, 0.5)
    proj_weight = normal_values(arg_keys[6], (2 * CH, EMB), (2 * CH) ** -0.5, 0.125, (), jnp.float32)
    smooth_kernel = jnp.clip(jax.random.uniform(arg_keys[7], (3, 3), jnp.float32, 0.2, 1.0), 0.2, 1.0)
    return dict(frames=frames, seg_start=seg_start, seg_dest=seg_dest, rec_id=rec_id, conv_weight=conv_weight, conv_bias=conv_bias, proj_weight=proj_weight, smooth_kernel=smooth_kernel)


PRECISE = lax.Precision.HIGHEST
AFF_SCALE = 8.0

def pool_segments(windows, conv_weight, conv_bias, proj_weight):
    seg_total = windows.shape[0]
    block_size = math.gcd(seg_total, 16)
    grouped = windows.reshape(seg_total // block_size, block_size, SEGLEN + 2, FEAT)

    def one_block(win_block):
        stacked = jnp.concatenate([win_block[:, 0:SEGLEN], win_block[:, 1:SEGLEN + 1], win_block[:, 2:SEGLEN + 2]], axis=2)
        preact = jnp.dot(stacked.reshape(block_size * SEGLEN, 3 * FEAT), conv_weight, precision=PRECISE, preferred_element_type=jnp.float32)
        activated = jax.nn.relu(preact + conv_bias).reshape(block_size, SEGLEN, CH)
        frame_mean = lax.optimization_barrier(jnp.mean(activated, axis=1))
        deviation = activated - frame_mean[:, None, :]
        frame_std = jnp.sqrt(lax.optimization_barrier(jnp.mean(deviation * deviation, axis=1)) + 1e-05)
        return jnp.concatenate([frame_mean, frame_std], axis=1)
    pooled = lax.map(one_block, grouped).reshape(seg_total, 2 * CH)
    return jnp.dot(pooled, proj_weight, precision=PRECISE, preferred_element_type=jnp.float32)

def smooth_rows(padded_rows, smooth_kernel):
    padded = jnp.pad(padded_rows, ((0, 0), (1, 1)))
    height = padded.shape[0] - 2
    col_count = padded.shape[1] - 2
    result = jnp.zeros((height, col_count), padded.dtype)
    for row_off in range(3):
        for col_off in range(3):
            result = result + smooth_kernel[row_off, col_off] * padded[row_off:row_off + height, col_off:col_off + col_count]
    return result

def reference(frames, seg_start, seg_dest, rec_id, conv_weight, conv_bias, proj_weight, smooth_kernel):
    slot_ids = jnp.arange(SLOTS, dtype=jnp.int32)
    sort_key = jnp.where(seg_dest >= 0, seg_dest * SLOTS + slot_ids, N_WIDE * SLOTS).astype(jnp.int32)
    chosen = jnp.argsort(sort_key, stable=True)[:TOTAL].astype(jnp.int32)
    first_row = (chosen // SEG_CAP * F_DEV + seg_start[chosen] - 1).astype(jnp.int32)

    def cut_one(row_start):
        return lax.dynamic_slice_in_dim(frames, row_start, SEGLEN + 2, 0)
    block_rows = math.gcd(TOTAL, 64)

    def embed_block(starts):
        windows = jax.vmap(cut_one)(starts)
        return pool_segments(windows, conv_weight, conv_bias, proj_weight)
    embedded = lax.map(embed_block, first_row.reshape(TOTAL // block_rows, block_rows)).reshape(TOTAL, EMB)
    row_rec = rec_id[chosen]
    centred = embedded - lax.optimization_barrier(jnp.sum(embedded, axis=0)) / TOTAL
    unit = (centred / jnp.sqrt(lax.optimization_barrier(jnp.sum(centred * centred, axis=1, keepdims=True)) + 1e-06)).astype(jnp.bfloat16)
    affinity = AFF_SCALE * jnp.dot(unit, unit.T, preferred_element_type=jnp.float32)
    affinity = jnp.where(row_rec[:, None] == row_rec[None, :], 0.0, affinity)
    padded = jnp.pad(affinity, ((1, 1), (0, 0)))
    return smooth_rows(padded, smooth_kernel)
```

```python
import functools

import jax
import jax.numpy as jnp
from jax import lax
from jax.experimental import pallas as pl
from jax.experimental.pallas import tpu as pltpu
from jax.sharding import PartitionSpec as P

FEAT = 80
CH = 1024
EMB = 192
SEGLEN = 64
SEG_DEV = 32


PRECISE = lax.Precision.HIGHEST
AFF_SCALE = 8.0
SEG_BLOCK = 8
WIN = SEGLEN + 8


def _pool_kernel(starts_ref, x3_hbm, w_ref, b_ref, out_ref, buf, sem):
    step = pl.program_id(0)
    steps = pl.num_programs(0)
    block = buf.shape[1]
    rows = x3_hbm.shape[0]

    def aligned_start(blk, j):
        start = starts_ref[blk * block + j]
        return jnp.minimum((start // 8) * 8, rows - WIN)

    def window_copy(blk, slot, j):
        base = pl.multiple_of(aligned_start(blk, j), 8)
        return pltpu.make_async_copy(
            x3_hbm.at[pl.ds(base, WIN)], buf.at[slot, j], sem.at[slot, j]
        )

    @pl.when(step == 0)
    def _():
        for j in range(block):
            window_copy(0, 0, j).start()

    slot = step % 2

    @pl.when(step + 1 < steps)
    def _():
        for j in range(block):
            window_copy(step + 1, 1 - slot, j).start()

    for j in range(block):
        window_copy(step, slot, j).wait()

    stacked = buf[slot].reshape(block * WIN, 3 * FEAT)
    preact = jnp.dot(stacked, w_ref[...], precision=PRECISE, preferred_element_type=jnp.float32)
    activated = jnp.maximum(preact + b_ref[...], 0.0)
    frame_idx = lax.broadcasted_iota(jnp.int32, (WIN, CH), 0)
    means = []
    stds = []
    for j in range(block):
        shift = starts_ref[step * block + j] - aligned_start(step, j)
        inside = (frame_idx >= shift) & (frame_idx < shift + SEGLEN)
        seg_act = activated[j * WIN : (j + 1) * WIN]
        frame_mean = jnp.sum(jnp.where(inside, seg_act, 0.0), axis=0, keepdims=True) / SEGLEN
        deviation = jnp.where(inside, seg_act - frame_mean, 0.0)
        frame_var = jnp.sum(deviation * deviation, axis=0, keepdims=True) / SEGLEN
        means.append(frame_mean)
        stds.append(jnp.sqrt(frame_var + 1e-05))
    out_ref[:, :CH] = jnp.concatenate(means, axis=0)
    out_ref[:, CH:] = jnp.concatenate(stds, axis=0)


def pool_slots(frames, seg_start, conv_weight, conv_bias):
    rows = frames.shape[0]
    slots = seg_start.shape[0]
    zero = jnp.zeros((1, FEAT), frames.dtype)
    x3 = jnp.concatenate(
        [
            jnp.concatenate([zero, frames[:-1]], axis=0),
            frames,
            jnp.concatenate([frames[1:], zero], axis=0),
        ],
        axis=1,
    )
    starts = jnp.clip(seg_start, 0, rows - SEGLEN).astype(jnp.int32)
    block = SEG_BLOCK if slots % SEG_BLOCK == 0 else 1
    grid_spec = pltpu.PrefetchScalarGridSpec(
        num_scalar_prefetch=1,
        grid=(slots // block,),
        in_specs=[
            pl.BlockSpec(memory_space=pl.ANY),
            pl.BlockSpec((3 * FEAT, CH), lambda i, s: (0, 0)),
            pl.BlockSpec((1, CH), lambda i, s: (0, 0)),
        ],
        out_specs=pl.BlockSpec((block, 2 * CH), lambda i, s: (i, 0)),
        scratch_shapes=[
            pltpu.VMEM((2, block, WIN, 3 * FEAT), jnp.float32),
            pltpu.SemaphoreType.DMA((2, block)),
        ],
    )
    return pl.pallas_call(
        _pool_kernel,
        out_shape=jax.ShapeDtypeStruct((slots, 2 * CH), jnp.float32),
        grid_spec=grid_spec,
        compiler_params=pltpu.CompilerParams(dimension_semantics=("arbitrary",)),
        cost_estimate=pl.CostEstimate(
            flops=2 * slots * WIN * 3 * FEAT * CH * 6,
            transcendentals=slots * CH,
            bytes_accessed=slots * WIN * 3 * FEAT * 4 + 3 * FEAT * CH * 4 + slots * 2 * CH * 4,
        ),
    )(starts, x3, conv_weight, conv_bias.reshape(1, CH))


def smooth_rows(padded_rows, smooth_kernel):
    padded = jnp.pad(padded_rows, ((0, 0), (1, 1)))
    height = padded.shape[0] - 2
    col_count = padded.shape[1] - 2
    result = jnp.zeros((height, col_count), padded.dtype)
    for row_off in range(3):
        for col_off in range(3):
            result = (
                result
                + smooth_kernel[row_off, col_off]
                * padded[row_off : row_off + height, col_off : col_off + col_count]
            )
    return result


def per_device(
    frames, seg_start, seg_dest, rec_id, conv_weight, conv_bias, proj_weight, smooth_kernel
):
    group_size = lax.axis_size("wide")
    total_rows = SEG_DEV * group_size
    pooled = pool_slots(frames, seg_start, conv_weight, conv_bias)
    embedded = jnp.dot(pooled, proj_weight, precision=PRECISE, preferred_element_type=jnp.float32)
    packed = jnp.concatenate(
        [
            embedded,
            seg_dest.astype(jnp.float32)[:, None],
            rec_id.astype(jnp.float32)[:, None],
        ],
        axis=1,
    )
    every = lax.all_gather(packed, "wide", axis=0, tiled=True)
    all_emb = every[:, :EMB]
    all_dest = every[:, EMB].astype(jnp.int32)
    all_rec = every[:, EMB + 1].astype(jnp.int32)
    slot_total = all_dest.shape[0]
    used = all_dest >= 0

    mean_sum = jnp.sum(jnp.where(used[:, None], all_emb, 0.0), axis=0)
    centred = all_emb - mean_sum / total_rows
    unit = (centred / jnp.sqrt(jnp.sum(centred * centred, axis=1, keepdims=True) + 1e-06)).astype(
        jnp.bfloat16
    )

    slot_ids = jnp.arange(slot_total, dtype=jnp.int32)
    earlier = (slot_ids[None, :] < slot_ids[:, None]) & (all_dest[None, :] == all_dest[:, None])
    rank = jnp.sum(earlier.astype(jnp.int32), axis=1)
    position = jnp.where(used, all_dest * SEG_DEV + rank, -1)
    picks = position[None, :] == jnp.arange(total_rows, dtype=jnp.int32)[:, None]
    slot_of_pos = jnp.sum(jnp.where(picks, slot_ids[None, :], 0), axis=1)

    col_unit = jnp.take(unit, slot_of_pos, axis=0)
    col_rec = jnp.take(all_rec, slot_of_pos, axis=0)
    zero_unit = jnp.zeros((1, EMB), jnp.bfloat16)
    pad_unit = jnp.concatenate([zero_unit, col_unit, zero_unit], axis=0)
    pad_rec = jnp.concatenate([jnp.full((1,), -1, jnp.int32), col_rec, jnp.full((1,), -1, jnp.int32)])
    my_index = lax.axis_index("wide")
    row_unit = lax.dynamic_slice_in_dim(pad_unit, my_index * SEG_DEV, SEG_DEV + 2, 0)
    row_rec = lax.dynamic_slice_in_dim(pad_rec, my_index * SEG_DEV, SEG_DEV + 2, 0)
    scores = AFF_SCALE * jnp.dot(row_unit, col_unit.T, preferred_element_type=jnp.float32)
    affinity = jnp.where(row_rec[:, None] == col_rec[None, :], 0.0, scores)
    return smooth_rows(affinity, smooth_kernel)


def solution(mesh):
    in_specs = (
        P(("parts", "wide"), None),
        P(("parts", "wide")),
        P(("parts", "wide")),
        P(("parts", "wide")),
        P(),
        P(),
        P(),
        P(),
    )
    out_specs = P(("parts", "wide"), None)
    return jax.shard_map(
        per_device, mesh=mesh, in_specs=in_specs, out_specs=out_specs, check_vma=False
    )
```

```python
import functools

import jax
import jax.numpy as jnp
from jax import lax
from jax.experimental import pallas as pl
from jax.experimental.pallas import tpu as pltpu
from jax.sharding import PartitionSpec as P

FEAT = 80
CH = 1024
EMB = 192
SEGLEN = 64
SEG_DEV = 32


PRECISE = lax.Precision.HIGHEST
AFF_SCALE = 8.0
SEG_BLOCK = 8
WIN = SEGLEN + 8


def _pool_kernel(starts_ref, x3_hbm, w_ref, b_ref, out_ref, buf, sem):
    step = pl.program_id(0)
    steps = pl.num_programs(0)
    block = buf.shape[1]
    rows = x3_hbm.shape[0]

    def aligned_start(blk, j):
        start = starts_ref[blk * block + j]
        return jnp.minimum((start // 8) * 8, rows - WIN)

    def window_copy(blk, slot, j):
        base = pl.multiple_of(aligned_start(blk, j), 8)
        return pltpu.make_async_copy(
            x3_hbm.at[pl.ds(base, WIN)], buf.at[slot, j], sem.at[slot, j]
        )

    @pl.when(step == 0)
    def _():
        for j in range(block):
            window_copy(0, 0, j).start()

    slot = step % 2

    @pl.when(step + 1 < steps)
    def _():
        for j in range(block):
            window_copy(step + 1, 1 - slot, j).start()

    for j in range(block):
        window_copy(step, slot, j).wait()

    stacked = buf[slot].reshape(block * WIN, 3 * FEAT)
    preact = jnp.dot(stacked, w_ref[...], precision=PRECISE, preferred_element_type=jnp.float32)
    activated = jnp.maximum(preact + b_ref[...], 0.0)
    frame_idx = lax.broadcasted_iota(jnp.int32, (WIN, CH), 0)
    means = []
    stds = []
    for j in range(block):
        shift = starts_ref[step * block + j] - aligned_start(step, j)
        inside = (frame_idx >= shift) & (frame_idx < shift + SEGLEN)
        seg_act = activated[j * WIN : (j + 1) * WIN]
        frame_mean = jnp.sum(jnp.where(inside, seg_act, 0.0), axis=0, keepdims=True) / SEGLEN
        deviation = jnp.where(inside, seg_act - frame_mean, 0.0)
        frame_var = jnp.sum(deviation * deviation, axis=0, keepdims=True) / SEGLEN
        means.append(frame_mean)
        stds.append(jnp.sqrt(frame_var + 1e-05))
    out_ref[:, :CH] = jnp.concatenate(means, axis=0)
    out_ref[:, CH:] = jnp.concatenate(stds, axis=0)


def pool_slots(frames, seg_start, conv_weight, conv_bias):
    rows = frames.shape[0]
    slots = seg_start.shape[0]
    zero = jnp.zeros((1, FEAT), frames.dtype)
    x3 = jnp.concatenate(
        [
            jnp.concatenate([zero, frames[:-1]], axis=0),
            frames,
            jnp.concatenate([frames[1:], zero], axis=0),
        ],
        axis=1,
    )
    starts = jnp.clip(seg_start, 0, rows - SEGLEN).astype(jnp.int32)
    block = SEG_BLOCK if slots % SEG_BLOCK == 0 else 1
    grid_spec = pltpu.PrefetchScalarGridSpec(
        num_scalar_prefetch=1,
        grid=(slots // block,),
        in_specs=[
            pl.BlockSpec(memory_space=pl.ANY),
            pl.BlockSpec((3 * FEAT, CH), lambda i, s: (0, 0)),
            pl.BlockSpec((1, CH), lambda i, s: (0, 0)),
        ],
        out_specs=pl.BlockSpec((block, 2 * CH), lambda i, s: (i, 0)),
        scratch_shapes=[
            pltpu.VMEM((2, block, WIN, 3 * FEAT), jnp.float32),
            pltpu.SemaphoreType.DMA((2, block)),
        ],
    )
    return pl.pallas_call(
        _pool_kernel,
        out_shape=jax.ShapeDtypeStruct((slots, 2 * CH), jnp.float32),
        grid_spec=grid_spec,
        compiler_params=pltpu.CompilerParams(dimension_semantics=("arbitrary",)),
        cost_estimate=pl.CostEstimate(
            flops=2 * slots * WIN * 3 * FEAT * CH * 6,
            transcendentals=slots * CH,
            bytes_accessed=slots * WIN * 3 * FEAT * 4 + 3 * FEAT * CH * 4 + slots * 2 * CH * 4,
        ),
    )(starts, x3, conv_weight, conv_bias.reshape(1, CH))


def smooth_rows(padded_rows, smooth_kernel):
    padded = jnp.pad(padded_rows, ((0, 0), (1, 1)))
    height = padded.shape[0] - 2
    col_count = padded.shape[1] - 2
    result = jnp.zeros((height, col_count), padded.dtype)
    for row_off in range(3):
        for col_off in range(3):
            result = (
                result
                + smooth_kernel[row_off, col_off]
                * padded[row_off : row_off + height, col_off : col_off + col_count]
            )
    return result


def gather_wide(x, group_size):
    my_index = lax.axis_index("wide")
    if group_size & (group_size - 1):
        every = lax.all_gather(x, "wide", axis=0, tiled=False)
        source = jnp.arange(group_size, dtype=jnp.int32)
        return every, source
    pattern = [0]
    buf = x[None]
    dist = group_size // 2
    while dist >= 1:
        perm = [(i, i ^ dist) for i in range(group_size)]
        buf = jnp.concatenate([buf, lax.ppermute(buf, "wide", perm)], axis=0)
        pattern = pattern + [p ^ dist for p in pattern]
        dist //= 2
    source = jnp.asarray(pattern, dtype=jnp.int32) ^ my_index
    return buf, source


def per_device(
    frames, seg_start, seg_dest, rec_id, conv_weight, conv_bias, proj_weight, smooth_kernel
):
    group_size = lax.axis_size("wide")
    total_rows = SEG_DEV * group_size
    pooled = pool_slots(frames, seg_start, conv_weight, conv_bias)
    embedded = jnp.dot(pooled, proj_weight, precision=PRECISE, preferred_element_type=jnp.float32)
    packed = jnp.concatenate(
        [
            embedded,
            seg_dest.astype(jnp.float32)[:, None],
            rec_id.astype(jnp.float32)[:, None],
        ],
        axis=1,
    )
    blocks, source = gather_wide(packed, group_size)
    per_block = packed.shape[0]
    every = blocks.reshape(group_size * per_block, packed.shape[1])
    slot_ids = (
        source[:, None] * per_block + jnp.arange(per_block, dtype=jnp.int32)[None, :]
    ).reshape(-1)
    all_emb = every[:, :EMB]
    all_dest = every[:, EMB].astype(jnp.int32)
    all_rec = every[:, EMB + 1].astype(jnp.int32)
    slot_total = all_dest.shape[0]
    used = all_dest >= 0

    mean_sum = jnp.sum(jnp.where(used[:, None], all_emb, 0.0), axis=0)
    centred = all_emb - mean_sum / total_rows
    unit = (centred / jnp.sqrt(jnp.sum(centred * centred, axis=1, keepdims=True) + 1e-06)).astype(
        jnp.bfloat16
    )

    earlier = (slot_ids[None, :] < slot_ids[:, None]) & (all_dest[None, :] == all_dest[:, None])
    rank = jnp.sum(earlier.astype(jnp.int32), axis=1)
    position = jnp.where(used, all_dest * SEG_DEV + rank, -1)
    picks = position[None, :] == jnp.arange(total_rows, dtype=jnp.int32)[:, None]
    row_ids = jnp.arange(slot_total, dtype=jnp.int32)
    slot_of_pos = jnp.sum(jnp.where(picks, row_ids[None, :], 0), axis=1)

    col_unit = jnp.take(unit, slot_of_pos, axis=0)
    col_rec = jnp.take(all_rec, slot_of_pos, axis=0)
    zero_unit = jnp.zeros((1, EMB), jnp.bfloat16)
    pad_unit = jnp.concatenate([zero_unit, col_unit, zero_unit], axis=0)
    pad_rec = jnp.concatenate([jnp.full((1,), -1, jnp.int32), col_rec, jnp.full((1,), -1, jnp.int32)])
    my_index = lax.axis_index("wide")
    row_unit = lax.dynamic_slice_in_dim(pad_unit, my_index * SEG_DEV, SEG_DEV + 2, 0)
    row_rec = lax.dynamic_slice_in_dim(pad_rec, my_index * SEG_DEV, SEG_DEV + 2, 0)
    scores = AFF_SCALE * jnp.dot(row_unit, col_unit.T, preferred_element_type=jnp.float32)
    affinity = jnp.where(row_rec[:, None] == col_rec[None, :], 0.0, scores)
    return smooth_rows(affinity, smooth_kernel)


def solution(mesh):
    in_specs = (
        P(("parts", "wide"), None),
        P(("parts", "wide")),
        P(("parts", "wide")),
        P(("parts", "wide")),
        P(),
        P(),
        P(),
        P(),
    )
    out_specs = P(("parts", "wide"), None)
    return jax.shard_map(
        per_device, mesh=mesh, in_specs=in_specs, out_specs=out_specs, check_vma=False
    )
```

```python
import functools

import jax
import jax.numpy as jnp
from jax import lax
from jax.experimental import pallas as pl
from jax.experimental.pallas import tpu as pltpu
from jax.sharding import PartitionSpec as P

FEAT = 80
CH = 1024
EMB = 192
SEGLEN = 64
SEG_DEV = 32


PRECISE = lax.Precision.HIGHEST
AFF_SCALE = 8.0
SEG_BLOCK = 8
WIN = SEGLEN + 8


def _pool_kernel(starts_ref, x3_hbm, w_ref, b_ref, out_ref, buf, sem):
    step = pl.program_id(0)
    steps = pl.num_programs(0)
    block = buf.shape[1]
    rows = x3_hbm.shape[0]

    def aligned_start(blk, j):
        start = starts_ref[blk * block + j]
        return jnp.minimum((start // 8) * 8, rows - WIN)

    def window_copy(blk, slot, j):
        base = pl.multiple_of(aligned_start(blk, j), 8)
        return pltpu.make_async_copy(
            x3_hbm.at[pl.ds(base, WIN)], buf.at[slot, j], sem.at[slot, j]
        )

    @pl.when(step == 0)
    def _():
        for j in range(block):
            window_copy(0, 0, j).start()

    slot = step % 2

    @pl.when(step + 1 < steps)
    def _():
        for j in range(block):
            window_copy(step + 1, 1 - slot, j).start()

    for j in range(block):
        window_copy(step, slot, j).wait()

    stacked = buf[slot].reshape(block * WIN, 3 * FEAT)
    preact = jnp.dot(stacked, w_ref[...], precision=PRECISE, preferred_element_type=jnp.float32)
    activated = jnp.maximum(preact + b_ref[...], 0.0)
    frame_idx = lax.broadcasted_iota(jnp.int32, (WIN, CH), 0)
    means = []
    stds = []
    for j in range(block):
        shift = starts_ref[step * block + j] - aligned_start(step, j)
        inside = (frame_idx >= shift) & (frame_idx < shift + SEGLEN)
        seg_act = activated[j * WIN : (j + 1) * WIN]
        frame_mean = jnp.sum(jnp.where(inside, seg_act, 0.0), axis=0, keepdims=True) / SEGLEN
        deviation = jnp.where(inside, seg_act - frame_mean, 0.0)
        frame_var = jnp.sum(deviation * deviation, axis=0, keepdims=True) / SEGLEN
        means.append(frame_mean)
        stds.append(jnp.sqrt(frame_var + 1e-05))
    out_ref[:, :CH] = jnp.concatenate(means, axis=0)
    out_ref[:, CH:] = jnp.concatenate(stds, axis=0)


def pool_slots(frames, seg_start, conv_weight, conv_bias):
    rows = frames.shape[0]
    slots = seg_start.shape[0]
    zero = jnp.zeros((1, FEAT), frames.dtype)
    x3 = jnp.concatenate(
        [
            jnp.concatenate([zero, frames[:-1]], axis=0),
            frames,
            jnp.concatenate([frames[1:], zero], axis=0),
        ],
        axis=1,
    )
    starts = jnp.clip(seg_start, 0, rows - SEGLEN).astype(jnp.int32)
    block = SEG_BLOCK if slots % SEG_BLOCK == 0 else 1
    grid_spec = pltpu.PrefetchScalarGridSpec(
        num_scalar_prefetch=1,
        grid=(slots // block,),
        in_specs=[
            pl.BlockSpec(memory_space=pl.ANY),
            pl.BlockSpec((3 * FEAT, CH), lambda i, s: (0, 0)),
            pl.BlockSpec((1, CH), lambda i, s: (0, 0)),
        ],
        out_specs=pl.BlockSpec((block, 2 * CH), lambda i, s: (i, 0)),
        scratch_shapes=[
            pltpu.VMEM((2, block, WIN, 3 * FEAT), jnp.float32),
            pltpu.SemaphoreType.DMA((2, block)),
        ],
    )
    return pl.pallas_call(
        _pool_kernel,
        out_shape=jax.ShapeDtypeStruct((slots, 2 * CH), jnp.float32),
        grid_spec=grid_spec,
        compiler_params=pltpu.CompilerParams(dimension_semantics=("arbitrary",)),
        cost_estimate=pl.CostEstimate(
            flops=2 * slots * WIN * 3 * FEAT * CH * 6,
            transcendentals=slots * CH,
            bytes_accessed=slots * WIN * 3 * FEAT * 4 + 3 * FEAT * CH * 4 + slots * 2 * CH * 4,
        ),
    )(starts, x3, conv_weight, conv_bias.reshape(1, CH))


def smooth_rows(padded_rows, smooth_kernel):
    padded = jnp.pad(padded_rows, ((0, 0), (1, 1)))
    height = padded.shape[0] - 2
    col_count = padded.shape[1] - 2
    result = jnp.zeros((height, col_count), padded.dtype)
    for row_off in range(3):
        for col_off in range(3):
            result = (
                result
                + smooth_kernel[row_off, col_off]
                * padded[row_off : row_off + height, col_off : col_off + col_count]
            )
    return result


def gather_wide(x, group_size):
    spread = jnp.broadcast_to(x[None], (group_size,) + x.shape)
    every = lax.all_to_all(spread, "wide", 0, 0, tiled=True)
    source = jnp.arange(group_size, dtype=jnp.int32)
    return every, source


def per_device(
    frames, seg_start, seg_dest, rec_id, conv_weight, conv_bias, proj_weight, smooth_kernel
):
    group_size = lax.axis_size("wide")
    total_rows = SEG_DEV * group_size
    pooled = pool_slots(frames, seg_start, conv_weight, conv_bias)
    embedded = jnp.dot(pooled, proj_weight, precision=PRECISE, preferred_element_type=jnp.float32)
    packed = jnp.concatenate(
        [
            embedded,
            seg_dest.astype(jnp.float32)[:, None],
            rec_id.astype(jnp.float32)[:, None],
        ],
        axis=1,
    )
    blocks, source = gather_wide(packed, group_size)
    per_block = packed.shape[0]
    every = blocks.reshape(group_size * per_block, packed.shape[1])
    slot_ids = (
        source[:, None] * per_block + jnp.arange(per_block, dtype=jnp.int32)[None, :]
    ).reshape(-1)
    all_emb = every[:, :EMB]
    all_dest = every[:, EMB].astype(jnp.int32)
    all_rec = every[:, EMB + 1].astype(jnp.int32)
    slot_total = all_dest.shape[0]
    used = all_dest >= 0

    mean_sum = jnp.sum(jnp.where(used[:, None], all_emb, 0.0), axis=0)
    centred = all_emb - mean_sum / total_rows
    unit = (centred / jnp.sqrt(jnp.sum(centred * centred, axis=1, keepdims=True) + 1e-06)).astype(
        jnp.bfloat16
    )

    earlier = (slot_ids[None, :] < slot_ids[:, None]) & (all_dest[None, :] == all_dest[:, None])
    rank = jnp.sum(earlier.astype(jnp.int32), axis=1)
    position = jnp.where(used, all_dest * SEG_DEV + rank, -1)
    picks = position[None, :] == jnp.arange(total_rows, dtype=jnp.int32)[:, None]
    row_ids = jnp.arange(slot_total, dtype=jnp.int32)
    slot_of_pos = jnp.sum(jnp.where(picks, row_ids[None, :], 0), axis=1)

    col_unit = jnp.take(unit, slot_of_pos, axis=0)
    col_rec = jnp.take(all_rec, slot_of_pos, axis=0)
    zero_unit = jnp.zeros((1, EMB), jnp.bfloat16)
    pad_unit = jnp.concatenate([zero_unit, col_unit, zero_unit], axis=0)
    pad_rec = jnp.concatenate([jnp.full((1,), -1, jnp.int32), col_rec, jnp.full((1,), -1, jnp.int32)])
    my_index = lax.axis_index("wide")
    row_unit = lax.dynamic_slice_in_dim(pad_unit, my_index * SEG_DEV, SEG_DEV + 2, 0)
    row_rec = lax.dynamic_slice_in_dim(pad_rec, my_index * SEG_DEV, SEG_DEV + 2, 0)
    scores = AFF_SCALE * jnp.dot(row_unit, col_unit.T, preferred_element_type=jnp.float32)
    affinity = jnp.where(row_rec[:, None] == col_rec[None, :], 0.0, scores)
    return smooth_rows(affinity, smooth_kernel)


def solution(mesh):
    in_specs = (
        P(("parts", "wide"), None),
        P(("parts", "wide")),
        P(("parts", "wide")),
        P(("parts", "wide")),
        P(),
        P(),
        P(),
        P(),
    )
    out_specs = P(("parts", "wide"), None)
    return jax.shard_map(
        per_device, mesh=mesh, in_specs=in_specs, out_specs=out_specs, check_vma=False
    )
```

```python
import functools

import jax
import jax.numpy as jnp
from jax import lax
from jax.experimental import pallas as pl
from jax.experimental.pallas import tpu as pltpu
from jax.sharding import PartitionSpec as P

FEAT = 80
CH = 1024
EMB = 192
SEGLEN = 64
SEG_DEV = 32


PRECISE = lax.Precision.HIGHEST
AFF_SCALE = 8.0
SEG_BLOCK = 8
WIN = SEGLEN + 8


def _pool_kernel(starts_ref, x3_hbm, w_ref, b_ref, out_ref, buf, sem):
    step = pl.program_id(0)
    steps = pl.num_programs(0)
    block = buf.shape[1]
    rows = x3_hbm.shape[0]

    def aligned_start(blk, j):
        start = starts_ref[blk * block + j]
        return jnp.minimum((start // 8) * 8, rows - WIN)

    def window_copy(blk, slot, j):
        base = pl.multiple_of(aligned_start(blk, j), 8)
        return pltpu.make_async_copy(
            x3_hbm.at[pl.ds(base, WIN)], buf.at[slot, j], sem.at[slot, j]
        )

    @pl.when(step == 0)
    def _():
        for j in range(block):
            window_copy(0, 0, j).start()

    slot = step % 2

    @pl.when(step + 1 < steps)
    def _():
        for j in range(block):
            window_copy(step + 1, 1 - slot, j).start()

    for j in range(block):
        window_copy(step, slot, j).wait()

    stacked = buf[slot].reshape(block * WIN, 3 * FEAT)
    preact = jnp.dot(stacked, w_ref[...], precision=PRECISE, preferred_element_type=jnp.float32)
    activated = jnp.maximum(preact + b_ref[...], 0.0)
    frame_idx = lax.broadcasted_iota(jnp.int32, (WIN, CH), 0)
    means = []
    stds = []
    for j in range(block):
        shift = starts_ref[step * block + j] - aligned_start(step, j)
        inside = (frame_idx >= shift) & (frame_idx < shift + SEGLEN)
        seg_act = activated[j * WIN : (j + 1) * WIN]
        frame_mean = jnp.sum(jnp.where(inside, seg_act, 0.0), axis=0, keepdims=True) / SEGLEN
        deviation = jnp.where(inside, seg_act - frame_mean, 0.0)
        frame_var = jnp.sum(deviation * deviation, axis=0, keepdims=True) / SEGLEN
        means.append(frame_mean)
        stds.append(jnp.sqrt(frame_var + 1e-05))
    out_ref[:, :CH] = jnp.concatenate(means, axis=0)
    out_ref[:, CH:] = jnp.concatenate(stds, axis=0)


def pool_slots(frames, seg_start, conv_weight, conv_bias):
    rows = frames.shape[0]
    slots = seg_start.shape[0]
    zero = jnp.zeros((1, FEAT), frames.dtype)
    x3 = jnp.concatenate(
        [
            jnp.concatenate([zero, frames[:-1]], axis=0),
            frames,
            jnp.concatenate([frames[1:], zero], axis=0),
        ],
        axis=1,
    )
    starts = jnp.clip(seg_start, 0, rows - SEGLEN).astype(jnp.int32)
    block = SEG_BLOCK if slots % SEG_BLOCK == 0 else 1
    grid_spec = pltpu.PrefetchScalarGridSpec(
        num_scalar_prefetch=1,
        grid=(slots // block,),
        in_specs=[
            pl.BlockSpec(memory_space=pl.ANY),
            pl.BlockSpec((3 * FEAT, CH), lambda i, s: (0, 0)),
            pl.BlockSpec((1, CH), lambda i, s: (0, 0)),
        ],
        out_specs=pl.BlockSpec((block, 2 * CH), lambda i, s: (i, 0)),
        scratch_shapes=[
            pltpu.VMEM((2, block, WIN, 3 * FEAT), jnp.float32),
            pltpu.SemaphoreType.DMA((2, block)),
        ],
    )
    return pl.pallas_call(
        _pool_kernel,
        out_shape=jax.ShapeDtypeStruct((slots, 2 * CH), jnp.float32),
        grid_spec=grid_spec,
        compiler_params=pltpu.CompilerParams(dimension_semantics=("arbitrary",)),
        cost_estimate=pl.CostEstimate(
            flops=2 * slots * WIN * 3 * FEAT * CH * 6,
            transcendentals=slots * CH,
            bytes_accessed=slots * WIN * 3 * FEAT * 4 + 3 * FEAT * CH * 4 + slots * 2 * CH * 4,
        ),
    )(starts, x3, conv_weight, conv_bias.reshape(1, CH))


def smooth_rows(padded_rows, smooth_kernel):
    padded = jnp.pad(padded_rows, ((0, 0), (1, 1)))
    height = padded.shape[0] - 2
    col_count = padded.shape[1] - 2
    result = jnp.zeros((height, col_count), padded.dtype)
    for row_off in range(3):
        for col_off in range(3):
            result = (
                result
                + smooth_kernel[row_off, col_off]
                * padded[row_off : row_off + height, col_off : col_off + col_count]
            )
    return result


def gather_wide(x, group_size):
    my_index = lax.axis_index("wide")
    if group_size % 2 or group_size & (group_size - 1):
        every = lax.all_gather(x, "wide", axis=0, tiled=False)
        return every, jnp.arange(group_size, dtype=jnp.int32)
    pattern = [0]
    blocks = [x]
    for flip in range(2, group_size, 2):
        perm = [(i, i ^ flip) for i in range(group_size)]
        blocks.append(lax.ppermute(x, "wide", perm))
        pattern.append(flip)
    buf = jnp.stack(blocks, axis=0)
    perm = [(i, i ^ 1) for i in range(group_size)]
    buf = jnp.concatenate([buf, lax.ppermute(buf, "wide", perm)], axis=0)
    pattern = pattern + [p ^ 1 for p in pattern]
    source = jnp.asarray(pattern, dtype=jnp.int32) ^ my_index
    return buf, source


def per_device(
    frames, seg_start, seg_dest, rec_id, conv_weight, conv_bias, proj_weight, smooth_kernel
):
    group_size = lax.axis_size("wide")
    total_rows = SEG_DEV * group_size
    pooled = pool_slots(frames, seg_start, conv_weight, conv_bias)
    embedded = jnp.dot(pooled, proj_weight, precision=PRECISE, preferred_element_type=jnp.float32)
    packed = jnp.concatenate(
        [
            embedded,
            seg_dest.astype(jnp.float32)[:, None],
            rec_id.astype(jnp.float32)[:, None],
        ],
        axis=1,
    )
    blocks, source = gather_wide(packed, group_size)
    per_block = packed.shape[0]
    every = blocks.reshape(group_size * per_block, packed.shape[1])
    slot_ids = (
        source[:, None] * per_block + jnp.arange(per_block, dtype=jnp.int32)[None, :]
    ).reshape(-1)
    all_emb = every[:, :EMB]
    all_dest = every[:, EMB].astype(jnp.int32)
    all_rec = every[:, EMB + 1].astype(jnp.int32)
    slot_total = all_dest.shape[0]
    used = all_dest >= 0

    mean_sum = jnp.sum(jnp.where(used[:, None], all_emb, 0.0), axis=0)
    centred = all_emb - mean_sum / total_rows
    unit = (centred / jnp.sqrt(jnp.sum(centred * centred, axis=1, keepdims=True) + 1e-06)).astype(
        jnp.bfloat16
    )

    earlier = (slot_ids[None, :] < slot_ids[:, None]) & (all_dest[None, :] == all_dest[:, None])
    rank = jnp.sum(earlier.astype(jnp.int32), axis=1)
    position = jnp.where(used, all_dest * SEG_DEV + rank, -1)
    picks = position[None, :] == jnp.arange(total_rows, dtype=jnp.int32)[:, None]
    row_ids = jnp.arange(slot_total, dtype=jnp.int32)
    slot_of_pos = jnp.sum(jnp.where(picks, row_ids[None, :], 0), axis=1)

    col_unit = jnp.take(unit, slot_of_pos, axis=0)
    col_rec = jnp.take(all_rec, slot_of_pos, axis=0)
    zero_unit = jnp.zeros((1, EMB), jnp.bfloat16)
    pad_unit = jnp.concatenate([zero_unit, col_unit, zero_unit], axis=0)
    pad_rec = jnp.concatenate([jnp.full((1,), -1, jnp.int32), col_rec, jnp.full((1,), -1, jnp.int32)])
    my_index = lax.axis_index("wide")
    row_unit = lax.dynamic_slice_in_dim(pad_unit, my_index * SEG_DEV, SEG_DEV + 2, 0)
    row_rec = lax.dynamic_slice_in_dim(pad_rec, my_index * SEG_DEV, SEG_DEV + 2, 0)
    scores = AFF_SCALE * jnp.dot(row_unit, col_unit.T, preferred_element_type=jnp.float32)
    affinity = jnp.where(row_rec[:, None] == col_rec[None, :], 0.0, scores)
    return smooth_rows(affinity, smooth_kernel)


def solution(mesh):
    in_specs = (
        P(("parts", "wide"), None),
        P(("parts", "wide")),
        P(("parts", "wide")),
        P(("parts", "wide")),
        P(),
        P(),
        P(),
        P(),
    )
    out_specs = P(("parts", "wide"), None)
    return jax.shard_map(
        per_device, mesh=mesh, in_specs=in_specs, out_specs=out_specs, check_vma=False
    )
```

```python
import functools

import jax
import jax.numpy as jnp
from jax import lax
from jax.experimental import pallas as pl
from jax.experimental.pallas import tpu as pltpu
from jax.sharding import PartitionSpec as P

FEAT = 80
CH = 1024
EMB = 192
SEGLEN = 64
SEG_DEV = 32


PRECISE = lax.Precision.HIGHEST
AFF_SCALE = 8.0
SEG_BLOCK = 8
WIN = SEGLEN + 8
CONV_ROWS = 256


def _pool_kernel(starts_ref, frames_ref, w_ref, b_ref, out_ref, x3_ref, act_ref):
    rows = frames_ref.shape[0]
    slots = out_ref.shape[0]
    frames = frames_ref[...]
    x3_ref[...] = jnp.concatenate(
        [pltpu.roll(frames, 1, 0), frames, pltpu.roll(frames, rows - 1, 0)], axis=1
    )
    chunk = CONV_ROWS if rows % CONV_ROWS == 0 else rows

    def conv_chunk(c, carry):
        base = pl.multiple_of(c * chunk, chunk)
        preact = jnp.dot(
            x3_ref[pl.ds(base, chunk), :],
            w_ref[...],
            precision=PRECISE,
            preferred_element_type=jnp.float32,
        )
        act_ref[pl.ds(base, chunk), :] = jnp.maximum(preact + b_ref[...], 0.0)
        return carry

    lax.fori_loop(0, rows // chunk, conv_chunk, 0)
    frame_idx = lax.broadcasted_iota(jnp.int32, (WIN, CH), 0)

    def stats_block(blk, carry):
        means = []
        stds = []
        for j in range(SEG_BLOCK):
            start = starts_ref[blk * SEG_BLOCK + j]
            base = jnp.minimum((start // 8) * 8, rows - WIN)
            shift = start - base
            inside = (frame_idx >= shift) & (frame_idx < shift + SEGLEN)
            seg_act = act_ref[pl.ds(pl.multiple_of(base, 8), WIN), :]
            frame_mean = jnp.sum(jnp.where(inside, seg_act, 0.0), axis=0, keepdims=True) / SEGLEN
            deviation = jnp.where(inside, seg_act - frame_mean, 0.0)
            frame_var = jnp.sum(deviation * deviation, axis=0, keepdims=True) / SEGLEN
            means.append(frame_mean)
            stds.append(jnp.sqrt(frame_var + 1e-05))
        row0 = pl.multiple_of(blk * SEG_BLOCK, SEG_BLOCK)
        out_ref[pl.ds(row0, SEG_BLOCK), :CH] = jnp.concatenate(means, axis=0)
        out_ref[pl.ds(row0, SEG_BLOCK), CH:] = jnp.concatenate(stds, axis=0)
        return carry

    lax.fori_loop(0, slots // SEG_BLOCK, stats_block, 0)


def pool_slots(frames, seg_start, conv_weight, conv_bias):
    rows = frames.shape[0]
    slots = seg_start.shape[0]
    starts = jnp.clip(seg_start, 0, rows - SEGLEN).astype(jnp.int32)
    vmem = pltpu.MemorySpace.VMEM
    return pl.pallas_call(
        _pool_kernel,
        out_shape=jax.ShapeDtypeStruct((slots, 2 * CH), jnp.float32),
        in_specs=[
            pl.BlockSpec(memory_space=pltpu.MemorySpace.SMEM),
            pl.BlockSpec(memory_space=vmem),
            pl.BlockSpec(memory_space=vmem),
            pl.BlockSpec(memory_space=vmem),
        ],
        out_specs=pl.BlockSpec(memory_space=vmem),
        scratch_shapes=[
            pltpu.VMEM((rows, 3 * FEAT), jnp.float32),
            pltpu.VMEM((rows, CH), jnp.float32),
        ],
        compiler_params=pltpu.CompilerParams(vmem_limit_bytes=48 * 1024 * 1024),
        cost_estimate=pl.CostEstimate(
            flops=2 * rows * 3 * FEAT * CH * 6 + 8 * slots * WIN * CH,
            transcendentals=slots * CH,
            bytes_accessed=rows * FEAT * 4 + 3 * FEAT * CH * 4 + slots * 2 * CH * 4,
        ),
    )(starts, frames, conv_weight, conv_bias.reshape(1, CH))


def smooth_rows(padded_rows, smooth_kernel):
    padded = jnp.pad(padded_rows, ((0, 0), (1, 1)))
    height = padded.shape[0] - 2
    col_count = padded.shape[1] - 2
    result = jnp.zeros((height, col_count), padded.dtype)
    for row_off in range(3):
        for col_off in range(3):
            result = (
                result
                + smooth_kernel[row_off, col_off]
                * padded[row_off : row_off + height, col_off : col_off + col_count]
            )
    return result


def gather_wide(x, group_size):
    my_index = lax.axis_index("wide")
    if group_size % 2 or group_size & (group_size - 1):
        every = lax.all_gather(x, "wide", axis=0, tiled=False)
        return every, jnp.arange(group_size, dtype=jnp.int32)
    pattern = [0]
    blocks = [x]
    for flip in range(2, group_size, 2):
        perm = [(i, i ^ flip) for i in range(group_size)]
        blocks.append(lax.ppermute(x, "wide", perm))
        pattern.append(flip)
    buf = jnp.stack(blocks, axis=0)
    perm = [(i, i ^ 1) for i in range(group_size)]
    buf = jnp.concatenate([buf, lax.ppermute(buf, "wide", perm)], axis=0)
    pattern = pattern + [p ^ 1 for p in pattern]
    source = jnp.asarray(pattern, dtype=jnp.int32) ^ my_index
    return buf, source


def per_device(
    frames, seg_start, seg_dest, rec_id, conv_weight, conv_bias, proj_weight, smooth_kernel
):
    group_size = lax.axis_size("wide")
    total_rows = SEG_DEV * group_size
    pooled = pool_slots(frames, seg_start, conv_weight, conv_bias)
    embedded = jnp.dot(pooled, proj_weight, precision=PRECISE, preferred_element_type=jnp.float32)
    packed = jnp.concatenate(
        [
            embedded,
            seg_dest.astype(jnp.float32)[:, None],
            rec_id.astype(jnp.float32)[:, None],
        ],
        axis=1,
    )
    blocks, source = gather_wide(packed, group_size)
    per_block = packed.shape[0]
    every = blocks.reshape(group_size * per_block, packed.shape[1])
    slot_ids = (
        source[:, None] * per_block + jnp.arange(per_block, dtype=jnp.int32)[None, :]
    ).reshape(-1)
    all_emb = every[:, :EMB]
    all_dest = every[:, EMB].astype(jnp.int32)
    all_rec = every[:, EMB + 1].astype(jnp.int32)
    slot_total = all_dest.shape[0]
    used = all_dest >= 0

    mean_sum = jnp.sum(jnp.where(used[:, None], all_emb, 0.0), axis=0)
    centred = all_emb - mean_sum / total_rows
    unit = (centred / jnp.sqrt(jnp.sum(centred * centred, axis=1, keepdims=True) + 1e-06)).astype(
        jnp.bfloat16
    )

    earlier = (slot_ids[None, :] < slot_ids[:, None]) & (all_dest[None, :] == all_dest[:, None])
    rank = jnp.sum(earlier.astype(jnp.int32), axis=1)
    position = jnp.where(used, all_dest * SEG_DEV + rank, -1)
    picks = position[None, :] == jnp.arange(total_rows, dtype=jnp.int32)[:, None]
    row_ids = jnp.arange(slot_total, dtype=jnp.int32)
    slot_of_pos = jnp.sum(jnp.where(picks, row_ids[None, :], 0), axis=1)

    col_unit = jnp.take(unit, slot_of_pos, axis=0)
    col_rec = jnp.take(all_rec, slot_of_pos, axis=0)
    zero_unit = jnp.zeros((1, EMB), jnp.bfloat16)
    pad_unit = jnp.concatenate([zero_unit, col_unit, zero_unit], axis=0)
    pad_rec = jnp.concatenate([jnp.full((1,), -1, jnp.int32), col_rec, jnp.full((1,), -1, jnp.int32)])
    my_index = lax.axis_index("wide")
    row_unit = lax.dynamic_slice_in_dim(pad_unit, my_index * SEG_DEV, SEG_DEV + 2, 0)
    row_rec = lax.dynamic_slice_in_dim(pad_rec, my_index * SEG_DEV, SEG_DEV + 2, 0)
    scores = AFF_SCALE * jnp.dot(row_unit, col_unit.T, preferred_element_type=jnp.float32)
    affinity = jnp.where(row_rec[:, None] == col_rec[None, :], 0.0, scores)
    return smooth_rows(affinity, smooth_kernel)


def solution(mesh):
    in_specs = (
        P(("parts", "wide"), None),
        P(("parts", "wide")),
        P(("parts", "wide")),
        P(("parts", "wide")),
        P(),
        P(),
        P(),
        P(),
    )
    out_specs = P(("parts", "wide"), None)
    return jax.shard_map(
        per_device, mesh=mesh, in_specs=in_specs, out_specs=out_specs, check_vma=False
    )
```

```python
import functools

import jax
import jax.numpy as jnp
from jax import lax
from jax.experimental import pallas as pl
from jax.experimental.pallas import tpu as pltpu
from jax.sharding import PartitionSpec as P

FEAT = 80
CH = 1024
EMB = 192
SEGLEN = 64
SEG_DEV = 32


PRECISE = lax.Precision.HIGHEST
AFF_SCALE = 8.0
SEG_BLOCK = 8
WIN = SEGLEN + 8
CONV_ROWS = 256
ONE_HOT_LIMIT = 1 << 20


def _pool_kernel(starts_ref, frames_ref, w_ref, b_ref, out_ref, x3_ref, act_ref):
    rows = frames_ref.shape[0]
    slots = out_ref.shape[0]
    frames = frames_ref[...]
    x3_ref[...] = jnp.concatenate(
        [pltpu.roll(frames, 1, 0), frames, pltpu.roll(frames, rows - 1, 0)], axis=1
    )
    chunk = CONV_ROWS if rows % CONV_ROWS == 0 else rows

    def conv_chunk(c, carry):
        base = pl.multiple_of(c * chunk, chunk)
        preact = jnp.dot(
            x3_ref[pl.ds(base, chunk), :],
            w_ref[...],
            precision=PRECISE,
            preferred_element_type=jnp.float32,
        )
        act_ref[pl.ds(base, chunk), :] = jnp.maximum(preact + b_ref[...], 0.0)
        return carry

    lax.fori_loop(0, rows // chunk, conv_chunk, 0)
    frame_idx = lax.broadcasted_iota(jnp.int32, (WIN, CH), 0)

    def stats_block(blk, carry):
        means = []
        stds = []
        for j in range(SEG_BLOCK):
            start = starts_ref[blk * SEG_BLOCK + j]
            base = jnp.minimum((start // 8) * 8, rows - WIN)
            shift = start - base
            inside = (frame_idx >= shift) & (frame_idx < shift + SEGLEN)
            seg_act = act_ref[pl.ds(pl.multiple_of(base, 8), WIN), :]
            frame_mean = jnp.sum(jnp.where(inside, seg_act, 0.0), axis=0, keepdims=True) / SEGLEN
            deviation = jnp.where(inside, seg_act - frame_mean, 0.0)
            frame_var = jnp.sum(deviation * deviation, axis=0, keepdims=True) / SEGLEN
            means.append(frame_mean)
            stds.append(jnp.sqrt(frame_var + 1e-05))
        row0 = pl.multiple_of(blk * SEG_BLOCK, SEG_BLOCK)
        out_ref[pl.ds(row0, SEG_BLOCK), :CH] = jnp.concatenate(means, axis=0)
        out_ref[pl.ds(row0, SEG_BLOCK), CH:] = jnp.concatenate(stds, axis=0)
        return carry

    lax.fori_loop(0, slots // SEG_BLOCK, stats_block, 0)


def pool_slots(frames, seg_start, conv_weight, conv_bias):
    rows = frames.shape[0]
    slots = seg_start.shape[0]
    starts = jnp.clip(seg_start, 0, rows - SEGLEN).astype(jnp.int32)
    vmem = pltpu.MemorySpace.VMEM
    return pl.pallas_call(
        _pool_kernel,
        out_shape=jax.ShapeDtypeStruct((slots, 2 * CH), jnp.float32),
        in_specs=[
            pl.BlockSpec(memory_space=pltpu.MemorySpace.SMEM),
            pl.BlockSpec(memory_space=vmem),
            pl.BlockSpec(memory_space=vmem),
            pl.BlockSpec(memory_space=vmem),
        ],
        out_specs=pl.BlockSpec(memory_space=vmem),
        scratch_shapes=[
            pltpu.VMEM((rows, 3 * FEAT), jnp.float32),
            pltpu.VMEM((rows, CH), jnp.float32),
        ],
        compiler_params=pltpu.CompilerParams(vmem_limit_bytes=48 * 1024 * 1024),
        cost_estimate=pl.CostEstimate(
            flops=2 * rows * 3 * FEAT * CH * 6 + 8 * slots * WIN * CH,
            transcendentals=slots * CH,
            bytes_accessed=rows * FEAT * 4 + 3 * FEAT * CH * 4 + slots * 2 * CH * 4,
        ),
    )(starts, frames, conv_weight, conv_bias.reshape(1, CH))


def _affinity_kernel(k_ref, row_unit_ref, col_unit_ref, row_rec_ref, col_rec_ref, out_ref, pad_ref):
    height, width = out_ref.shape
    scores = lax.dot_general(
        row_unit_ref[...],
        col_unit_ref[...],
        (((1,), (1,)), ((), ())),
        preferred_element_type=jnp.float32,
    )
    affinity = jnp.where(row_rec_ref[...] == col_rec_ref[...], 0.0, AFF_SCALE * scores)
    pad_ref[...] = jnp.zeros(pad_ref.shape, jnp.float32)
    pad_ref[0 : height + 2, 1 : width + 1] = affinity
    result = jnp.zeros((height, width), jnp.float32)
    for row_off in range(3):
        for col_off in range(3):
            result = result + k_ref[row_off, col_off] * pad_ref[
                row_off : row_off + height, col_off : col_off + width
            ]
    out_ref[...] = result


def smooth_affinity(row_unit, col_unit, row_rec, col_rec, smooth_kernel):
    height = row_unit.shape[0] - 2
    width = col_unit.shape[0]
    vmem = pltpu.MemorySpace.VMEM
    return pl.pallas_call(
        _affinity_kernel,
        out_shape=jax.ShapeDtypeStruct((height, width), jnp.float32),
        in_specs=[pl.BlockSpec(memory_space=pltpu.MemorySpace.SMEM)]
        + [pl.BlockSpec(memory_space=vmem)] * 4,
        out_specs=pl.BlockSpec(memory_space=vmem),
        scratch_shapes=[
            pltpu.VMEM((-(-(height + 2) // 8) * 8, -(-(width + 2) // 128) * 128), jnp.float32)
        ],
        compiler_params=pltpu.CompilerParams(vmem_limit_bytes=48 * 1024 * 1024),
        cost_estimate=pl.CostEstimate(
            flops=2 * (height + 2) * width * EMB + 20 * height * width,
            transcendentals=0,
            bytes_accessed=(width + height + 2) * EMB * 2 + height * width * 4,
        ),
    )(smooth_kernel, row_unit, col_unit, row_rec.reshape(-1, 1), col_rec.reshape(1, -1))


def gather_wide(x, group_size):
    my_index = lax.axis_index("wide")
    if group_size % 2 or group_size & (group_size - 1):
        every = lax.all_gather(x, "wide", axis=0, tiled=False)
        return every, jnp.arange(group_size, dtype=jnp.int32)
    pattern = [0]
    blocks = [x]
    for flip in range(2, group_size, 2):
        perm = [(i, i ^ flip) for i in range(group_size)]
        blocks.append(lax.ppermute(x, "wide", perm))
        pattern.append(flip)
    buf = jnp.stack(blocks, axis=0)
    perm = [(i, i ^ 1) for i in range(group_size)]
    buf = jnp.concatenate([buf, lax.ppermute(buf, "wide", perm)], axis=0)
    pattern = pattern + [p ^ 1 for p in pattern]
    source = jnp.asarray(pattern, dtype=jnp.int32) ^ my_index
    return buf, source


def per_device(
    frames, seg_start, seg_dest, rec_id, conv_weight, conv_bias, proj_weight, smooth_kernel
):
    group_size = lax.axis_size("wide")
    total_rows = SEG_DEV * group_size
    pooled = pool_slots(frames, seg_start, conv_weight, conv_bias)
    embedded = jnp.dot(pooled, proj_weight, precision=PRECISE, preferred_element_type=jnp.float32)
    packed = jnp.concatenate(
        [
            embedded,
            seg_dest.astype(jnp.float32)[:, None],
            rec_id.astype(jnp.float32)[:, None],
        ],
        axis=1,
    )
    blocks, source = gather_wide(packed, group_size)
    per_block = packed.shape[0]
    every = blocks.reshape(group_size * per_block, packed.shape[1])
    slot_ids = (
        source[:, None] * per_block + jnp.arange(per_block, dtype=jnp.int32)[None, :]
    ).reshape(-1)
    all_emb = every[:, :EMB]
    all_dest = every[:, EMB].astype(jnp.int32)
    all_rec = every[:, EMB + 1].astype(jnp.int32)
    slot_total = all_dest.shape[0]
    used = all_dest >= 0

    mean_sum = jnp.sum(jnp.where(used[:, None], all_emb, 0.0), axis=0)
    centred = all_emb - mean_sum / total_rows
    unit = (centred / jnp.sqrt(jnp.sum(centred * centred, axis=1, keepdims=True) + 1e-06)).astype(
        jnp.bfloat16
    )

    earlier = (slot_ids[None, :] < slot_ids[:, None]) & (all_dest[None, :] == all_dest[:, None])
    rank = jnp.sum(earlier.astype(jnp.int32), axis=1)
    position = jnp.where(used, all_dest * SEG_DEV + rank, -1)
    picks = position[None, :] == jnp.arange(total_rows, dtype=jnp.int32)[:, None]
    row_ids = jnp.arange(slot_total, dtype=jnp.int32)
    slot_of_pos = jnp.sum(jnp.where(picks, row_ids[None, :], 0), axis=1)

    if total_rows * slot_total <= ONE_HOT_LIMIT:
        rec_hi = (all_rec // 16).astype(jnp.bfloat16)[:, None]
        rec_lo = (all_rec % 16).astype(jnp.bfloat16)[:, None]
        unit_ext = jnp.concatenate([unit, rec_hi, rec_lo], axis=1)
        selector = picks.astype(jnp.bfloat16)
        col_ext = jnp.dot(selector, unit_ext, preferred_element_type=jnp.float32)
        col_unit = col_ext[:, :EMB].astype(jnp.bfloat16)
        col_rec = (col_ext[:, EMB] * 16 + col_ext[:, EMB + 1]).astype(jnp.int32)
    else:
        col_unit = jnp.take(unit, slot_of_pos, axis=0)
        col_rec = jnp.take(all_rec, slot_of_pos, axis=0)
    zero_unit = jnp.zeros((1, EMB), jnp.bfloat16)
    pad_unit = jnp.concatenate([zero_unit, col_unit, zero_unit], axis=0)
    pad_rec = jnp.concatenate([jnp.full((1,), -1, jnp.int32), col_rec, jnp.full((1,), -1, jnp.int32)])
    my_index = lax.axis_index("wide")
    row_unit = lax.dynamic_slice_in_dim(pad_unit, my_index * SEG_DEV, SEG_DEV + 2, 0)
    row_rec = lax.dynamic_slice_in_dim(pad_rec, my_index * SEG_DEV, SEG_DEV + 2, 0)
    return smooth_affinity(row_unit, col_unit, row_rec, col_rec, smooth_kernel)


def solution(mesh):
    in_specs = (
        P(("parts", "wide"), None),
        P(("parts", "wide")),
        P(("parts", "wide")),
        P(("parts", "wide")),
        P(),
        P(),
        P(),
        P(),
    )
    out_specs = P(("parts", "wide"), None)
    return jax.shard_map(
        per_device, mesh=mesh, in_specs=in_specs, out_specs=out_specs, check_vma=False
    )
```

```python
import functools

import jax
import jax.numpy as jnp
from jax import lax
from jax.experimental import pallas as pl
from jax.experimental.pallas import tpu as pltpu
from jax.sharding import PartitionSpec as P

FEAT = 80
CH = 1024
EMB = 192
SEGLEN = 64
SEG_DEV = 32


PRECISE = lax.Precision.HIGHEST
AFF_SCALE = 8.0
SEG_BLOCK = 8
WIN = SEGLEN + 8
CONV_ROWS = 256
ONE_HOT_LIMIT = 1 << 20


def _pool_kernel(starts_ref, frames_ref, w_ref, b_ref, out_ref, x3_ref, act_ref):
    rows = frames_ref.shape[0]
    slots = out_ref.shape[0]
    frames = frames_ref[...]
    x3_ref[...] = jnp.concatenate(
        [pltpu.roll(frames, 1, 0), frames, pltpu.roll(frames, rows - 1, 0)], axis=1
    )
    chunk = CONV_ROWS if rows % CONV_ROWS == 0 else rows

    def conv_chunk(c, carry):
        base = pl.multiple_of(c * chunk, chunk)
        preact = jnp.dot(
            x3_ref[pl.ds(base, chunk), :],
            w_ref[...],
            precision=PRECISE,
            preferred_element_type=jnp.float32,
        )
        act_ref[pl.ds(base, chunk), :] = jnp.maximum(preact + b_ref[...], 0.0)
        return carry

    lax.fori_loop(0, rows // chunk, conv_chunk, 0)
    frame_idx = lax.broadcasted_iota(jnp.int32, (WIN, 1), 0)

    def stats_block(blk, carry):
        means = []
        stds = []
        for j in range(SEG_BLOCK):
            start = starts_ref[blk * SEG_BLOCK + j]
            base = jnp.minimum((start // 8) * 8, rows - WIN)
            shift = start - base
            inside = (frame_idx >= shift) & (frame_idx < shift + SEGLEN)
            seg_act = act_ref[pl.ds(pl.multiple_of(base, 8), WIN), :]
            frame_mean = jnp.sum(jnp.where(inside, seg_act, 0.0), axis=0, keepdims=True) / SEGLEN
            deviation = jnp.where(inside, seg_act - frame_mean, 0.0)
            frame_var = jnp.sum(deviation * deviation, axis=0, keepdims=True) / SEGLEN
            means.append(frame_mean)
            stds.append(jnp.sqrt(frame_var + 1e-05))
        row0 = pl.multiple_of(blk * SEG_BLOCK, SEG_BLOCK)
        out_ref[pl.ds(row0, SEG_BLOCK), :CH] = jnp.concatenate(means, axis=0)
        out_ref[pl.ds(row0, SEG_BLOCK), CH:] = jnp.concatenate(stds, axis=0)
        return carry

    lax.fori_loop(0, slots // SEG_BLOCK, stats_block, 0)


def pool_slots(frames, seg_start, conv_weight, conv_bias):
    rows = frames.shape[0]
    slots = seg_start.shape[0]
    starts = jnp.clip(seg_start, 0, rows - SEGLEN).astype(jnp.int32)
    vmem = pltpu.MemorySpace.VMEM
    return pl.pallas_call(
        _pool_kernel,
        out_shape=jax.ShapeDtypeStruct((slots, 2 * CH), jnp.float32),
        in_specs=[
            pl.BlockSpec(memory_space=pltpu.MemorySpace.SMEM),
            pl.BlockSpec(memory_space=vmem),
            pl.BlockSpec(memory_space=vmem),
            pl.BlockSpec(memory_space=vmem),
        ],
        out_specs=pl.BlockSpec(memory_space=vmem),
        scratch_shapes=[
            pltpu.VMEM((rows, 3 * FEAT), jnp.float32),
            pltpu.VMEM((rows, CH), jnp.float32),
        ],
        compiler_params=pltpu.CompilerParams(vmem_limit_bytes=48 * 1024 * 1024),
        cost_estimate=pl.CostEstimate(
            flops=2 * rows * 3 * FEAT * CH * 6 + 8 * slots * WIN * CH,
            transcendentals=slots * CH,
            bytes_accessed=rows * FEAT * 4 + 3 * FEAT * CH * 4 + slots * 2 * CH * 4,
        ),
    )(starts, frames, conv_weight, conv_bias.reshape(1, CH))


def _affinity_kernel(k_ref, row_unit_ref, col_unit_ref, row_rec_ref, col_rec_ref, out_ref, pad_ref):
    height, width = out_ref.shape
    scores = lax.dot_general(
        row_unit_ref[...],
        col_unit_ref[...],
        (((1,), (1,)), ((), ())),
        preferred_element_type=jnp.float32,
    )
    affinity = jnp.where(row_rec_ref[...] == col_rec_ref[...], 0.0, AFF_SCALE * scores)
    pad_ref[...] = jnp.zeros(pad_ref.shape, jnp.float32)
    pad_ref[0 : height + 2, 1 : width + 1] = affinity
    result = jnp.zeros((height, width), jnp.float32)
    for row_off in range(3):
        for col_off in range(3):
            result = result + k_ref[row_off, col_off] * pad_ref[
                row_off : row_off + height, col_off : col_off + width
            ]
    out_ref[...] = result


def smooth_affinity(row_unit, col_unit, row_rec, col_rec, smooth_kernel):
    height = row_unit.shape[0] - 2
    width = col_unit.shape[0]
    vmem = pltpu.MemorySpace.VMEM
    return pl.pallas_call(
        _affinity_kernel,
        out_shape=jax.ShapeDtypeStruct((height, width), jnp.float32),
        in_specs=[pl.BlockSpec(memory_space=pltpu.MemorySpace.SMEM)]
        + [pl.BlockSpec(memory_space=vmem)] * 4,
        out_specs=pl.BlockSpec(memory_space=vmem),
        scratch_shapes=[
            pltpu.VMEM((-(-(height + 2) // 8) * 8, -(-(width + 2) // 128) * 128), jnp.float32)
        ],
        compiler_params=pltpu.CompilerParams(vmem_limit_bytes=48 * 1024 * 1024),
        cost_estimate=pl.CostEstimate(
            flops=2 * (height + 2) * width * EMB + 20 * height * width,
            transcendentals=0,
            bytes_accessed=(width + height + 2) * EMB * 2 + height * width * 4,
        ),
    )(smooth_kernel, row_unit, col_unit, row_rec.reshape(-1, 1), col_rec.reshape(1, -1))


def gather_wide(x, group_size):
    my_index = lax.axis_index("wide")
    if group_size % 2 or group_size & (group_size - 1):
        every = lax.all_gather(x, "wide", axis=0, tiled=False)
        return every, jnp.arange(group_size, dtype=jnp.int32)
    pattern = [0]
    blocks = [x]
    for flip in range(2, group_size, 2):
        perm = [(i, i ^ flip) for i in range(group_size)]
        blocks.append(lax.ppermute(x, "wide", perm))
        pattern.append(flip)
    buf = jnp.stack(blocks, axis=0)
    perm = [(i, i ^ 1) for i in range(group_size)]
    buf = jnp.concatenate([buf, lax.ppermute(buf, "wide", perm)], axis=0)
    pattern = pattern + [p ^ 1 for p in pattern]
    source = jnp.asarray(pattern, dtype=jnp.int32) ^ my_index
    return buf, source


def per_device(
    frames, seg_start, seg_dest, rec_id, conv_weight, conv_bias, proj_weight, smooth_kernel
):
    group_size = lax.axis_size("wide")
    total_rows = SEG_DEV * group_size
    pooled = pool_slots(frames, seg_start, conv_weight, conv_bias)
    embedded = jnp.dot(pooled, proj_weight, precision=PRECISE, preferred_element_type=jnp.float32)
    packed = jnp.concatenate(
        [
            embedded,
            seg_dest.astype(jnp.float32)[:, None],
            rec_id.astype(jnp.float32)[:, None],
        ],
        axis=1,
    )
    blocks, source = gather_wide(packed, group_size)
    per_block = packed.shape[0]
    every = blocks.reshape(group_size * per_block, packed.shape[1])
    slot_ids = (
        source[:, None] * per_block + jnp.arange(per_block, dtype=jnp.int32)[None, :]
    ).reshape(-1)
    all_emb = every[:, :EMB]
    all_dest = every[:, EMB].astype(jnp.int32)
    all_rec = every[:, EMB + 1].astype(jnp.int32)
    slot_total = all_dest.shape[0]
    used = all_dest >= 0

    mean_sum = jnp.sum(jnp.where(used[:, None], all_emb, 0.0), axis=0)
    centred = all_emb - mean_sum / total_rows
    unit = (centred / jnp.sqrt(jnp.sum(centred * centred, axis=1, keepdims=True) + 1e-06)).astype(
        jnp.bfloat16
    )

    earlier = (slot_ids[None, :] < slot_ids[:, None]) & (all_dest[None, :] == all_dest[:, None])
    rank = jnp.sum(earlier.astype(jnp.int32), axis=1)
    position = jnp.where(used, all_dest * SEG_DEV + rank, -1)
    picks = position[None, :] == jnp.arange(total_rows, dtype=jnp.int32)[:, None]
    row_ids = jnp.arange(slot_total, dtype=jnp.int32)
    slot_of_pos = jnp.sum(jnp.where(picks, row_ids[None, :], 0), axis=1)

    if total_rows * slot_total <= ONE_HOT_LIMIT:
        rec_hi = (all_rec // 16).astype(jnp.bfloat16)[:, None]
        rec_lo = (all_rec % 16).astype(jnp.bfloat16)[:, None]
        unit_ext = jnp.concatenate([unit, rec_hi, rec_lo], axis=1)
        selector = picks.astype(jnp.bfloat16)
        col_ext = jnp.dot(selector, unit_ext, preferred_element_type=jnp.float32)
        col_unit = col_ext[:, :EMB].astype(jnp.bfloat16)
        col_rec = (col_ext[:, EMB] * 16 + col_ext[:, EMB + 1]).astype(jnp.int32)
    else:
        col_unit = jnp.take(unit, slot_of_pos, axis=0)
        col_rec = jnp.take(all_rec, slot_of_pos, axis=0)
    zero_unit = jnp.zeros((1, EMB), jnp.bfloat16)
    pad_unit = jnp.concatenate([zero_unit, col_unit, zero_unit], axis=0)
    pad_rec = jnp.concatenate([jnp.full((1,), -1, jnp.int32), col_rec, jnp.full((1,), -1, jnp.int32)])
    my_index = lax.axis_index("wide")
    row_unit = lax.dynamic_slice_in_dim(pad_unit, my_index * SEG_DEV, SEG_DEV + 2, 0)
    row_rec = lax.dynamic_slice_in_dim(pad_rec, my_index * SEG_DEV, SEG_DEV + 2, 0)
    return smooth_affinity(row_unit, col_unit, row_rec, col_rec, smooth_kernel)


def solution(mesh):
    in_specs = (
        P(("parts", "wide"), None),
        P(("parts", "wide")),
        P(("parts", "wide")),
        P(("parts", "wide")),
        P(),
        P(),
        P(),
        P(),
    )
    out_specs = P(("parts", "wide"), None)
    return jax.shard_map(
        per_device, mesh=mesh, in_specs=in_specs, out_specs=out_specs, check_vma=False
    )
```

```python
import functools

import jax
import jax.numpy as jnp
from jax import lax
from jax.experimental import pallas as pl
from jax.experimental.pallas import tpu as pltpu
from jax.sharding import PartitionSpec as P

FEAT = 80
CH = 1024
EMB = 192
SEGLEN = 64
SEG_DEV = 32


PRECISE = lax.Precision.HIGHEST
AFF_SCALE = 8.0
SEG_BLOCK = 8
WIN = SEGLEN + 8
CONV_ROWS = 256
ONE_HOT_LIMIT = 1 << 20


def _pool_kernel(starts_ref, frames_ref, w_hi_ref, w_lo_ref, b_ref, out_ref, hi_ref, lo_ref, act_ref):
    rows = frames_ref.shape[0]
    slots = out_ref.shape[0]
    frames = frames_ref[...]
    x3 = jnp.concatenate(
        [pltpu.roll(frames, 1, 0), frames, pltpu.roll(frames, rows - 1, 0)], axis=1
    )
    x3_hi = x3.astype(jnp.bfloat16)
    hi_ref[...] = x3_hi
    lo_ref[...] = (x3 - x3_hi.astype(jnp.float32)).astype(jnp.bfloat16)
    chunk = CONV_ROWS if rows % CONV_ROWS == 0 else rows

    def conv_chunk(c, carry):
        base = pl.multiple_of(c * chunk, chunk)
        x_hi = hi_ref[pl.ds(base, chunk), :]
        x_lo = lo_ref[pl.ds(base, chunk), :]
        w_hi = w_hi_ref[...]
        preact = jnp.dot(x_hi, w_hi, preferred_element_type=jnp.float32)
        preact = preact + jnp.dot(x_hi, w_lo_ref[...], preferred_element_type=jnp.float32)
        preact = preact + jnp.dot(x_lo, w_hi, preferred_element_type=jnp.float32)
        act_ref[pl.ds(base, chunk), :] = jnp.maximum(preact + b_ref[...], 0.0)
        return carry

    lax.fori_loop(0, rows // chunk, conv_chunk, 0)
    frame_idx = lax.broadcasted_iota(jnp.int32, (WIN, CH), 0)

    def stats_block(blk, carry):
        means = []
        stds = []
        for j in range(SEG_BLOCK):
            start = starts_ref[blk * SEG_BLOCK + j]
            base = jnp.minimum((start // 8) * 8, rows - WIN)
            shift = start - base
            inside = (frame_idx >= shift) & (frame_idx < shift + SEGLEN)
            seg_act = act_ref[pl.ds(pl.multiple_of(base, 8), WIN), :]
            frame_mean = jnp.sum(jnp.where(inside, seg_act, 0.0), axis=0, keepdims=True) / SEGLEN
            deviation = jnp.where(inside, seg_act - frame_mean, 0.0)
            frame_var = jnp.sum(deviation * deviation, axis=0, keepdims=True) / SEGLEN
            means.append(frame_mean)
            stds.append(jnp.sqrt(frame_var + 1e-05))
        row0 = pl.multiple_of(blk * SEG_BLOCK, SEG_BLOCK)
        out_ref[pl.ds(row0, SEG_BLOCK), :CH] = jnp.concatenate(means, axis=0)
        out_ref[pl.ds(row0, SEG_BLOCK), CH:] = jnp.concatenate(stds, axis=0)
        return carry

    lax.fori_loop(0, slots // SEG_BLOCK, stats_block, 0)


def pool_slots(frames, seg_start, conv_weight, conv_bias):
    rows = frames.shape[0]
    slots = seg_start.shape[0]
    starts = jnp.clip(seg_start, 0, rows - SEGLEN).astype(jnp.int32)
    vmem = pltpu.MemorySpace.VMEM
    w_hi = conv_weight.astype(jnp.bfloat16)
    w_lo = (conv_weight - w_hi.astype(jnp.float32)).astype(jnp.bfloat16)
    return pl.pallas_call(
        _pool_kernel,
        out_shape=jax.ShapeDtypeStruct((slots, 2 * CH), jnp.float32),
        in_specs=[
            pl.BlockSpec(memory_space=pltpu.MemorySpace.SMEM),
            pl.BlockSpec(memory_space=vmem),
            pl.BlockSpec(memory_space=vmem),
            pl.BlockSpec(memory_space=vmem),
            pl.BlockSpec(memory_space=vmem),
        ],
        out_specs=pl.BlockSpec(memory_space=vmem),
        scratch_shapes=[
            pltpu.VMEM((rows, 3 * FEAT), jnp.bfloat16),
            pltpu.VMEM((rows, 3 * FEAT), jnp.bfloat16),
            pltpu.VMEM((rows, CH), jnp.float32),
        ],
        compiler_params=pltpu.CompilerParams(vmem_limit_bytes=48 * 1024 * 1024),
        cost_estimate=pl.CostEstimate(
            flops=2 * rows * 3 * FEAT * CH * 3 + 8 * slots * WIN * CH,
            transcendentals=slots * CH,
            bytes_accessed=rows * FEAT * 4 + 3 * FEAT * CH * 4 + slots * 2 * CH * 4,
        ),
    )(starts, frames, w_hi, w_lo, conv_bias.reshape(1, CH))


def _affinity_kernel(k_ref, row_unit_ref, col_unit_ref, row_rec_ref, col_rec_ref, out_ref, pad_ref):
    height, width = out_ref.shape
    scores = lax.dot_general(
        row_unit_ref[...],
        col_unit_ref[...],
        (((1,), (1,)), ((), ())),
        preferred_element_type=jnp.float32,
    )
    affinity = jnp.where(row_rec_ref[...] == col_rec_ref[...], 0.0, AFF_SCALE * scores)
    pad_ref[...] = jnp.zeros(pad_ref.shape, jnp.float32)
    pad_ref[0 : height + 2, 1 : width + 1] = affinity
    result = jnp.zeros((height, width), jnp.float32)
    for row_off in range(3):
        for col_off in range(3):
            result = result + k_ref[row_off, col_off] * pad_ref[
                row_off : row_off + height, col_off : col_off + width
            ]
    out_ref[...] = result


def smooth_affinity(row_unit, col_unit, row_rec, col_rec, smooth_kernel):
    height = row_unit.shape[0] - 2
    width = col_unit.shape[0]
    vmem = pltpu.MemorySpace.VMEM
    return pl.pallas_call(
        _affinity_kernel,
        out_shape=jax.ShapeDtypeStruct((height, width), jnp.float32),
        in_specs=[pl.BlockSpec(memory_space=pltpu.MemorySpace.SMEM)]
        + [pl.BlockSpec(memory_space=vmem)] * 4,
        out_specs=pl.BlockSpec(memory_space=vmem),
        scratch_shapes=[
            pltpu.VMEM((-(-(height + 2) // 8) * 8, -(-(width + 2) // 128) * 128), jnp.float32)
        ],
        compiler_params=pltpu.CompilerParams(vmem_limit_bytes=48 * 1024 * 1024),
        cost_estimate=pl.CostEstimate(
            flops=2 * (height + 2) * width * EMB + 20 * height * width,
            transcendentals=0,
            bytes_accessed=(width + height + 2) * EMB * 2 + height * width * 4,
        ),
    )(smooth_kernel, row_unit, col_unit, row_rec.reshape(-1, 1), col_rec.reshape(1, -1))


def gather_wide(x, group_size):
    my_index = lax.axis_index("wide")
    if group_size % 2 or group_size & (group_size - 1):
        every = lax.all_gather(x, "wide", axis=0, tiled=False)
        return every, jnp.arange(group_size, dtype=jnp.int32)
    pattern = [0]
    blocks = [x]
    for flip in range(2, group_size, 2):
        perm = [(i, i ^ flip) for i in range(group_size)]
        blocks.append(lax.ppermute(x, "wide", perm))
        pattern.append(flip)
    buf = jnp.stack(blocks, axis=0)
    perm = [(i, i ^ 1) for i in range(group_size)]
    buf = jnp.concatenate([buf, lax.ppermute(buf, "wide", perm)], axis=0)
    pattern = pattern + [p ^ 1 for p in pattern]
    source = jnp.asarray(pattern, dtype=jnp.int32) ^ my_index
    return buf, source


def per_device(
    frames, seg_start, seg_dest, rec_id, conv_weight, conv_bias, proj_weight, smooth_kernel
):
    group_size = lax.axis_size("wide")
    total_rows = SEG_DEV * group_size
    pooled = pool_slots(frames, seg_start, conv_weight, conv_bias)
    embedded = jnp.dot(pooled, proj_weight, precision=PRECISE, preferred_element_type=jnp.float32)
    packed = jnp.concatenate(
        [
            embedded,
            seg_dest.astype(jnp.float32)[:, None],
            rec_id.astype(jnp.float32)[:, None],
        ],
        axis=1,
    )
    blocks, source = gather_wide(packed, group_size)
    per_block = packed.shape[0]
    every = blocks.reshape(group_size * per_block, packed.shape[1])
    slot_ids = (
        source[:, None] * per_block + jnp.arange(per_block, dtype=jnp.int32)[None, :]
    ).reshape(-1)
    all_emb = every[:, :EMB]
    all_dest = every[:, EMB].astype(jnp.int32)
    all_rec = every[:, EMB + 1].astype(jnp.int32)
    slot_total = all_dest.shape[0]
    used = all_dest >= 0

    mean_sum = jnp.sum(jnp.where(used[:, None], all_emb, 0.0), axis=0)
    centred = all_emb - mean_sum / total_rows
    unit = (centred / jnp.sqrt(jnp.sum(centred * centred, axis=1, keepdims=True) + 1e-06)).astype(
        jnp.bfloat16
    )

    earlier = (slot_ids[None, :] < slot_ids[:, None]) & (all_dest[None, :] == all_dest[:, None])
    rank = jnp.sum(earlier.astype(jnp.int32), axis=1)
    position = jnp.where(used, all_dest * SEG_DEV + rank, -1)
    picks = position[None, :] == jnp.arange(total_rows, dtype=jnp.int32)[:, None]
    row_ids = jnp.arange(slot_total, dtype=jnp.int32)
    slot_of_pos = jnp.sum(jnp.where(picks, row_ids[None, :], 0), axis=1)

    if total_rows * slot_total <= ONE_HOT_LIMIT:
        rec_hi = (all_rec // 16).astype(jnp.bfloat16)[:, None]
        rec_lo = (all_rec % 16).astype(jnp.bfloat16)[:, None]
        unit_ext = jnp.concatenate([unit, rec_hi, rec_lo], axis=1)
        selector = picks.astype(jnp.bfloat16)
        col_ext = jnp.dot(selector, unit_ext, preferred_element_type=jnp.float32)
        col_unit = col_ext[:, :EMB].astype(jnp.bfloat16)
        col_rec = (col_ext[:, EMB] * 16 + col_ext[:, EMB + 1]).astype(jnp.int32)
    else:
        col_unit = jnp.take(unit, slot_of_pos, axis=0)
        col_rec = jnp.take(all_rec, slot_of_pos, axis=0)
    zero_unit = jnp.zeros((1, EMB), jnp.bfloat16)
    pad_unit = jnp.concatenate([zero_unit, col_unit, zero_unit], axis=0)
    pad_rec = jnp.concatenate([jnp.full((1,), -1, jnp.int32), col_rec, jnp.full((1,), -1, jnp.int32)])
    my_index = lax.axis_index("wide")
    row_unit = lax.dynamic_slice_in_dim(pad_unit, my_index * SEG_DEV, SEG_DEV + 2, 0)
    row_rec = lax.dynamic_slice_in_dim(pad_rec, my_index * SEG_DEV, SEG_DEV + 2, 0)
    return smooth_affinity(row_unit, col_unit, row_rec, col_rec, smooth_kernel)


def solution(mesh):
    in_specs = (
        P(("parts", "wide"), None),
        P(("parts", "wide")),
        P(("parts", "wide")),
        P(("parts", "wide")),
        P(),
        P(),
        P(),
        P(),
    )
    out_specs = P(("parts", "wide"), None)
    return jax.shard_map(
        per_device, mesh=mesh, in_specs=in_specs, out_specs=out_specs, check_vma=False
    )
```

```python
import functools

import jax
import jax.numpy as jnp
from jax import lax
from jax.experimental import pallas as pl
from jax.experimental.pallas import tpu as pltpu
from jax.sharding import PartitionSpec as P

FEAT = 80
CH = 1024
EMB = 192
SEGLEN = 64
SEG_DEV = 32


PRECISE = lax.Precision.HIGHEST
AFF_SCALE = 8.0
SEG_BLOCK = 8
WIN = SEGLEN + 8
CONV_ROWS = 256
ONE_HOT_LIMIT = 1 << 20


def _pool_kernel(starts_ref, frames_ref, w_ref, b_ref, out_ref, x3_ref, act_ref):
    rows = frames_ref.shape[0]
    slots = out_ref.shape[0]
    frames = frames_ref[...]
    x3_ref[...] = jnp.concatenate(
        [pltpu.roll(frames, 1, 0), frames, pltpu.roll(frames, rows - 1, 0)], axis=1
    )
    chunk = CONV_ROWS if rows % CONV_ROWS == 0 else rows

    def conv_chunk(c, carry):
        base = pl.multiple_of(c * chunk, chunk)
        preact = jnp.dot(
            x3_ref[pl.ds(base, chunk), :],
            w_ref[...],
            precision=PRECISE,
            preferred_element_type=jnp.float32,
        )
        act_ref[pl.ds(base, chunk), :] = jnp.maximum(preact + b_ref[...], 0.0)
        return carry

    lax.fori_loop(0, rows // chunk, conv_chunk, 0)
    frame_idx = lax.broadcasted_iota(jnp.int32, (WIN, CH), 0)

    def stats_block(blk, carry):
        means = []
        stds = []
        for j in range(SEG_BLOCK):
            start = starts_ref[blk * SEG_BLOCK + j]
            base = jnp.minimum((start // 8) * 8, rows - WIN)
            shift = start - base
            inside = (frame_idx >= shift) & (frame_idx < shift + SEGLEN)
            seg_act = act_ref[pl.ds(pl.multiple_of(base, 8), WIN), :]
            frame_mean = jnp.sum(jnp.where(inside, seg_act, 0.0), axis=0, keepdims=True) / SEGLEN
            deviation = jnp.where(inside, seg_act - frame_mean, 0.0)
            frame_var = jnp.sum(deviation * deviation, axis=0, keepdims=True) / SEGLEN
            means.append(frame_mean)
            stds.append(jnp.sqrt(frame_var + 1e-05))
        row0 = pl.multiple_of(blk * SEG_BLOCK, SEG_BLOCK)
        out_ref[pl.ds(row0, SEG_BLOCK), :CH] = jnp.concatenate(means, axis=0)
        out_ref[pl.ds(row0, SEG_BLOCK), CH:] = jnp.concatenate(stds, axis=0)
        return carry

    lax.fori_loop(0, slots // SEG_BLOCK, stats_block, 0)


def pool_slots(frames, seg_start, conv_weight, conv_bias):
    rows = frames.shape[0]
    slots = seg_start.shape[0]
    starts = jnp.clip(seg_start, 0, rows - SEGLEN).astype(jnp.int32)
    vmem = pltpu.MemorySpace.VMEM
    return pl.pallas_call(
        _pool_kernel,
        out_shape=jax.ShapeDtypeStruct((slots, 2 * CH), jnp.float32),
        in_specs=[
            pl.BlockSpec(memory_space=pltpu.MemorySpace.SMEM),
            pl.BlockSpec(memory_space=vmem),
            pl.BlockSpec(memory_space=vmem),
            pl.BlockSpec(memory_space=vmem),
        ],
        out_specs=pl.BlockSpec(memory_space=vmem),
        scratch_shapes=[
            pltpu.VMEM((rows, 3 * FEAT), jnp.float32),
            pltpu.VMEM((rows, CH), jnp.float32),
        ],
        compiler_params=pltpu.CompilerParams(vmem_limit_bytes=48 * 1024 * 1024),
        cost_estimate=pl.CostEstimate(
            flops=2 * rows * 3 * FEAT * CH * 6 + 8 * slots * WIN * CH,
            transcendentals=slots * CH,
            bytes_accessed=rows * FEAT * 4 + 3 * FEAT * CH * 4 + slots * 2 * CH * 4,
        ),
    )(starts, frames, conv_weight, conv_bias.reshape(1, CH))


def _affinity_kernel(k_ref, row_unit_ref, col_unit_ref, row_rec_ref, col_rec_ref, out_ref, pad_ref):
    height, width = out_ref.shape
    scores = lax.dot_general(
        row_unit_ref[...],
        col_unit_ref[...],
        (((1,), (1,)), ((), ())),
        preferred_element_type=jnp.float32,
    )
    affinity = jnp.where(row_rec_ref[...] == col_rec_ref[...], 0.0, AFF_SCALE * scores)
    pad_ref[...] = jnp.zeros(pad_ref.shape, jnp.float32)
    pad_ref[0 : height + 2, 1 : width + 1] = affinity
    result = jnp.zeros((height, width), jnp.float32)
    for row_off in range(3):
        for col_off in range(3):
            result = result + k_ref[row_off, col_off] * pad_ref[
                row_off : row_off + height, col_off : col_off + width
            ]
    out_ref[...] = result


def smooth_affinity(row_unit, col_unit, row_rec, col_rec, smooth_kernel):
    height = row_unit.shape[0] - 2
    width = col_unit.shape[0]
    vmem = pltpu.MemorySpace.VMEM
    return pl.pallas_call(
        _affinity_kernel,
        out_shape=jax.ShapeDtypeStruct((height, width), jnp.float32),
        in_specs=[pl.BlockSpec(memory_space=pltpu.MemorySpace.SMEM)]
        + [pl.BlockSpec(memory_space=vmem)] * 4,
        out_specs=pl.BlockSpec(memory_space=vmem),
        scratch_shapes=[
            pltpu.VMEM((-(-(height + 2) // 8) * 8, -(-(width + 2) // 128) * 128), jnp.float32)
        ],
        compiler_params=pltpu.CompilerParams(vmem_limit_bytes=48 * 1024 * 1024),
        cost_estimate=pl.CostEstimate(
            flops=2 * (height + 2) * width * EMB + 20 * height * width,
            transcendentals=0,
            bytes_accessed=(width + height + 2) * EMB * 2 + height * width * 4,
        ),
    )(smooth_kernel, row_unit, col_unit, row_rec.reshape(-1, 1), col_rec.reshape(1, -1))


def gather_wide(x, group_size):
    lanes = -(-x.shape[1] // 256) * 256
    wide = jnp.pad(x, ((0, 0), (0, lanes - x.shape[1])))
    every = lax.all_gather(wide, "wide", axis=0, tiled=False)
    return every[:, :, : x.shape[1]], jnp.arange(group_size, dtype=jnp.int32)


def per_device(
    frames, seg_start, seg_dest, rec_id, conv_weight, conv_bias, proj_weight, smooth_kernel
):
    group_size = lax.axis_size("wide")
    total_rows = SEG_DEV * group_size
    pooled = pool_slots(frames, seg_start, conv_weight, conv_bias)
    embedded = jnp.dot(pooled, proj_weight, precision=PRECISE, preferred_element_type=jnp.float32)
    packed = jnp.concatenate(
        [
            embedded,
            seg_dest.astype(jnp.float32)[:, None],
            rec_id.astype(jnp.float32)[:, None],
        ],
        axis=1,
    )
    blocks, source = gather_wide(packed, group_size)
    per_block = packed.shape[0]
    every = blocks.reshape(group_size * per_block, packed.shape[1])
    slot_ids = (
        source[:, None] * per_block + jnp.arange(per_block, dtype=jnp.int32)[None, :]
    ).reshape(-1)
    all_emb = every[:, :EMB]
    all_dest = every[:, EMB].astype(jnp.int32)
    all_rec = every[:, EMB + 1].astype(jnp.int32)
    slot_total = all_dest.shape[0]
    used = all_dest >= 0

    mean_sum = jnp.sum(jnp.where(used[:, None], all_emb, 0.0), axis=0)
    centred = all_emb - mean_sum / total_rows
    unit = (centred / jnp.sqrt(jnp.sum(centred * centred, axis=1, keepdims=True) + 1e-06)).astype(
        jnp.bfloat16
    )

    earlier = (slot_ids[None, :] < slot_ids[:, None]) & (all_dest[None, :] == all_dest[:, None])
    rank = jnp.sum(earlier.astype(jnp.int32), axis=1)
    position = jnp.where(used, all_dest * SEG_DEV + rank, -1)
    picks = position[None, :] == jnp.arange(total_rows, dtype=jnp.int32)[:, None]
    row_ids = jnp.arange(slot_total, dtype=jnp.int32)
    slot_of_pos = jnp.sum(jnp.where(picks, row_ids[None, :], 0), axis=1)

    if total_rows * slot_total <= ONE_HOT_LIMIT:
        rec_hi = (all_rec // 16).astype(jnp.bfloat16)[:, None]
        rec_lo = (all_rec % 16).astype(jnp.bfloat16)[:, None]
        unit_ext = jnp.concatenate([unit, rec_hi, rec_lo], axis=1)
        selector = picks.astype(jnp.bfloat16)
        col_ext = jnp.dot(selector, unit_ext, preferred_element_type=jnp.float32)
        col_unit = col_ext[:, :EMB].astype(jnp.bfloat16)
        col_rec = (col_ext[:, EMB] * 16 + col_ext[:, EMB + 1]).astype(jnp.int32)
    else:
        col_unit = jnp.take(unit, slot_of_pos, axis=0)
        col_rec = jnp.take(all_rec, slot_of_pos, axis=0)
    zero_unit = jnp.zeros((1, EMB), jnp.bfloat16)
    pad_unit = jnp.concatenate([zero_unit, col_unit, zero_unit], axis=0)
    pad_rec = jnp.concatenate([jnp.full((1,), -1, jnp.int32), col_rec, jnp.full((1,), -1, jnp.int32)])
    my_index = lax.axis_index("wide")
    row_unit = lax.dynamic_slice_in_dim(pad_unit, my_index * SEG_DEV, SEG_DEV + 2, 0)
    row_rec = lax.dynamic_slice_in_dim(pad_rec, my_index * SEG_DEV, SEG_DEV + 2, 0)
    return smooth_affinity(row_unit, col_unit, row_rec, col_rec, smooth_kernel)


def solution(mesh):
    in_specs = (
        P(("parts", "wide"), None),
        P(("parts", "wide")),
        P(("parts", "wide")),
        P(("parts", "wide")),
        P(),
        P(),
        P(),
        P(),
    )
    out_specs = P(("parts", "wide"), None)
    return jax.shard_map(
        per_device, mesh=mesh, in_specs=in_specs, out_specs=out_specs, check_vma=False
    )
```

```python
import functools

import jax
import jax.numpy as jnp
from jax import lax
from jax.experimental import pallas as pl
from jax.experimental.pallas import tpu as pltpu
from jax.sharding import PartitionSpec as P

FEAT = 80
CH = 1024
EMB = 192
SEGLEN = 64
SEG_DEV = 32


PRECISE = lax.Precision.HIGHEST
AFF_SCALE = 8.0
SEG_BLOCK = 8
WIN = SEGLEN + 8
CONV_ROWS = 256
ONE_HOT_LIMIT = 1 << 20


def _pool_kernel(
    starts_ref, frames_hbm, w_hbm, b_ref, out_ref, frames_ref, w_ref, x3_ref, act_ref, sem
):
    rows = frames_ref.shape[0]
    slots = out_ref.shape[0]
    frames_copy = pltpu.make_async_copy(frames_hbm, frames_ref, sem.at[0])
    w_copy = pltpu.make_async_copy(w_hbm, w_ref, sem.at[1])
    frames_copy.start()
    w_copy.start()
    frames_copy.wait()
    frames = frames_ref[...]
    x3_ref[...] = jnp.concatenate(
        [pltpu.roll(frames, 1, 0), frames, pltpu.roll(frames, rows - 1, 0)], axis=1
    )
    chunk = CONV_ROWS if rows % CONV_ROWS == 0 else rows
    w_copy.wait()

    def conv_chunk(c, carry):
        base = pl.multiple_of(c * chunk, chunk)
        preact = jnp.dot(
            x3_ref[pl.ds(base, chunk), :],
            w_ref[...],
            precision=PRECISE,
            preferred_element_type=jnp.float32,
        )
        act_ref[pl.ds(base, chunk), :] = jnp.maximum(preact + b_ref[...], 0.0)
        return carry

    lax.fori_loop(0, rows // chunk, conv_chunk, 0)
    frame_idx = lax.broadcasted_iota(jnp.int32, (WIN, CH), 0)

    def stats_block(blk, carry):
        means = []
        stds = []
        for j in range(SEG_BLOCK):
            start = starts_ref[blk * SEG_BLOCK + j]
            base = jnp.minimum((start // 8) * 8, rows - WIN)
            shift = start - base
            inside = (frame_idx >= shift) & (frame_idx < shift + SEGLEN)
            seg_act = act_ref[pl.ds(pl.multiple_of(base, 8), WIN), :]
            frame_mean = jnp.sum(jnp.where(inside, seg_act, 0.0), axis=0, keepdims=True) / SEGLEN
            deviation = jnp.where(inside, seg_act - frame_mean, 0.0)
            frame_var = jnp.sum(deviation * deviation, axis=0, keepdims=True) / SEGLEN
            means.append(frame_mean)
            stds.append(jnp.sqrt(frame_var + 1e-05))
        row0 = pl.multiple_of(blk * SEG_BLOCK, SEG_BLOCK)
        out_ref[pl.ds(row0, SEG_BLOCK), :CH] = jnp.concatenate(means, axis=0)
        out_ref[pl.ds(row0, SEG_BLOCK), CH:] = jnp.concatenate(stds, axis=0)
        return carry

    lax.fori_loop(0, slots // SEG_BLOCK, stats_block, 0)


def pool_slots(frames, seg_start, conv_weight, conv_bias):
    rows = frames.shape[0]
    slots = seg_start.shape[0]
    starts = jnp.clip(seg_start, 0, rows - SEGLEN).astype(jnp.int32)
    vmem = pltpu.MemorySpace.VMEM
    return pl.pallas_call(
        _pool_kernel,
        out_shape=jax.ShapeDtypeStruct((slots, 2 * CH), jnp.float32),
        in_specs=[
            pl.BlockSpec(memory_space=pltpu.MemorySpace.SMEM),
            pl.BlockSpec(memory_space=pl.ANY),
            pl.BlockSpec(memory_space=pl.ANY),
            pl.BlockSpec(memory_space=vmem),
        ],
        out_specs=pl.BlockSpec(memory_space=vmem),
        scratch_shapes=[
            pltpu.VMEM((rows, FEAT), jnp.float32),
            pltpu.VMEM((3 * FEAT, CH), jnp.float32),
            pltpu.VMEM((rows, 3 * FEAT), jnp.float32),
            pltpu.VMEM((rows, CH), jnp.float32),
            pltpu.SemaphoreType.DMA((2,)),
        ],
        compiler_params=pltpu.CompilerParams(vmem_limit_bytes=48 * 1024 * 1024),
        cost_estimate=pl.CostEstimate(
            flops=2 * rows * 3 * FEAT * CH * 6 + 8 * slots * WIN * CH,
            transcendentals=slots * CH,
            bytes_accessed=rows * FEAT * 4 + 3 * FEAT * CH * 4 + slots * 2 * CH * 4,
        ),
    )(starts, frames, conv_weight, conv_bias.reshape(1, CH))


def _affinity_kernel(k_ref, row_unit_ref, col_unit_ref, row_rec_ref, col_rec_ref, out_ref, pad_ref):
    height, width = out_ref.shape
    scores = lax.dot_general(
        row_unit_ref[...],
        col_unit_ref[...],
        (((1,), (1,)), ((), ())),
        preferred_element_type=jnp.float32,
    )
    affinity = jnp.where(row_rec_ref[...] == col_rec_ref[...], 0.0, AFF_SCALE * scores)
    pad_ref[...] = jnp.zeros(pad_ref.shape, jnp.float32)
    pad_ref[0 : height + 2, 1 : width + 1] = affinity
    result = jnp.zeros((height, width), jnp.float32)
    for row_off in range(3):
        for col_off in range(3):
            result = result + k_ref[row_off, col_off] * pad_ref[
                row_off : row_off + height, col_off : col_off + width
            ]
    out_ref[...] = result


def smooth_affinity(row_unit, col_unit, row_rec, col_rec, smooth_kernel):
    height = row_unit.shape[0] - 2
    width = col_unit.shape[0]
    vmem = pltpu.MemorySpace.VMEM
    return pl.pallas_call(
        _affinity_kernel,
        out_shape=jax.ShapeDtypeStruct((height, width), jnp.float32),
        in_specs=[pl.BlockSpec(memory_space=pltpu.MemorySpace.SMEM)]
        + [pl.BlockSpec(memory_space=vmem)] * 4,
        out_specs=pl.BlockSpec(memory_space=vmem),
        scratch_shapes=[
            pltpu.VMEM((-(-(height + 2) // 8) * 8, -(-(width + 2) // 128) * 128), jnp.float32)
        ],
        compiler_params=pltpu.CompilerParams(vmem_limit_bytes=48 * 1024 * 1024),
        cost_estimate=pl.CostEstimate(
            flops=2 * (height + 2) * width * EMB + 20 * height * width,
            transcendentals=0,
            bytes_accessed=(width + height + 2) * EMB * 2 + height * width * 4,
        ),
    )(smooth_kernel, row_unit, col_unit, row_rec.reshape(-1, 1), col_rec.reshape(1, -1))


def gather_wide(x, group_size):
    my_index = lax.axis_index("wide")
    if group_size % 2 or group_size & (group_size - 1):
        every = lax.all_gather(x, "wide", axis=0, tiled=False)
        return every, jnp.arange(group_size, dtype=jnp.int32)
    pattern = [0]
    blocks = [x]
    for flip in range(2, group_size, 2):
        perm = [(i, i ^ flip) for i in range(group_size)]
        blocks.append(lax.ppermute(x, "wide", perm))
        pattern.append(flip)
    buf = jnp.stack(blocks, axis=0)
    perm = [(i, i ^ 1) for i in range(group_size)]
    buf = jnp.concatenate([buf, lax.ppermute(buf, "wide", perm)], axis=0)
    pattern = pattern + [p ^ 1 for p in pattern]
    source = jnp.asarray(pattern, dtype=jnp.int32) ^ my_index
    return buf, source


def per_device(
    frames, seg_start, seg_dest, rec_id, conv_weight, conv_bias, proj_weight, smooth_kernel
):
    group_size = lax.axis_size("wide")
    total_rows = SEG_DEV * group_size
    pooled = pool_slots(frames, seg_start, conv_weight, conv_bias)
    embedded = jnp.dot(pooled, proj_weight, precision=PRECISE, preferred_element_type=jnp.float32)
    slots = embedded.shape[0]
    meta = jnp.concatenate(
        [seg_dest.astype(jnp.float32), rec_id.astype(jnp.float32)]
    )
    if meta.shape[0] <= EMB:
        meta_rows = jnp.zeros((8, EMB), jnp.float32).at[0, : meta.shape[0]].set(meta)
    else:
        meta_rows = jnp.zeros((-(-meta.shape[0] // EMB) // 8 * 8 + 8, EMB), jnp.float32)
        meta_rows = meta_rows.reshape(-1).at[: meta.shape[0]].set(meta).reshape(-1, EMB)
    packed = jnp.concatenate([embedded, meta_rows], axis=0)
    blocks, source = gather_wide(packed, group_size)
    per_block = slots
    all_emb = blocks[:, :slots, :].reshape(group_size * slots, EMB)
    meta_all = blocks[:, slots:, :].reshape(group_size, -1)[:, : 2 * slots]
    all_dest = meta_all[:, :slots].reshape(-1).astype(jnp.int32)
    all_rec = meta_all[:, slots:].reshape(-1).astype(jnp.int32)
    slot_ids = (
        source[:, None] * per_block + jnp.arange(per_block, dtype=jnp.int32)[None, :]
    ).reshape(-1)
    slot_total = all_dest.shape[0]
    used = all_dest >= 0

    mean_sum = jnp.sum(jnp.where(used[:, None], all_emb, 0.0), axis=0)
    centred = all_emb - mean_sum / total_rows
    unit = (centred / jnp.sqrt(jnp.sum(centred * centred, axis=1, keepdims=True) + 1e-06)).astype(
        jnp.bfloat16
    )

    earlier = (slot_ids[None, :] < slot_ids[:, None]) & (all_dest[None, :] == all_dest[:, None])
    rank = jnp.sum(earlier.astype(jnp.int32), axis=1)
    position = jnp.where(used, all_dest * SEG_DEV + rank, -1)
    picks = position[None, :] == jnp.arange(total_rows, dtype=jnp.int32)[:, None]
    row_ids = jnp.arange(slot_total, dtype=jnp.int32)
    slot_of_pos = jnp.sum(jnp.where(picks, row_ids[None, :], 0), axis=1)

    if total_rows * slot_total <= ONE_HOT_LIMIT:
        rec_hi = (all_rec // 16).astype(jnp.bfloat16)[:, None]
        rec_lo = (all_rec % 16).astype(jnp.bfloat16)[:, None]
        unit_ext = jnp.concatenate([unit, rec_hi, rec_lo], axis=1)
        selector = picks.astype(jnp.bfloat16)
        col_ext = jnp.dot(selector, unit_ext, preferred_element_type=jnp.float32)
        col_unit = col_ext[:, :EMB].astype(jnp.bfloat16)
        col_rec = (col_ext[:, EMB] * 16 + col_ext[:, EMB + 1]).astype(jnp.int32)
    else:
        col_unit = jnp.take(unit, slot_of_pos, axis=0)
        col_rec = jnp.take(all_rec, slot_of_pos, axis=0)
    zero_unit = jnp.zeros((1, EMB), jnp.bfloat16)
    pad_unit = jnp.concatenate([zero_unit, col_unit, zero_unit], axis=0)
    pad_rec = jnp.concatenate([jnp.full((1,), -1, jnp.int32), col_rec, jnp.full((1,), -1, jnp.int32)])
    my_index = lax.axis_index("wide")
    row_unit = lax.dynamic_slice_in_dim(pad_unit, my_index * SEG_DEV, SEG_DEV + 2, 0)
    row_rec = lax.dynamic_slice_in_dim(pad_rec, my_index * SEG_DEV, SEG_DEV + 2, 0)
    return smooth_affinity(row_unit, col_unit, row_rec, col_rec, smooth_kernel)


def solution(mesh):
    in_specs = (
        P(("parts", "wide"), None),
        P(("parts", "wide")),
        P(("parts", "wide")),
        P(("parts", "wide")),
        P(),
        P(),
        P(),
        P(),
    )
    out_specs = P(("parts", "wide"), None)
    return jax.shard_map(
        per_device, mesh=mesh, in_specs=in_specs, out_specs=out_specs, check_vma=False
    )
```

```python
import functools

import jax
import jax.numpy as jnp
from jax import lax
from jax.experimental import pallas as pl
from jax.experimental.pallas import tpu as pltpu
from jax.sharding import PartitionSpec as P

FEAT = 80
CH = 1024
EMB = 192
SEGLEN = 64
SEG_DEV = 32


PRECISE = lax.Precision.HIGHEST
AFF_SCALE = 8.0
SEG_BLOCK = 8
WIN = SEGLEN + 8
CONV_ROWS = 256
ONE_HOT_LIMIT = 1 << 20
VMEM_ALL = 67043328


def _pool_kernel(
    starts_ref, frames_hbm, w_hbm, b_ref, out_ref, frames_ref, w_ref, x3_ref, act_ref, sem
):
    rows = frames_ref.shape[1]
    slots = out_ref.shape[0]
    frames_copy = pltpu.make_async_copy(frames_hbm, frames_ref, sem.at[0])
    w_copy = pltpu.make_async_copy(w_hbm, w_ref, sem.at[1])
    frames_copy.start()
    w_copy.start()
    frames_copy.wait()
    frames = jnp.transpose(frames_ref[...])
    x3_ref[...] = jnp.concatenate(
        [pltpu.roll(frames, 1, 0), frames, pltpu.roll(frames, rows - 1, 0)], axis=1
    )
    chunk = CONV_ROWS if rows % CONV_ROWS == 0 else rows
    w_copy.wait()

    def conv_chunk(c, carry):
        base = pl.multiple_of(c * chunk, chunk)
        preact = jnp.dot(
            x3_ref[pl.ds(base, chunk), :],
            w_ref[...],
            precision=PRECISE,
            preferred_element_type=jnp.float32,
        )
        act_ref[pl.ds(base, chunk), :] = jnp.maximum(preact + b_ref[...], 0.0)
        return carry

    lax.fori_loop(0, rows // chunk, conv_chunk, 0)
    frame_idx = lax.broadcasted_iota(jnp.int32, (WIN, CH), 0)

    def stats_block(blk, carry):
        means = []
        stds = []
        for j in range(SEG_BLOCK):
            start = starts_ref[blk * SEG_BLOCK + j]
            base = jnp.minimum((start // 8) * 8, rows - WIN)
            shift = start - base
            inside = (frame_idx >= shift) & (frame_idx < shift + SEGLEN)
            seg_act = act_ref[pl.ds(pl.multiple_of(base, 8), WIN), :]
            frame_mean = jnp.sum(jnp.where(inside, seg_act, 0.0), axis=0, keepdims=True) / SEGLEN
            deviation = jnp.where(inside, seg_act - frame_mean, 0.0)
            frame_var = jnp.sum(deviation * deviation, axis=0, keepdims=True) / SEGLEN
            means.append(frame_mean)
            stds.append(jnp.sqrt(frame_var + 1e-05))
        row0 = pl.multiple_of(blk * SEG_BLOCK, SEG_BLOCK)
        out_ref[pl.ds(row0, SEG_BLOCK), :CH] = jnp.concatenate(means, axis=0)
        out_ref[pl.ds(row0, SEG_BLOCK), CH:] = jnp.concatenate(stds, axis=0)
        return carry

    lax.fori_loop(0, slots // SEG_BLOCK, stats_block, 0)


def pool_slots(frames, seg_start, conv_weight, conv_bias):
    rows = frames.shape[0]
    slots = seg_start.shape[0]
    starts = jnp.clip(seg_start, 0, rows - SEGLEN).astype(jnp.int32)
    vmem = pltpu.MemorySpace.VMEM
    return pl.pallas_call(
        _pool_kernel,
        out_shape=jax.ShapeDtypeStruct((slots, 2 * CH), jnp.float32),
        in_specs=[
            pl.BlockSpec(memory_space=pltpu.MemorySpace.SMEM),
            pl.BlockSpec(memory_space=pl.ANY),
            pl.BlockSpec(memory_space=pl.ANY),
            pl.BlockSpec(memory_space=vmem),
        ],
        out_specs=pl.BlockSpec(memory_space=vmem),
        scratch_shapes=[
            pltpu.VMEM((FEAT, rows), jnp.float32),
            pltpu.VMEM((3 * FEAT, CH), jnp.float32),
            pltpu.VMEM((rows, 3 * FEAT), jnp.float32),
            pltpu.VMEM((rows, CH), jnp.float32),
            pltpu.SemaphoreType.DMA((2,)),
        ],
        compiler_params=pltpu.CompilerParams(vmem_limit_bytes=VMEM_ALL),
        cost_estimate=pl.CostEstimate(
            flops=2 * rows * 3 * FEAT * CH * 6 + 8 * slots * WIN * CH,
            transcendentals=slots * CH,
            bytes_accessed=rows * FEAT * 4 + 3 * FEAT * CH * 4 + slots * 2 * CH * 4,
        ),
    )(starts, frames.T, conv_weight, conv_bias.reshape(1, CH))


def _affinity_kernel(k_ref, row_unit_ref, col_unit_ref, row_rec_ref, col_rec_ref, out_ref, pad_ref):
    height, width = out_ref.shape
    scores = lax.dot_general(
        row_unit_ref[...],
        col_unit_ref[...],
        (((1,), (1,)), ((), ())),
        preferred_element_type=jnp.float32,
    )
    affinity = jnp.where(row_rec_ref[...] == col_rec_ref[...], 0.0, AFF_SCALE * scores)
    pad_ref[...] = jnp.zeros(pad_ref.shape, jnp.float32)
    pad_ref[0 : height + 2, 1 : width + 1] = affinity
    result = jnp.zeros((height, width), jnp.float32)
    for row_off in range(3):
        for col_off in range(3):
            result = result + k_ref[row_off, col_off] * pad_ref[
                row_off : row_off + height, col_off : col_off + width
            ]
    out_ref[...] = result


def smooth_affinity(row_unit, col_unit, row_rec, col_rec, smooth_kernel):
    height = row_unit.shape[0] - 2
    width = col_unit.shape[0]
    vmem = pltpu.MemorySpace.VMEM
    return pl.pallas_call(
        _affinity_kernel,
        out_shape=jax.ShapeDtypeStruct((height, width), jnp.float32),
        in_specs=[pl.BlockSpec(memory_space=pltpu.MemorySpace.SMEM)]
        + [pl.BlockSpec(memory_space=vmem)] * 4,
        out_specs=pl.BlockSpec(memory_space=vmem),
        scratch_shapes=[
            pltpu.VMEM((-(-(height + 2) // 8) * 8, -(-(width + 2) // 128) * 128), jnp.float32)
        ],
        compiler_params=pltpu.CompilerParams(vmem_limit_bytes=48 * 1024 * 1024),
        cost_estimate=pl.CostEstimate(
            flops=2 * (height + 2) * width * EMB + 20 * height * width,
            transcendentals=0,
            bytes_accessed=(width + height + 2) * EMB * 2 + height * width * 4,
        ),
    )(smooth_kernel, row_unit, col_unit, row_rec.reshape(-1, 1), col_rec.reshape(1, -1))


def gather_wide(x, group_size):
    my_index = lax.axis_index("wide")
    if group_size % 2 or group_size & (group_size - 1):
        every = lax.all_gather(x, "wide", axis=0, tiled=False)
        return every, jnp.arange(group_size, dtype=jnp.int32)
    pattern = [0]
    blocks = [x]
    for flip in range(2, group_size, 2):
        perm = [(i, i ^ flip) for i in range(group_size)]
        blocks.append(lax.ppermute(x, "wide", perm))
        pattern.append(flip)
    buf = jnp.stack(blocks, axis=0)
    perm = [(i, i ^ 1) for i in range(group_size)]
    buf = jnp.concatenate([buf, lax.ppermute(buf, "wide", perm)], axis=0)
    pattern = pattern + [p ^ 1 for p in pattern]
    source = jnp.asarray(pattern, dtype=jnp.int32) ^ my_index
    return buf, source


def per_device(
    frames, seg_start, seg_dest, rec_id, conv_weight, conv_bias, proj_weight, smooth_kernel
):
    group_size = lax.axis_size("wide")
    total_rows = SEG_DEV * group_size
    pooled = pool_slots(frames, seg_start, conv_weight, conv_bias)
    embedded = jnp.dot(pooled, proj_weight, precision=PRECISE, preferred_element_type=jnp.float32)
    slots = embedded.shape[0]
    meta = jnp.concatenate(
        [seg_dest.astype(jnp.float32), rec_id.astype(jnp.float32)]
    )
    if meta.shape[0] <= EMB:
        meta_rows = jnp.zeros((8, EMB), jnp.float32).at[0, : meta.shape[0]].set(meta)
    else:
        meta_rows = jnp.zeros((-(-meta.shape[0] // EMB) // 8 * 8 + 8, EMB), jnp.float32)
        meta_rows = meta_rows.reshape(-1).at[: meta.shape[0]].set(meta).reshape(-1, EMB)
    packed = jnp.concatenate([embedded, meta_rows], axis=0)
    blocks, source = gather_wide(packed, group_size)
    per_block = slots
    all_emb = blocks[:, :slots, :].reshape(group_size * slots, EMB)
    meta_all = blocks[:, slots:, :].reshape(group_size, -1)[:, : 2 * slots]
    all_dest = meta_all[:, :slots].reshape(-1).astype(jnp.int32)
    all_rec = meta_all[:, slots:].reshape(-1).astype(jnp.int32)
    slot_ids = (
        source[:, None] * per_block + jnp.arange(per_block, dtype=jnp.int32)[None, :]
    ).reshape(-1)
    slot_total = all_dest.shape[0]
    used = all_dest >= 0

    mean_sum = jnp.sum(jnp.where(used[:, None], all_emb, 0.0), axis=0)
    centred = all_emb - mean_sum / total_rows
    unit = (centred / jnp.sqrt(jnp.sum(centred * centred, axis=1, keepdims=True) + 1e-06)).astype(
        jnp.bfloat16
    )

    earlier = (slot_ids[None, :] < slot_ids[:, None]) & (all_dest[None, :] == all_dest[:, None])
    rank = jnp.sum(earlier.astype(jnp.int32), axis=1)
    position = jnp.where(used, all_dest * SEG_DEV + rank, -1)
    picks = position[None, :] == jnp.arange(total_rows, dtype=jnp.int32)[:, None]
    row_ids = jnp.arange(slot_total, dtype=jnp.int32)
    slot_of_pos = jnp.sum(jnp.where(picks, row_ids[None, :], 0), axis=1)

    if total_rows * slot_total <= ONE_HOT_LIMIT:
        rec_hi = (all_rec // 16).astype(jnp.bfloat16)[:, None]
        rec_lo = (all_rec % 16).astype(jnp.bfloat16)[:, None]
        unit_ext = jnp.concatenate([unit, rec_hi, rec_lo], axis=1)
        selector = picks.astype(jnp.bfloat16)
        col_ext = jnp.dot(selector, unit_ext, preferred_element_type=jnp.float32)
        col_unit = col_ext[:, :EMB].astype(jnp.bfloat16)
        col_rec = (col_ext[:, EMB] * 16 + col_ext[:, EMB + 1]).astype(jnp.int32)
    else:
        col_unit = jnp.take(unit, slot_of_pos, axis=0)
        col_rec = jnp.take(all_rec, slot_of_pos, axis=0)
    zero_unit = jnp.zeros((1, EMB), jnp.bfloat16)
    pad_unit = jnp.concatenate([zero_unit, col_unit, zero_unit], axis=0)
    pad_rec = jnp.concatenate([jnp.full((1,), -1, jnp.int32), col_rec, jnp.full((1,), -1, jnp.int32)])
    my_index = lax.axis_index("wide")
    row_unit = lax.dynamic_slice_in_dim(pad_unit, my_index * SEG_DEV, SEG_DEV + 2, 0)
    row_rec = lax.dynamic_slice_in_dim(pad_rec, my_index * SEG_DEV, SEG_DEV + 2, 0)
    return smooth_affinity(row_unit, col_unit, row_rec, col_rec, smooth_kernel)


def solution(mesh):
    in_specs = (
        P(("parts", "wide"), None),
        P(("parts", "wide")),
        P(("parts", "wide")),
        P(("parts", "wide")),
        P(),
        P(),
        P(),
        P(),
    )
    out_specs = P(("parts", "wide"), None)
    return jax.shard_map(
        per_device, mesh=mesh, in_specs=in_specs, out_specs=out_specs, check_vma=False
    )
```

```python
import functools

import jax
import jax.numpy as jnp
from jax import lax
from jax.experimental import pallas as pl
from jax.experimental.pallas import tpu as pltpu
from jax.sharding import PartitionSpec as P

FEAT = 80
CH = 1024
EMB = 192
SEGLEN = 64
SEG_DEV = 32


PRECISE = lax.Precision.HIGHEST
AFF_SCALE = 8.0
SEG_BLOCK = 8
WIN = SEGLEN + 8
CONV_ROWS = 256
ONE_HOT_LIMIT = 1 << 20


def _pool_kernel(
    starts_ref, frames_hbm, w_hbm, b_ref, out_ref, frames_ref, w_ref, x3_ref, act_ref, sem
):
    rows = frames_ref.shape[1]
    slots = out_ref.shape[0]
    frames_copy = pltpu.make_async_copy(frames_hbm, frames_ref, sem.at[0])
    w_copy = pltpu.make_async_copy(w_hbm, w_ref, sem.at[1])
    frames_copy.start()
    w_copy.start()
    frames_copy.wait()
    frames = jnp.transpose(frames_ref[...])
    x3_ref[...] = jnp.concatenate(
        [pltpu.roll(frames, 1, 0), frames, pltpu.roll(frames, rows - 1, 0)], axis=1
    )
    chunk = CONV_ROWS if rows % CONV_ROWS == 0 else rows
    w_copy.wait()

    def conv_chunk(c, carry):
        base = pl.multiple_of(c * chunk, chunk)
        preact = jnp.dot(
            x3_ref[pl.ds(base, chunk), :],
            w_ref[...],
            precision=PRECISE,
            preferred_element_type=jnp.float32,
        )
        act_ref[pl.ds(base, chunk), :] = jnp.maximum(preact + b_ref[...], 0.0)
        return carry

    lax.fori_loop(0, rows // chunk, conv_chunk, 0)
    frame_idx = lax.broadcasted_iota(jnp.int32, (WIN, CH), 0)

    def stats_block(blk, carry):
        means = []
        stds = []
        for j in range(SEG_BLOCK):
            start = starts_ref[blk * SEG_BLOCK + j]
            base = jnp.minimum((start // 8) * 8, rows - WIN)
            shift = start - base
            inside = (frame_idx >= shift) & (frame_idx < shift + SEGLEN)
            seg_act = act_ref[pl.ds(pl.multiple_of(base, 8), WIN), :]
            frame_mean = jnp.sum(jnp.where(inside, seg_act, 0.0), axis=0, keepdims=True) / SEGLEN
            deviation = jnp.where(inside, seg_act - frame_mean, 0.0)
            frame_var = jnp.sum(deviation * deviation, axis=0, keepdims=True) / SEGLEN
            means.append(frame_mean)
            stds.append(jnp.sqrt(frame_var + 1e-05))
        row0 = pl.multiple_of(blk * SEG_BLOCK, SEG_BLOCK)
        out_ref[pl.ds(row0, SEG_BLOCK), :CH] = jnp.concatenate(means, axis=0)
        out_ref[pl.ds(row0, SEG_BLOCK), CH:] = jnp.concatenate(stds, axis=0)
        return carry

    lax.fori_loop(0, slots // SEG_BLOCK, stats_block, 0)


def pool_slots(frames, seg_start, conv_weight, conv_bias):
    rows = frames.shape[0]
    slots = seg_start.shape[0]
    starts = jnp.clip(seg_start, 0, rows - SEGLEN).astype(jnp.int32)
    vmem = pltpu.MemorySpace.VMEM
    return pl.pallas_call(
        _pool_kernel,
        out_shape=jax.ShapeDtypeStruct((slots, 2 * CH), jnp.float32),
        in_specs=[
            pl.BlockSpec(memory_space=pltpu.MemorySpace.SMEM),
            pl.BlockSpec(memory_space=pl.ANY),
            pl.BlockSpec(memory_space=pl.ANY),
            pl.BlockSpec(memory_space=vmem),
        ],
        out_specs=pl.BlockSpec(memory_space=vmem),
        scratch_shapes=[
            pltpu.VMEM((FEAT, rows), jnp.float32),
            pltpu.VMEM((3 * FEAT, CH), jnp.float32),
            pltpu.VMEM((rows, 3 * FEAT), jnp.float32),
            pltpu.VMEM((rows, CH), jnp.float32),
            pltpu.SemaphoreType.DMA((2,)),
        ],
        compiler_params=pltpu.CompilerParams(vmem_limit_bytes=48 * 1024 * 1024),
        cost_estimate=pl.CostEstimate(
            flops=2 * rows * 3 * FEAT * CH * 6 + 8 * slots * WIN * CH,
            transcendentals=slots * CH,
            bytes_accessed=rows * FEAT * 4 + 3 * FEAT * CH * 4 + slots * 2 * CH * 4,
        ),
    )(starts, frames.T, conv_weight, conv_bias.reshape(1, CH))


def _affinity_kernel(k_ref, row_unit_ref, col_unit_ref, row_rec_ref, col_rec_ref, out_ref, pad_ref):
    height, width = out_ref.shape
    scores = lax.dot_general(
        row_unit_ref[...],
        col_unit_ref[...],
        (((1,), (1,)), ((), ())),
        preferred_element_type=jnp.float32,
    )
    affinity = jnp.where(row_rec_ref[...] == col_rec_ref[...], 0.0, AFF_SCALE * scores)
    pad_ref[...] = jnp.zeros(pad_ref.shape, jnp.float32)
    pad_ref[0 : height + 2, 1 : width + 1] = affinity
    result = jnp.zeros((height, width), jnp.float32)
    for row_off in range(3):
        for col_off in range(3):
            result = result + k_ref[row_off, col_off] * pad_ref[
                row_off : row_off + height, col_off : col_off + width
            ]
    out_ref[...] = result


def smooth_affinity(row_unit, col_unit, row_rec, col_rec, smooth_kernel):
    height = row_unit.shape[0] - 2
    width = col_unit.shape[0]
    vmem = pltpu.MemorySpace.VMEM
    return pl.pallas_call(
        _affinity_kernel,
        out_shape=jax.ShapeDtypeStruct((height, width), jnp.float32),
        in_specs=[pl.BlockSpec(memory_space=pltpu.MemorySpace.SMEM)]
        + [pl.BlockSpec(memory_space=vmem)] * 4,
        out_specs=pl.BlockSpec(memory_space=vmem),
        scratch_shapes=[
            pltpu.VMEM((-(-(height + 2) // 8) * 8, -(-(width + 2) // 128) * 128), jnp.float32)
        ],
        compiler_params=pltpu.CompilerParams(vmem_limit_bytes=48 * 1024 * 1024),
        cost_estimate=pl.CostEstimate(
            flops=2 * (height + 2) * width * EMB + 20 * height * width,
            transcendentals=0,
            bytes_accessed=(width + height + 2) * EMB * 2 + height * width * 4,
        ),
    )(smooth_kernel, row_unit, col_unit, row_rec.reshape(-1, 1), col_rec.reshape(1, -1))


def gather_wide(x, group_size):
    my_index = lax.axis_index("wide")
    if group_size % 2 or group_size & (group_size - 1):
        every = lax.all_gather(x, "wide", axis=0, tiled=False)
        return every, jnp.arange(group_size, dtype=jnp.int32)
    pattern = [0]
    blocks = [x]
    for flip in range(2, group_size, 2):
        perm = [(i, i ^ flip) for i in range(group_size)]
        blocks.append(lax.ppermute(x, "wide", perm))
        pattern.append(flip)
    buf = jnp.stack(blocks, axis=0)
    perm = [(i, i ^ 1) for i in range(group_size)]
    buf = jnp.concatenate([buf, lax.ppermute(buf, "wide", perm)], axis=0)
    pattern = pattern + [p ^ 1 for p in pattern]
    source = jnp.asarray(pattern, dtype=jnp.int32) ^ my_index
    return buf, source


def per_device(
    frames, seg_start, seg_dest, rec_id, conv_weight, conv_bias, proj_weight, smooth_kernel
):
    group_size = lax.axis_size("wide")
    total_rows = SEG_DEV * group_size
    pooled = pool_slots(frames, seg_start, conv_weight, conv_bias)
    embedded = jnp.dot(pooled, proj_weight, precision=PRECISE, preferred_element_type=jnp.float32)
    slots = embedded.shape[0]
    meta = jnp.concatenate(
        [seg_dest.astype(jnp.float32), rec_id.astype(jnp.float32)]
    )
    if meta.shape[0] <= EMB:
        meta_rows = jnp.zeros((8, EMB), jnp.float32).at[0, : meta.shape[0]].set(meta)
    else:
        meta_rows = jnp.zeros((-(-meta.shape[0] // EMB) // 8 * 8 + 8, EMB), jnp.float32)
        meta_rows = meta_rows.reshape(-1).at[: meta.shape[0]].set(meta).reshape(-1, EMB)
    packed = jnp.concatenate([embedded, meta_rows], axis=0)
    blocks, source = gather_wide(packed, group_size)
    per_block = slots
    all_emb = blocks[:, :slots, :].reshape(group_size * slots, EMB)
    meta_all = blocks[:, slots:, :].reshape(group_size, -1)[:, : 2 * slots]
    all_dest = meta_all[:, :slots].reshape(-1).astype(jnp.int32)
    all_rec = meta_all[:, slots:].reshape(-1).astype(jnp.int32)
    slot_ids = (
        source[:, None] * per_block + jnp.arange(per_block, dtype=jnp.int32)[None, :]
    ).reshape(-1)
    slot_total = all_dest.shape[0]
    used = all_dest >= 0

    mean_sum = jnp.sum(jnp.where(used[:, None], all_emb, 0.0), axis=0)
    centred = all_emb - mean_sum / total_rows
    unit = (centred / jnp.sqrt(jnp.sum(centred * centred, axis=1, keepdims=True) + 1e-06)).astype(
        jnp.bfloat16
    )

    earlier = (slot_ids[None, :] < slot_ids[:, None]) & (all_dest[None, :] == all_dest[:, None])
    rank = jnp.sum(earlier.astype(jnp.int32), axis=1)
    position = jnp.where(used, all_dest * SEG_DEV + rank, -1)
    picks = position[None, :] == jnp.arange(total_rows, dtype=jnp.int32)[:, None]
    row_ids = jnp.arange(slot_total, dtype=jnp.int32)
    slot_of_pos = jnp.sum(jnp.where(picks, row_ids[None, :], 0), axis=1)

    if total_rows * slot_total <= ONE_HOT_LIMIT:
        rec_hi = (all_rec // 16).astype(jnp.bfloat16)[:, None]
        rec_lo = (all_rec % 16).astype(jnp.bfloat16)[:, None]
        unit_ext = jnp.concatenate([unit, rec_hi, rec_lo], axis=1)
        selector = picks.astype(jnp.bfloat16)
        col_ext = jnp.dot(selector, unit_ext, preferred_element_type=jnp.float32)
        col_unit = col_ext[:, :EMB].astype(jnp.bfloat16)
        col_rec = (col_ext[:, EMB] * 16 + col_ext[:, EMB + 1]).astype(jnp.int32)
    else:
        col_unit = jnp.take(unit, slot_of_pos, axis=0)
        col_rec = jnp.take(all_rec, slot_of_pos, axis=0)
    zero_unit = jnp.zeros((1, EMB), jnp.bfloat16)
    pad_unit = jnp.concatenate([zero_unit, col_unit, zero_unit], axis=0)
    pad_rec = jnp.concatenate([jnp.full((1,), -1, jnp.int32), col_rec, jnp.full((1,), -1, jnp.int32)])
    my_index = lax.axis_index("wide")
    row_unit = lax.dynamic_slice_in_dim(pad_unit, my_index * SEG_DEV, SEG_DEV + 2, 0)
    row_rec = lax.dynamic_slice_in_dim(pad_rec, my_index * SEG_DEV, SEG_DEV + 2, 0)
    return smooth_affinity(row_unit, col_unit, row_rec, col_rec, smooth_kernel)


def solution(mesh):
    in_specs = (
        P(("parts", "wide"), None),
        P(("parts", "wide")),
        P(("parts", "wide")),
        P(("parts", "wide")),
        P(),
        P(),
        P(),
        P(),
    )
    out_specs = P(("parts", "wide"), None)
    return jax.shard_map(
        per_device, mesh=mesh, in_specs=in_specs, out_specs=out_specs, check_vma=False
    )
```

```python
import functools

import jax
import jax.numpy as jnp
from jax import lax
from jax.experimental import pallas as pl
from jax.experimental.pallas import tpu as pltpu
from jax.sharding import PartitionSpec as P

FEAT = 80
CH = 1024
EMB = 192
SEGLEN = 64
SEG_DEV = 32


PRECISE = lax.Precision.HIGHEST
AFF_SCALE = 8.0
SEG_BLOCK = 8
WIN = SEGLEN + 8
CONV_ROWS = 256
ONE_HOT_LIMIT = 1 << 20


def _pool_kernel(
    starts_ref, frames_hbm, w_hbm, b_ref, out_ref, frames_ref, w_ref, x3_ref, act_ref, sem
):
    rows = frames_ref.shape[0]
    slots = out_ref.shape[0]
    frames_copy = pltpu.make_async_copy(frames_hbm, frames_ref, sem.at[0])
    w_copy = pltpu.make_async_copy(w_hbm, w_ref, sem.at[1])
    frames_copy.start()
    w_copy.start()
    frames_copy.wait()
    frames = frames_ref[...]
    x3_ref[...] = jnp.concatenate(
        [pltpu.roll(frames, 1, 0), frames, pltpu.roll(frames, rows - 1, 0)], axis=1
    )
    chunk = CONV_ROWS if rows % CONV_ROWS == 0 else rows
    w_copy.wait()

    def conv_chunk(c, carry):
        base = pl.multiple_of(c * chunk, chunk)
        preact = jnp.dot(
            x3_ref[pl.ds(base, chunk), :],
            w_ref[...],
            precision=PRECISE,
            preferred_element_type=jnp.float32,
        )
        act_ref[pl.ds(base, chunk), :] = jnp.maximum(preact + b_ref[...], 0.0)
        return carry

    lax.fori_loop(0, rows // chunk, conv_chunk, 0)
    frame_idx = lax.broadcasted_iota(jnp.int32, (WIN, CH), 0)

    def stats_block(blk, carry):
        means = []
        stds = []
        for j in range(SEG_BLOCK):
            start = starts_ref[blk * SEG_BLOCK + j]
            base = jnp.minimum((start // 8) * 8, rows - WIN)
            shift = start - base
            inside = (frame_idx >= shift) & (frame_idx < shift + SEGLEN)
            seg_act = act_ref[pl.ds(pl.multiple_of(base, 8), WIN), :]
            frame_mean = jnp.sum(jnp.where(inside, seg_act, 0.0), axis=0, keepdims=True) / SEGLEN
            deviation = jnp.where(inside, seg_act - frame_mean, 0.0)
            frame_var = jnp.sum(deviation * deviation, axis=0, keepdims=True) / SEGLEN
            means.append(frame_mean)
            stds.append(jnp.sqrt(frame_var + 1e-05))
        row0 = pl.multiple_of(blk * SEG_BLOCK, SEG_BLOCK)
        out_ref[pl.ds(row0, SEG_BLOCK), :CH] = jnp.concatenate(means, axis=0)
        out_ref[pl.ds(row0, SEG_BLOCK), CH:] = jnp.concatenate(stds, axis=0)
        return carry

    lax.fori_loop(0, slots // SEG_BLOCK, stats_block, 0)


def pool_slots(frames, seg_start, conv_weight, conv_bias):
    rows = frames.shape[0]
    slots = seg_start.shape[0]
    starts = jnp.clip(seg_start, 0, rows - SEGLEN).astype(jnp.int32)
    vmem = pltpu.MemorySpace.VMEM
    return pl.pallas_call(
        _pool_kernel,
        out_shape=jax.ShapeDtypeStruct((slots, 2 * CH), jnp.float32),
        in_specs=[
            pl.BlockSpec(memory_space=pltpu.MemorySpace.SMEM),
            pl.BlockSpec(memory_space=pl.ANY),
            pl.BlockSpec(memory_space=pl.ANY),
            pl.BlockSpec(memory_space=vmem),
        ],
        out_specs=pl.BlockSpec(memory_space=vmem),
        scratch_shapes=[
            pltpu.VMEM((rows, FEAT), jnp.float32),
            pltpu.VMEM((3 * FEAT, CH), jnp.float32),
            pltpu.VMEM((rows, 3 * FEAT), jnp.float32),
            pltpu.VMEM((rows, CH), jnp.float32),
            pltpu.SemaphoreType.DMA((2,)),
        ],
        compiler_params=pltpu.CompilerParams(vmem_limit_bytes=48 * 1024 * 1024),
        cost_estimate=pl.CostEstimate(
            flops=2 * rows * 3 * FEAT * CH * 6 + 8 * slots * WIN * CH,
            transcendentals=slots * CH,
            bytes_accessed=rows * FEAT * 4 + 3 * FEAT * CH * 4 + slots * 2 * CH * 4,
        ),
    )(starts, frames, conv_weight, conv_bias.reshape(1, CH))


def _affinity_kernel(k_ref, row_unit_ref, col_unit_ref, row_rec_ref, col_rec_ref, out_ref, pad_ref):
    height, width = out_ref.shape
    scores = lax.dot_general(
        row_unit_ref[...],
        col_unit_ref[...],
        (((1,), (1,)), ((), ())),
        preferred_element_type=jnp.float32,
    )
    affinity = jnp.where(row_rec_ref[...] == col_rec_ref[...], 0.0, AFF_SCALE * scores)
    pad_ref[...] = jnp.zeros(pad_ref.shape, jnp.float32)
    pad_ref[0 : height + 2, 1 : width + 1] = affinity
    result = jnp.zeros((height, width), jnp.float32)
    for row_off in range(3):
        for col_off in range(3):
            result = result + k_ref[row_off, col_off] * pad_ref[
                row_off : row_off + height, col_off : col_off + width
            ]
    out_ref[...] = result


def smooth_affinity(row_unit, col_unit, row_rec, col_rec, smooth_kernel):
    height = row_unit.shape[0] - 2
    width = col_unit.shape[0]
    vmem = pltpu.MemorySpace.VMEM
    return pl.pallas_call(
        _affinity_kernel,
        out_shape=jax.ShapeDtypeStruct((height, width), jnp.float32),
        in_specs=[pl.BlockSpec(memory_space=pltpu.MemorySpace.SMEM)]
        + [pl.BlockSpec(memory_space=vmem)] * 4,
        out_specs=pl.BlockSpec(memory_space=vmem),
        scratch_shapes=[
            pltpu.VMEM((-(-(height + 2) // 8) * 8, -(-(width + 2) // 128) * 128), jnp.float32)
        ],
        compiler_params=pltpu.CompilerParams(vmem_limit_bytes=48 * 1024 * 1024),
        cost_estimate=pl.CostEstimate(
            flops=2 * (height + 2) * width * EMB + 20 * height * width,
            transcendentals=0,
            bytes_accessed=(width + height + 2) * EMB * 2 + height * width * 4,
        ),
    )(smooth_kernel, row_unit, col_unit, row_rec.reshape(-1, 1), col_rec.reshape(1, -1))


def gather_wide(x, group_size):
    my_index = lax.axis_index("wide")
    if group_size % 2 or group_size & (group_size - 1):
        every = lax.all_gather(x, "wide", axis=0, tiled=False)
        return every, jnp.arange(group_size, dtype=jnp.int32)
    pair = jnp.stack([x, lax.ppermute(x, "wide", [(i, i ^ 1) for i in range(group_size)])])
    blocks = [pair]
    for flip in range(2, group_size, 2):
        perm = [(i, i ^ flip) for i in range(group_size)]
        blocks.append(lax.ppermute(pair, "wide", perm))
    buf = jnp.concatenate(blocks, axis=0)
    source = jnp.arange(group_size, dtype=jnp.int32) ^ my_index
    return buf, source


def per_device(
    frames, seg_start, seg_dest, rec_id, conv_weight, conv_bias, proj_weight, smooth_kernel
):
    group_size = lax.axis_size("wide")
    total_rows = SEG_DEV * group_size
    pooled = pool_slots(frames, seg_start, conv_weight, conv_bias)
    embedded = jnp.dot(pooled, proj_weight, precision=PRECISE, preferred_element_type=jnp.float32)
    slots = embedded.shape[0]
    meta = jnp.concatenate(
        [seg_dest.astype(jnp.float32), rec_id.astype(jnp.float32)]
    )
    if meta.shape[0] <= EMB:
        meta_rows = jnp.zeros((8, EMB), jnp.float32).at[0, : meta.shape[0]].set(meta)
    else:
        meta_rows = jnp.zeros((-(-meta.shape[0] // EMB) // 8 * 8 + 8, EMB), jnp.float32)
        meta_rows = meta_rows.reshape(-1).at[: meta.shape[0]].set(meta).reshape(-1, EMB)
    packed = jnp.concatenate([embedded, meta_rows], axis=0)
    blocks, source = gather_wide(packed, group_size)
    per_block = slots
    all_emb = blocks[:, :slots, :].reshape(group_size * slots, EMB)
    meta_all = blocks[:, slots:, :].reshape(group_size, -1)[:, : 2 * slots]
    all_dest = meta_all[:, :slots].reshape(-1).astype(jnp.int32)
    all_rec = meta_all[:, slots:].reshape(-1).astype(jnp.int32)
    slot_ids = (
        source[:, None] * per_block + jnp.arange(per_block, dtype=jnp.int32)[None, :]
    ).reshape(-1)
    slot_total = all_dest.shape[0]
    used = all_dest >= 0

    mean_sum = jnp.sum(jnp.where(used[:, None], all_emb, 0.0), axis=0)
    centred = all_emb - mean_sum / total_rows
    unit = (centred / jnp.sqrt(jnp.sum(centred * centred, axis=1, keepdims=True) + 1e-06)).astype(
        jnp.bfloat16
    )

    earlier = (slot_ids[None, :] < slot_ids[:, None]) & (all_dest[None, :] == all_dest[:, None])
    rank = jnp.sum(earlier.astype(jnp.int32), axis=1)
    position = jnp.where(used, all_dest * SEG_DEV + rank, -1)
    picks = position[None, :] == jnp.arange(total_rows, dtype=jnp.int32)[:, None]
    row_ids = jnp.arange(slot_total, dtype=jnp.int32)
    slot_of_pos = jnp.sum(jnp.where(picks, row_ids[None, :], 0), axis=1)

    if total_rows * slot_total <= ONE_HOT_LIMIT:
        rec_hi = (all_rec // 16).astype(jnp.bfloat16)[:, None]
        rec_lo = (all_rec % 16).astype(jnp.bfloat16)[:, None]
        unit_ext = jnp.concatenate([unit, rec_hi, rec_lo], axis=1)
        selector = picks.astype(jnp.bfloat16)
        col_ext = jnp.dot(selector, unit_ext, preferred_element_type=jnp.float32)
        col_unit = col_ext[:, :EMB].astype(jnp.bfloat16)
        col_rec = (col_ext[:, EMB] * 16 + col_ext[:, EMB + 1]).astype(jnp.int32)
    else:
        col_unit = jnp.take(unit, slot_of_pos, axis=0)
        col_rec = jnp.take(all_rec, slot_of_pos, axis=0)
    zero_unit = jnp.zeros((1, EMB), jnp.bfloat16)
    pad_unit = jnp.concatenate([zero_unit, col_unit, zero_unit], axis=0)
    pad_rec = jnp.concatenate([jnp.full((1,), -1, jnp.int32), col_rec, jnp.full((1,), -1, jnp.int32)])
    my_index = lax.axis_index("wide")
    row_unit = lax.dynamic_slice_in_dim(pad_unit, my_index * SEG_DEV, SEG_DEV + 2, 0)
    row_rec = lax.dynamic_slice_in_dim(pad_rec, my_index * SEG_DEV, SEG_DEV + 2, 0)
    return smooth_affinity(row_unit, col_unit, row_rec, col_rec, smooth_kernel)


def solution(mesh):
    in_specs = (
        P(("parts", "wide"), None),
        P(("parts", "wide")),
        P(("parts", "wide")),
        P(("parts", "wide")),
        P(),
        P(),
        P(),
        P(),
    )
    out_specs = P(("parts", "wide"), None)
    return jax.shard_map(
        per_device, mesh=mesh, in_specs=in_specs, out_specs=out_specs, check_vma=False
    )
```

```python
import functools

import jax
import jax.numpy as jnp
from jax import lax
from jax.experimental import pallas as pl
from jax.experimental.pallas import tpu as pltpu
from jax.sharding import PartitionSpec as P

FEAT = 80
CH = 1024
EMB = 192
SEGLEN = 64
SEG_DEV = 32


PRECISE = lax.Precision.HIGHEST
AFF_SCALE = 8.0
SEG_BLOCK = 8
WIN = SEGLEN + 8
CONV_ROWS = 256
ONE_HOT_LIMIT = 1 << 20


def _pool_kernel(
    starts_ref, frames_hbm, w_hbm, b_ref, out_ref, frames_ref, w_ref, x3_ref, act_ref, sem
):
    rows = frames_ref.shape[0]
    slots = out_ref.shape[0]
    frames_copy = pltpu.make_async_copy(frames_hbm, frames_ref, sem.at[0])
    w_copy = pltpu.make_async_copy(w_hbm, w_ref, sem.at[1])
    frames_copy.start()
    w_copy.start()
    frames_copy.wait()
    frames = frames_ref[...]
    x3_ref[...] = jnp.concatenate(
        [pltpu.roll(frames, 1, 0), frames, pltpu.roll(frames, rows - 1, 0)], axis=1
    )
    chunk = CONV_ROWS if rows % CONV_ROWS == 0 else rows
    w_copy.wait()

    def conv_chunk(c, carry):
        base = pl.multiple_of(c * chunk, chunk)
        preact = jnp.dot(
            x3_ref[pl.ds(base, chunk), :],
            w_ref[...],
            precision=PRECISE,
            preferred_element_type=jnp.float32,
        )
        act_ref[pl.ds(base, chunk), :] = jnp.maximum(preact + b_ref[...], 0.0)
        return carry

    lax.fori_loop(0, rows // chunk, conv_chunk, 0)
    frame_idx = lax.broadcasted_iota(jnp.int32, (WIN, CH), 0)

    def stats_block(blk, carry):
        means = []
        stds = []
        for j in range(SEG_BLOCK):
            start = starts_ref[blk * SEG_BLOCK + j]
            base = jnp.minimum((start // 8) * 8, rows - WIN)
            shift = start - base
            inside = (frame_idx >= shift) & (frame_idx < shift + SEGLEN)
            seg_act = act_ref[pl.ds(pl.multiple_of(base, 8), WIN), :]
            frame_mean = jnp.sum(jnp.where(inside, seg_act, 0.0), axis=0, keepdims=True) / SEGLEN
            deviation = jnp.where(inside, seg_act - frame_mean, 0.0)
            frame_var = jnp.sum(deviation * deviation, axis=0, keepdims=True) / SEGLEN
            means.append(frame_mean)
            stds.append(jnp.sqrt(frame_var + 1e-05))
        row0 = pl.multiple_of(blk * SEG_BLOCK, SEG_BLOCK)
        out_ref[pl.ds(row0, SEG_BLOCK), :CH] = jnp.concatenate(means, axis=0)
        out_ref[pl.ds(row0, SEG_BLOCK), CH:] = jnp.concatenate(stds, axis=0)
        return carry

    lax.fori_loop(0, slots // SEG_BLOCK, stats_block, 0)


def pool_slots(frames, seg_start, conv_weight, conv_bias):
    rows = frames.shape[0]
    slots = seg_start.shape[0]
    starts = jnp.clip(seg_start, 0, rows - SEGLEN).astype(jnp.int32)
    vmem = pltpu.MemorySpace.VMEM
    return pl.pallas_call(
        _pool_kernel,
        out_shape=jax.ShapeDtypeStruct((slots, 2 * CH), jnp.float32),
        in_specs=[
            pl.BlockSpec(memory_space=pltpu.MemorySpace.SMEM),
            pl.BlockSpec(memory_space=pl.ANY),
            pl.BlockSpec(memory_space=pl.ANY),
            pl.BlockSpec(memory_space=vmem),
        ],
        out_specs=pl.BlockSpec(memory_space=vmem),
        scratch_shapes=[
            pltpu.VMEM((rows, FEAT), jnp.float32),
            pltpu.VMEM((3 * FEAT, CH), jnp.float32),
            pltpu.VMEM((rows, 3 * FEAT), jnp.float32),
            pltpu.VMEM((rows, CH), jnp.float32),
            pltpu.SemaphoreType.DMA((2,)),
        ],
        compiler_params=pltpu.CompilerParams(vmem_limit_bytes=48 * 1024 * 1024),
        cost_estimate=pl.CostEstimate(
            flops=2 * rows * 3 * FEAT * CH * 6 + 8 * slots * WIN * CH,
            transcendentals=slots * CH,
            bytes_accessed=rows * FEAT * 4 + 3 * FEAT * CH * 4 + slots * 2 * CH * 4,
        ),
    )(starts, frames, conv_weight, conv_bias.reshape(1, CH))


def _affinity_kernel(k_ref, row_unit_ref, col_unit_ref, row_rec_ref, col_rec_ref, out_ref, pad_ref):
    height, width = out_ref.shape
    scores = lax.dot_general(
        row_unit_ref[...],
        col_unit_ref[...],
        (((1,), (1,)), ((), ())),
        preferred_element_type=jnp.float32,
    )
    affinity = jnp.where(row_rec_ref[...] == col_rec_ref[...], 0.0, AFF_SCALE * scores)
    pad_ref[...] = jnp.zeros(pad_ref.shape, jnp.float32)
    pad_ref[0 : height + 2, 1 : width + 1] = affinity
    result = jnp.zeros((height, width), jnp.float32)
    for row_off in range(3):
        for col_off in range(3):
            result = result + k_ref[row_off, col_off] * pad_ref[
                row_off : row_off + height, col_off : col_off + width
            ]
    out_ref[...] = result


def smooth_affinity(row_unit, col_unit, row_rec, col_rec, smooth_kernel):
    height = row_unit.shape[0] - 2
    width = col_unit.shape[0]
    vmem = pltpu.MemorySpace.VMEM
    return pl.pallas_call(
        _affinity_kernel,
        out_shape=jax.ShapeDtypeStruct((height, width), jnp.float32),
        in_specs=[pl.BlockSpec(memory_space=pltpu.MemorySpace.SMEM)]
        + [pl.BlockSpec(memory_space=vmem)] * 4,
        out_specs=pl.BlockSpec(memory_space=vmem),
        scratch_shapes=[
            pltpu.VMEM((-(-(height + 2) // 8) * 8, -(-(width + 2) // 128) * 128), jnp.float32)
        ],
        compiler_params=pltpu.CompilerParams(vmem_limit_bytes=48 * 1024 * 1024),
        cost_estimate=pl.CostEstimate(
            flops=2 * (height + 2) * width * EMB + 20 * height * width,
            transcendentals=0,
            bytes_accessed=(width + height + 2) * EMB * 2 + height * width * 4,
        ),
    )(smooth_kernel, row_unit, col_unit, row_rec.reshape(-1, 1), col_rec.reshape(1, -1))


def gather_wide(x, group_size):
    my_index = lax.axis_index("wide")
    if group_size & (group_size - 1):
        every = lax.all_gather(x, "wide", axis=0, tiled=False)
        return every, jnp.arange(group_size, dtype=jnp.int32)
    pattern = [0]
    buf = x[None]
    bit = group_size.bit_length() - 2
    while bit >= 0:
        if bit >= 2:
            flips = [m << (bit - 1) for m in (1, 2, 3)]
            bit -= 2
        else:
            flips = [1 << bit]
            bit -= 1
        received = [
            lax.ppermute(buf, "wide", [(i, i ^ f) for i in range(group_size)]) for f in flips
        ]
        buf = jnp.concatenate([buf] + received, axis=0)
        pattern = pattern + [p ^ f for f in flips for p in pattern]
    source = jnp.asarray(pattern, dtype=jnp.int32) ^ my_index
    return buf, source


def per_device(
    frames, seg_start, seg_dest, rec_id, conv_weight, conv_bias, proj_weight, smooth_kernel
):
    group_size = lax.axis_size("wide")
    total_rows = SEG_DEV * group_size
    pooled = pool_slots(frames, seg_start, conv_weight, conv_bias)
    embedded = jnp.dot(pooled, proj_weight, precision=PRECISE, preferred_element_type=jnp.float32)
    slots = embedded.shape[0]
    meta = jnp.concatenate(
        [seg_dest.astype(jnp.float32), rec_id.astype(jnp.float32)]
    )
    if meta.shape[0] <= EMB:
        meta_rows = jnp.zeros((8, EMB), jnp.float32).at[0, : meta.shape[0]].set(meta)
    else:
        meta_rows = jnp.zeros((-(-meta.shape[0] // EMB) // 8 * 8 + 8, EMB), jnp.float32)
        meta_rows = meta_rows.reshape(-1).at[: meta.shape[0]].set(meta).reshape(-1, EMB)
    packed = jnp.concatenate([embedded, meta_rows], axis=0)
    blocks, source = gather_wide(packed, group_size)
    per_block = slots
    all_emb = blocks[:, :slots, :].reshape(group_size * slots, EMB)
    meta_all = blocks[:, slots:, :].reshape(group_size, -1)[:, : 2 * slots]
    all_dest = meta_all[:, :slots].reshape(-1).astype(jnp.int32)
    all_rec = meta_all[:, slots:].reshape(-1).astype(jnp.int32)
    slot_ids = (
        source[:, None] * per_block + jnp.arange(per_block, dtype=jnp.int32)[None, :]
    ).reshape(-1)
    slot_total = all_dest.shape[0]
    used = all_dest >= 0

    mean_sum = jnp.sum(jnp.where(used[:, None], all_emb, 0.0), axis=0)
    centred = all_emb - mean_sum / total_rows
    unit = (centred / jnp.sqrt(jnp.sum(centred * centred, axis=1, keepdims=True) + 1e-06)).astype(
        jnp.bfloat16
    )

    earlier = (slot_ids[None, :] < slot_ids[:, None]) & (all_dest[None, :] == all_dest[:, None])
    rank = jnp.sum(earlier.astype(jnp.int32), axis=1)
    position = jnp.where(used, all_dest * SEG_DEV + rank, -1)
    picks = position[None, :] == jnp.arange(total_rows, dtype=jnp.int32)[:, None]
    row_ids = jnp.arange(slot_total, dtype=jnp.int32)
    slot_of_pos = jnp.sum(jnp.where(picks, row_ids[None, :], 0), axis=1)

    if total_rows * slot_total <= ONE_HOT_LIMIT:
        rec_hi = (all_rec // 16).astype(jnp.bfloat16)[:, None]
        rec_lo = (all_rec % 16).astype(jnp.bfloat16)[:, None]
        unit_ext = jnp.concatenate([unit, rec_hi, rec_lo], axis=1)
        selector = picks.astype(jnp.bfloat16)
        col_ext = jnp.dot(selector, unit_ext, preferred_element_type=jnp.float32)
        col_unit = col_ext[:, :EMB].astype(jnp.bfloat16)
        col_rec = (col_ext[:, EMB] * 16 + col_ext[:, EMB + 1]).astype(jnp.int32)
    else:
        col_unit = jnp.take(unit, slot_of_pos, axis=0)
        col_rec = jnp.take(all_rec, slot_of_pos, axis=0)
    zero_unit = jnp.zeros((1, EMB), jnp.bfloat16)
    pad_unit = jnp.concatenate([zero_unit, col_unit, zero_unit], axis=0)
    pad_rec = jnp.concatenate([jnp.full((1,), -1, jnp.int32), col_rec, jnp.full((1,), -1, jnp.int32)])
    my_index = lax.axis_index("wide")
    row_unit = lax.dynamic_slice_in_dim(pad_unit, my_index * SEG_DEV, SEG_DEV + 2, 0)
    row_rec = lax.dynamic_slice_in_dim(pad_rec, my_index * SEG_DEV, SEG_DEV + 2, 0)
    return smooth_affinity(row_unit, col_unit, row_rec, col_rec, smooth_kernel)


def solution(mesh):
    in_specs = (
        P(("parts", "wide"), None),
        P(("parts", "wide")),
        P(("parts", "wide")),
        P(("parts", "wide")),
        P(),
        P(),
        P(),
        P(),
    )
    out_specs = P(("parts", "wide"), None)
    return jax.shard_map(
        per_device, mesh=mesh, in_specs=in_specs, out_specs=out_specs, check_vma=False
    )
```

```python
import functools

import jax
import jax.numpy as jnp
from jax import lax
from jax.experimental import pallas as pl
from jax.experimental.pallas import tpu as pltpu
from jax.sharding import PartitionSpec as P

FEAT = 80
CH = 1024
EMB = 192
SEGLEN = 64
SEG_DEV = 32


PRECISE = lax.Precision.HIGHEST
AFF_SCALE = 8.0
SEG_BLOCK = 8
WIN = SEGLEN + 8
CONV_ROWS = 256
ONE_HOT_LIMIT = 1 << 20


def _pool_kernel(
    starts_ref, frames_hbm, w_hbm, b_ref, out_ref, frames_ref, w_ref, x3_ref, act_ref, sem
):
    rows = frames_ref.shape[0]
    slots = out_ref.shape[0]
    frames_copy = pltpu.make_async_copy(frames_hbm, frames_ref, sem.at[0])
    w_copy = pltpu.make_async_copy(w_hbm, w_ref, sem.at[1])
    frames_copy.start()
    w_copy.start()
    frames_copy.wait()
    frames = frames_ref[...]
    x3_ref[...] = jnp.concatenate(
        [pltpu.roll(frames, 1, 0), frames, pltpu.roll(frames, rows - 1, 0)], axis=1
    )
    chunk = CONV_ROWS if rows % CONV_ROWS == 0 else rows
    w_copy.wait()

    def conv_chunk(c, carry):
        base = pl.multiple_of(c * chunk, chunk)
        preact = jnp.dot(
            x3_ref[pl.ds(base, chunk), :],
            w_ref[...],
            precision=PRECISE,
            preferred_element_type=jnp.float32,
        )
        act_ref[pl.ds(base, chunk), :] = jnp.maximum(preact + b_ref[...], 0.0)
        return carry

    lax.fori_loop(0, rows // chunk, conv_chunk, 0)
    frame_idx = lax.broadcasted_iota(jnp.int32, (WIN, CH), 0)

    def stats_block(blk, carry):
        means = []
        stds = []
        for j in range(SEG_BLOCK):
            start = starts_ref[blk * SEG_BLOCK + j]
            base = jnp.minimum((start // 8) * 8, rows - WIN)
            shift = start - base
            inside = (frame_idx >= shift) & (frame_idx < shift + SEGLEN)
            seg_act = act_ref[pl.ds(pl.multiple_of(base, 8), WIN), :]
            frame_mean = jnp.sum(jnp.where(inside, seg_act, 0.0), axis=0, keepdims=True) / SEGLEN
            deviation = jnp.where(inside, seg_act - frame_mean, 0.0)
            frame_var = jnp.sum(deviation * deviation, axis=0, keepdims=True) / SEGLEN
            means.append(frame_mean)
            stds.append(jnp.sqrt(frame_var + 1e-05))
        row0 = pl.multiple_of(blk * SEG_BLOCK, SEG_BLOCK)
        out_ref[pl.ds(row0, SEG_BLOCK), :CH] = jnp.concatenate(means, axis=0)
        out_ref[pl.ds(row0, SEG_BLOCK), CH:] = jnp.concatenate(stds, axis=0)
        return carry

    lax.fori_loop(0, slots // SEG_BLOCK, stats_block, 0)


def pool_slots(frames, seg_start, conv_weight, conv_bias):
    rows = frames.shape[0]
    slots = seg_start.shape[0]
    starts = jnp.clip(seg_start, 0, rows - SEGLEN).astype(jnp.int32)
    vmem = pltpu.MemorySpace.VMEM
    return pl.pallas_call(
        _pool_kernel,
        out_shape=jax.ShapeDtypeStruct((slots, 2 * CH), jnp.float32),
        in_specs=[
            pl.BlockSpec(memory_space=pltpu.MemorySpace.SMEM),
            pl.BlockSpec(memory_space=pl.ANY),
            pl.BlockSpec(memory_space=pl.ANY),
            pl.BlockSpec(memory_space=vmem),
        ],
        out_specs=pl.BlockSpec(memory_space=vmem),
        scratch_shapes=[
            pltpu.VMEM((rows, FEAT), jnp.float32),
            pltpu.VMEM((3 * FEAT, CH), jnp.float32),
            pltpu.VMEM((rows, 3 * FEAT), jnp.float32),
            pltpu.VMEM((rows, CH), jnp.float32),
            pltpu.SemaphoreType.DMA((2,)),
        ],
        compiler_params=pltpu.CompilerParams(vmem_limit_bytes=48 * 1024 * 1024),
        cost_estimate=pl.CostEstimate(
            flops=2 * rows * 3 * FEAT * CH * 6 + 8 * slots * WIN * CH,
            transcendentals=slots * CH,
            bytes_accessed=rows * FEAT * 4 + 3 * FEAT * CH * 4 + slots * 2 * CH * 4,
        ),
    )(starts, frames, conv_weight, conv_bias.reshape(1, CH))


def _affinity_kernel(k_ref, row_unit_ref, col_unit_ref, row_rec_ref, col_rec_ref, out_ref, pad_ref):
    height, width = out_ref.shape
    scores = lax.dot_general(
        row_unit_ref[...],
        col_unit_ref[...],
        (((1,), (1,)), ((), ())),
        preferred_element_type=jnp.float32,
    )
    affinity = jnp.where(row_rec_ref[...] == col_rec_ref[...], 0.0, AFF_SCALE * scores)
    pad_ref[...] = jnp.zeros(pad_ref.shape, jnp.float32)
    pad_ref[0 : height + 2, 1 : width + 1] = affinity
    result = jnp.zeros((height, width), jnp.float32)
    for row_off in range(3):
        for col_off in range(3):
            result = result + k_ref[row_off, col_off] * pad_ref[
                row_off : row_off + height, col_off : col_off + width
            ]
    out_ref[...] = result


def smooth_affinity(row_unit, col_unit, row_rec, col_rec, smooth_kernel):
    height = row_unit.shape[0] - 2
    width = col_unit.shape[0]
    vmem = pltpu.MemorySpace.VMEM
    return pl.pallas_call(
        _affinity_kernel,
        out_shape=jax.ShapeDtypeStruct((height, width), jnp.float32),
        in_specs=[pl.BlockSpec(memory_space=pltpu.MemorySpace.SMEM)]
        + [pl.BlockSpec(memory_space=vmem)] * 4,
        out_specs=pl.BlockSpec(memory_space=vmem),
        scratch_shapes=[
            pltpu.VMEM((-(-(height + 2) // 8) * 8, -(-(width + 2) // 128) * 128), jnp.float32)
        ],
        compiler_params=pltpu.CompilerParams(vmem_limit_bytes=48 * 1024 * 1024),
        cost_estimate=pl.CostEstimate(
            flops=2 * (height + 2) * width * EMB + 20 * height * width,
            transcendentals=0,
            bytes_accessed=(width + height + 2) * EMB * 2 + height * width * 4,
        ),
    )(smooth_kernel, row_unit, col_unit, row_rec.reshape(-1, 1), col_rec.reshape(1, -1))


def gather_wide(x, group_size):
    my_index = lax.axis_index("wide")
    if group_size & (group_size - 1):
        every = lax.all_gather(x, "wide", axis=0, tiled=False)
        return every, jnp.arange(group_size, dtype=jnp.int32)
    pattern = [0]
    buf = x[None]
    bit = group_size.bit_length() - 2
    while bit >= 0:
        if bit % 2:
            flips = [m << (bit - 1) for m in (1, 2, 3)]
            bit -= 2
        else:
            flips = [1 << bit]
            bit -= 1
        received = [
            lax.ppermute(buf, "wide", [(i, i ^ f) for i in range(group_size)]) for f in flips
        ]
        buf = jnp.concatenate([buf] + received, axis=0)
        pattern = pattern + [p ^ f for f in flips for p in pattern]
    source = jnp.asarray(pattern, dtype=jnp.int32) ^ my_index
    return buf, source


def per_device(
    frames, seg_start, seg_dest, rec_id, conv_weight, conv_bias, proj_weight, smooth_kernel
):
    group_size = lax.axis_size("wide")
    total_rows = SEG_DEV * group_size
    pooled = pool_slots(frames, seg_start, conv_weight, conv_bias)
    embedded = jnp.dot(pooled, proj_weight, precision=PRECISE, preferred_element_type=jnp.float32)
    slots = embedded.shape[0]
    meta = jnp.concatenate(
        [seg_dest.astype(jnp.float32), rec_id.astype(jnp.float32)]
    )
    if meta.shape[0] <= EMB:
        meta_rows = jnp.zeros((8, EMB), jnp.float32).at[0, : meta.shape[0]].set(meta)
    else:
        meta_rows = jnp.zeros((-(-meta.shape[0] // EMB) // 8 * 8 + 8, EMB), jnp.float32)
        meta_rows = meta_rows.reshape(-1).at[: meta.shape[0]].set(meta).reshape(-1, EMB)
    packed = jnp.concatenate([embedded, meta_rows], axis=0)
    blocks, source = gather_wide(packed, group_size)
    per_block = slots
    all_emb = blocks[:, :slots, :].reshape(group_size * slots, EMB)
    meta_all = blocks[:, slots:, :].reshape(group_size, -1)[:, : 2 * slots]
    all_dest = meta_all[:, :slots].reshape(-1).astype(jnp.int32)
    all_rec = meta_all[:, slots:].reshape(-1).astype(jnp.int32)
    slot_ids = (
        source[:, None] * per_block + jnp.arange(per_block, dtype=jnp.int32)[None, :]
    ).reshape(-1)
    slot_total = all_dest.shape[0]
    used = all_dest >= 0

    mean_sum = jnp.sum(jnp.where(used[:, None], all_emb, 0.0), axis=0)
    centred = all_emb - mean_sum / total_rows
    unit = (centred / jnp.sqrt(jnp.sum(centred * centred, axis=1, keepdims=True) + 1e-06)).astype(
        jnp.bfloat16
    )

    earlier = (slot_ids[None, :] < slot_ids[:, None]) & (all_dest[None, :] == all_dest[:, None])
    rank = jnp.sum(earlier.astype(jnp.int32), axis=1)
    position = jnp.where(used, all_dest * SEG_DEV + rank, -1)
    picks = position[None, :] == jnp.arange(total_rows, dtype=jnp.int32)[:, None]
    row_ids = jnp.arange(slot_total, dtype=jnp.int32)
    slot_of_pos = jnp.sum(jnp.where(picks, row_ids[None, :], 0), axis=1)

    if total_rows * slot_total <= ONE_HOT_LIMIT:
        rec_hi = (all_rec // 16).astype(jnp.bfloat16)[:, None]
        rec_lo = (all_rec % 16).astype(jnp.bfloat16)[:, None]
        unit_ext = jnp.concatenate([unit, rec_hi, rec_lo], axis=1)
        selector = picks.astype(jnp.bfloat16)
        col_ext = jnp.dot(selector, unit_ext, preferred_element_type=jnp.float32)
        col_unit = col_ext[:, :EMB].astype(jnp.bfloat16)
        col_rec = (col_ext[:, EMB] * 16 + col_ext[:, EMB + 1]).astype(jnp.int32)
    else:
        col_unit = jnp.take(unit, slot_of_pos, axis=0)
        col_rec = jnp.take(all_rec, slot_of_pos, axis=0)
    zero_unit = jnp.zeros((1, EMB), jnp.bfloat16)
    pad_unit = jnp.concatenate([zero_unit, col_unit, zero_unit], axis=0)
    pad_rec = jnp.concatenate([jnp.full((1,), -1, jnp.int32), col_rec, jnp.full((1,), -1, jnp.int32)])
    my_index = lax.axis_index("wide")
    row_unit = lax.dynamic_slice_in_dim(pad_unit, my_index * SEG_DEV, SEG_DEV + 2, 0)
    row_rec = lax.dynamic_slice_in_dim(pad_rec, my_index * SEG_DEV, SEG_DEV + 2, 0)
    return smooth_affinity(row_unit, col_unit, row_rec, col_rec, smooth_kernel)


def solution(mesh):
    in_specs = (
        P(("parts", "wide"), None),
        P(("parts", "wide")),
        P(("parts", "wide")),
        P(("parts", "wide")),
        P(),
        P(),
        P(),
        P(),
    )
    out_specs = P(("parts", "wide"), None)
    return jax.shard_map(
        per_device, mesh=mesh, in_specs=in_specs, out_specs=out_specs, check_vma=False
    )
```

```python
import functools

import jax
import jax.numpy as jnp
from jax import lax
from jax.experimental import pallas as pl
from jax.experimental.pallas import tpu as pltpu
from jax.sharding import PartitionSpec as P

FEAT = 80
CH = 1024
EMB = 192
SEGLEN = 64
SEG_DEV = 32


PRECISE = lax.Precision.HIGHEST
AFF_SCALE = 8.0
SEG_BLOCK = 8
WIN = SEGLEN + 8
CONV_ROWS = 256
ONE_HOT_LIMIT = 1 << 20


def _pool_kernel(
    starts_ref, frames_hbm, w_hbm, b_ref, out_ref, frames_ref, w_ref, x3_ref, act_ref, sem
):
    rows = frames_ref.shape[0]
    slots = out_ref.shape[0]
    frames_copy = pltpu.make_async_copy(frames_hbm, frames_ref, sem.at[0])
    w_copy = pltpu.make_async_copy(w_hbm, w_ref, sem.at[1])
    frames_copy.start()
    w_copy.start()
    frames_copy.wait()
    frames = frames_ref[...]
    x3_ref[...] = jnp.concatenate(
        [pltpu.roll(frames, 1, 0), frames, pltpu.roll(frames, rows - 1, 0)], axis=1
    )
    chunk = CONV_ROWS if rows % CONV_ROWS == 0 else rows
    w_copy.wait()

    def conv_chunk(c, carry):
        base = pl.multiple_of(c * chunk, chunk)
        preact = jnp.dot(
            x3_ref[pl.ds(base, chunk), :],
            w_ref[...],
            precision=PRECISE,
            preferred_element_type=jnp.float32,
        )
        act_ref[pl.ds(base, chunk), :] = jnp.maximum(preact + b_ref[...], 0.0)
        return carry

    lax.fori_loop(0, rows // chunk, conv_chunk, 0)
    frame_idx = lax.broadcasted_iota(jnp.int32, (WIN, CH), 0)

    def stats_block(blk, carry):
        means = []
        stds = []
        for j in range(SEG_BLOCK):
            start = starts_ref[blk * SEG_BLOCK + j]
            base = jnp.minimum((start // 8) * 8, rows - WIN)
            shift = start - base
            inside = (frame_idx >= shift) & (frame_idx < shift + SEGLEN)
            seg_act = act_ref[pl.ds(pl.multiple_of(base, 8), WIN), :]
            frame_mean = jnp.sum(jnp.where(inside, seg_act, 0.0), axis=0, keepdims=True) / SEGLEN
            deviation = jnp.where(inside, seg_act - frame_mean, 0.0)
            frame_var = jnp.sum(deviation * deviation, axis=0, keepdims=True) / SEGLEN
            means.append(frame_mean)
            stds.append(jnp.sqrt(frame_var + 1e-05))
        row0 = pl.multiple_of(blk * SEG_BLOCK, SEG_BLOCK)
        out_ref[pl.ds(row0, SEG_BLOCK), :CH] = jnp.concatenate(means, axis=0)
        out_ref[pl.ds(row0, SEG_BLOCK), CH:] = jnp.concatenate(stds, axis=0)
        return carry

    lax.fori_loop(0, slots // SEG_BLOCK, stats_block, 0)


def pool_slots(frames, seg_start, conv_weight, conv_bias):
    rows = frames.shape[0]
    slots = seg_start.shape[0]
    starts = jnp.clip(seg_start, 0, rows - SEGLEN).astype(jnp.int32)
    vmem = pltpu.MemorySpace.VMEM
    return pl.pallas_call(
        _pool_kernel,
        out_shape=jax.ShapeDtypeStruct((slots, 2 * CH), jnp.float32),
        in_specs=[
            pl.BlockSpec(memory_space=pltpu.MemorySpace.SMEM),
            pl.BlockSpec(memory_space=pl.ANY),
            pl.BlockSpec(memory_space=pl.ANY),
            pl.BlockSpec(memory_space=vmem),
        ],
        out_specs=pl.BlockSpec(memory_space=vmem),
        scratch_shapes=[
            pltpu.VMEM((rows, FEAT), jnp.float32),
            pltpu.VMEM((3 * FEAT, CH), jnp.float32),
            pltpu.VMEM((rows, 3 * FEAT), jnp.float32),
            pltpu.VMEM((rows, CH), jnp.float32),
            pltpu.SemaphoreType.DMA((2,)),
        ],
        compiler_params=pltpu.CompilerParams(vmem_limit_bytes=48 * 1024 * 1024),
        cost_estimate=pl.CostEstimate(
            flops=2 * rows * 3 * FEAT * CH * 6 + 8 * slots * WIN * CH,
            transcendentals=slots * CH,
            bytes_accessed=rows * FEAT * 4 + 3 * FEAT * CH * 4 + slots * 2 * CH * 4,
        ),
    )(starts, frames, conv_weight, conv_bias.reshape(1, CH))


def _affinity_kernel(k_ref, row_unit_ref, col_unit_ref, row_rec_ref, col_rec_ref, out_ref, pad_ref):
    height, width = out_ref.shape
    scores = lax.dot_general(
        row_unit_ref[...],
        col_unit_ref[...],
        (((1,), (1,)), ((), ())),
        preferred_element_type=jnp.float32,
    )
    affinity = jnp.where(row_rec_ref[...] == col_rec_ref[...], 0.0, AFF_SCALE * scores)
    pad_ref[...] = jnp.zeros(pad_ref.shape, jnp.float32)
    pad_ref[0 : height + 2, 1 : width + 1] = affinity
    result = jnp.zeros((height, width), jnp.float32)
    for row_off in range(3):
        for col_off in range(3):
            result = result + k_ref[row_off, col_off] * pad_ref[
                row_off : row_off + height, col_off : col_off + width
            ]
    out_ref[...] = result


def smooth_affinity(row_unit, col_unit, row_rec, col_rec, smooth_kernel):
    height = row_unit.shape[0] - 2
    width = col_unit.shape[0]
    vmem = pltpu.MemorySpace.VMEM
    return pl.pallas_call(
        _affinity_kernel,
        out_shape=jax.ShapeDtypeStruct((height, width), jnp.float32),
        in_specs=[pl.BlockSpec(memory_space=pltpu.MemorySpace.SMEM)]
        + [pl.BlockSpec(memory_space=vmem)] * 4,
        out_specs=pl.BlockSpec(memory_space=vmem),
        scratch_shapes=[
            pltpu.VMEM((-(-(height + 2) // 8) * 8, -(-(width + 2) // 128) * 128), jnp.float32)
        ],
        compiler_params=pltpu.CompilerParams(vmem_limit_bytes=48 * 1024 * 1024),
        cost_estimate=pl.CostEstimate(
            flops=2 * (height + 2) * width * EMB + 20 * height * width,
            transcendentals=0,
            bytes_accessed=(width + height + 2) * EMB * 2 + height * width * 4,
        ),
    )(smooth_kernel, row_unit, col_unit, row_rec.reshape(-1, 1), col_rec.reshape(1, -1))


def gather_wide(x, group_size):
    my_index = lax.axis_index("wide")
    if group_size & (group_size - 1):
        every = lax.all_gather(x, "wide", axis=0, tiled=False)
        return every, jnp.arange(group_size, dtype=jnp.int32)
    pattern = [0]
    buf = x[None]
    bit = group_size.bit_length() - 2
    while bit >= 0:
        if bit >= 2:
            flips = [m << (bit - 1) for m in (1, 2, 3)]
            bit -= 2
        else:
            flips = [1 << bit]
            bit -= 1
        received = [
            lax.ppermute(buf, "wide", [(i, i ^ f) for i in range(group_size)]) for f in flips
        ]
        buf = jnp.concatenate([buf] + received, axis=0)
        pattern = pattern + [p ^ f for f in flips for p in pattern]
    source = jnp.asarray(pattern, dtype=jnp.int32) ^ my_index
    return buf, source


def per_device(
    frames, seg_start, seg_dest, rec_id, conv_weight, conv_bias, proj_weight, smooth_kernel
):
    group_size = lax.axis_size("wide")
    total_rows = SEG_DEV * group_size
    pooled = pool_slots(frames, seg_start, conv_weight, conv_bias)
    embedded = jnp.dot(pooled, proj_weight, precision=PRECISE, preferred_element_type=jnp.float32)
    slots = embedded.shape[0]
    meta = jnp.concatenate(
        [seg_dest.astype(jnp.float32), rec_id.astype(jnp.float32)]
    )
    if meta.shape[0] <= EMB:
        meta_rows = jnp.zeros((8, EMB), jnp.float32).at[0, : meta.shape[0]].set(meta)
    else:
        meta_rows = jnp.zeros((-(-meta.shape[0] // EMB) // 8 * 8 + 8, EMB), jnp.float32)
        meta_rows = meta_rows.reshape(-1).at[: meta.shape[0]].set(meta).reshape(-1, EMB)
    packed = jnp.concatenate([embedded, meta_rows], axis=0)
    blocks, source = gather_wide(packed, group_size)
    per_block = slots
    all_emb = blocks[:, :slots, :].reshape(group_size * slots, EMB)
    meta_all = blocks[:, slots:, :].reshape(group_size, -1)[:, : 2 * slots]
    all_dest = meta_all[:, :slots].reshape(-1).astype(jnp.int32)
    all_rec = meta_all[:, slots:].reshape(-1).astype(jnp.int32)
    slot_ids = (
        source[:, None] * per_block + jnp.arange(per_block, dtype=jnp.int32)[None, :]
    ).reshape(-1)
    slot_total = all_dest.shape[0]
    used = all_dest >= 0

    mean_sum = jnp.sum(jnp.where(used[:, None], all_emb, 0.0), axis=0)
    centred = all_emb - mean_sum / total_rows
    unit = (centred / jnp.sqrt(jnp.sum(centred * centred, axis=1, keepdims=True) + 1e-06)).astype(
        jnp.bfloat16
    )

    earlier = (slot_ids[None, :] < slot_ids[:, None]) & (all_dest[None, :] == all_dest[:, None])
    rank = jnp.sum(earlier.astype(jnp.int32), axis=1)
    position = jnp.where(used, all_dest * SEG_DEV + rank, -1)
    picks = position[None, :] == jnp.arange(total_rows, dtype=jnp.int32)[:, None]
    row_ids = jnp.arange(slot_total, dtype=jnp.int32)
    slot_of_pos = jnp.sum(jnp.where(picks, row_ids[None, :], 0), axis=1)

    if total_rows * slot_total <= ONE_HOT_LIMIT:
        selector = picks.astype(jnp.bfloat16)
        col_unit = jnp.dot(selector, unit, preferred_element_type=jnp.float32).astype(jnp.bfloat16)
        col_rec = jnp.sum(jnp.where(picks, all_rec[None, :], 0), axis=1)
    else:
        col_unit = jnp.take(unit, slot_of_pos, axis=0)
        col_rec = jnp.take(all_rec, slot_of_pos, axis=0)
    zero_unit = jnp.zeros((1, EMB), jnp.bfloat16)
    pad_unit = jnp.concatenate([zero_unit, col_unit, zero_unit], axis=0)
    pad_rec = jnp.concatenate([jnp.full((1,), -1, jnp.int32), col_rec, jnp.full((1,), -1, jnp.int32)])
    my_index = lax.axis_index("wide")
    row_unit = lax.dynamic_slice_in_dim(pad_unit, my_index * SEG_DEV, SEG_DEV + 2, 0)
    row_rec = lax.dynamic_slice_in_dim(pad_rec, my_index * SEG_DEV, SEG_DEV + 2, 0)
    return smooth_affinity(row_unit, col_unit, row_rec, col_rec, smooth_kernel)


def solution(mesh):
    in_specs = (
        P(("parts", "wide"), None),
        P(("parts", "wide")),
        P(("parts", "wide")),
        P(("parts", "wide")),
        P(),
        P(),
        P(),
        P(),
    )
    out_specs = P(("parts", "wide"), None)
    return jax.shard_map(
        per_device, mesh=mesh, in_specs=in_specs, out_specs=out_specs, check_vma=False
    )
```

```python
import functools

import jax
import jax.numpy as jnp
from jax import lax
from jax.experimental import pallas as pl
from jax.experimental.pallas import tpu as pltpu
from jax.sharding import PartitionSpec as P

FEAT = 80
CH = 1024
EMB = 192
SEGLEN = 64
SEG_DEV = 32


PRECISE = lax.Precision.HIGHEST
AFF_SCALE = 8.0
SEG_BLOCK = 8
WIN = SEGLEN + 8
CONV_ROWS = 256
ONE_HOT_LIMIT = 1 << 20


def _pool_kernel(
    starts_ref, frames_hbm, w_hbm, b_ref, out_ref, frames_ref, w_ref, x3_ref, act_ref, sem
):
    rows = frames_ref.shape[0]
    slots = out_ref.shape[0]
    frames_copy = pltpu.make_async_copy(frames_hbm, frames_ref, sem.at[0])
    w_copy = pltpu.make_async_copy(w_hbm, w_ref, sem.at[1])
    frames_copy.start()
    w_copy.start()
    frames_copy.wait()
    frames = frames_ref[...]
    x3_ref[...] = jnp.concatenate(
        [pltpu.roll(frames, 1, 0), frames, pltpu.roll(frames, rows - 1, 0)], axis=1
    )
    chunk = CONV_ROWS if rows % CONV_ROWS == 0 else rows
    w_copy.wait()

    def conv_chunk(c, carry):
        base = pl.multiple_of(c * chunk, chunk)
        preact = jnp.dot(
            x3_ref[pl.ds(base, chunk), :],
            w_ref[...],
            precision=PRECISE,
            preferred_element_type=jnp.float32,
        )
        act_ref[pl.ds(base, chunk), :] = jnp.maximum(preact + b_ref[...], 0.0)
        return carry

    lax.fori_loop(0, rows // chunk, conv_chunk, 0)
    frame_idx = lax.broadcasted_iota(jnp.int32, (WIN, CH), 0)

    def stats_block(blk, carry):
        means = []
        stds = []
        for j in range(SEG_BLOCK):
            start = starts_ref[blk * SEG_BLOCK + j]
            base = jnp.minimum((start // 8) * 8, rows - WIN)
            shift = start - base
            inside = (frame_idx >= shift) & (frame_idx < shift + SEGLEN)
            seg_act = act_ref[pl.ds(pl.multiple_of(base, 8), WIN), :]
            frame_mean = jnp.sum(jnp.where(inside, seg_act, 0.0), axis=0, keepdims=True) / SEGLEN
            deviation = jnp.where(inside, seg_act - frame_mean, 0.0)
            frame_var = jnp.sum(deviation * deviation, axis=0, keepdims=True) / SEGLEN
            means.append(frame_mean)
            stds.append(jnp.sqrt(frame_var + 1e-05))
        row0 = pl.multiple_of(blk * SEG_BLOCK, SEG_BLOCK)
        out_ref[pl.ds(row0, SEG_BLOCK), :CH] = jnp.concatenate(means, axis=0)
        out_ref[pl.ds(row0, SEG_BLOCK), CH:] = jnp.concatenate(stds, axis=0)
        return carry

    lax.fori_loop(0, slots // SEG_BLOCK, stats_block, 0)


def pool_slots(frames, seg_start, conv_weight, conv_bias):
    rows = frames.shape[0]
    slots = seg_start.shape[0]
    starts = jnp.clip(seg_start, 0, rows - SEGLEN).astype(jnp.int32)
    vmem = pltpu.MemorySpace.VMEM
    return pl.pallas_call(
        _pool_kernel,
        out_shape=jax.ShapeDtypeStruct((slots, 2 * CH), jnp.float32),
        in_specs=[
            pl.BlockSpec(memory_space=pltpu.MemorySpace.SMEM),
            pl.BlockSpec(memory_space=pl.ANY),
            pl.BlockSpec(memory_space=pl.ANY),
            pl.BlockSpec(memory_space=vmem),
        ],
        out_specs=pl.BlockSpec(memory_space=vmem),
        scratch_shapes=[
            pltpu.VMEM((rows, FEAT), jnp.float32),
            pltpu.VMEM((3 * FEAT, CH), jnp.float32),
            pltpu.VMEM((rows, 3 * FEAT), jnp.float32),
            pltpu.VMEM((rows, CH), jnp.float32),
            pltpu.SemaphoreType.DMA((2,)),
        ],
        compiler_params=pltpu.CompilerParams(vmem_limit_bytes=48 * 1024 * 1024),
        cost_estimate=pl.CostEstimate(
            flops=2 * rows * 3 * FEAT * CH * 6 + 8 * slots * WIN * CH,
            transcendentals=slots * CH,
            bytes_accessed=rows * FEAT * 4 + 3 * FEAT * CH * 4 + slots * 2 * CH * 4,
        ),
    )(
        starts,
        frames,
        pltpu.with_memory_space_constraint(conv_weight, pltpu.MemorySpace.HBM),
        conv_bias.reshape(1, CH),
    )


def _affinity_kernel(k_ref, row_unit_ref, col_unit_ref, row_rec_ref, col_rec_ref, out_ref, pad_ref):
    height, width = out_ref.shape
    scores = lax.dot_general(
        row_unit_ref[...],
        col_unit_ref[...],
        (((1,), (1,)), ((), ())),
        preferred_element_type=jnp.float32,
    )
    affinity = jnp.where(row_rec_ref[...] == col_rec_ref[...], 0.0, AFF_SCALE * scores)
    pad_ref[...] = jnp.zeros(pad_ref.shape, jnp.float32)
    pad_ref[0 : height + 2, 1 : width + 1] = affinity
    result = jnp.zeros((height, width), jnp.float32)
    for row_off in range(3):
        for col_off in range(3):
            result = result + k_ref[row_off, col_off] * pad_ref[
                row_off : row_off + height, col_off : col_off + width
            ]
    out_ref[...] = result


def smooth_affinity(row_unit, col_unit, row_rec, col_rec, smooth_kernel):
    height = row_unit.shape[0] - 2
    width = col_unit.shape[0]
    vmem = pltpu.MemorySpace.VMEM
    return pl.pallas_call(
        _affinity_kernel,
        out_shape=jax.ShapeDtypeStruct((height, width), jnp.float32),
        in_specs=[pl.BlockSpec(memory_space=pltpu.MemorySpace.SMEM)]
        + [pl.BlockSpec(memory_space=vmem)] * 4,
        out_specs=pl.BlockSpec(memory_space=vmem),
        scratch_shapes=[
            pltpu.VMEM((-(-(height + 2) // 8) * 8, -(-(width + 2) // 128) * 128), jnp.float32)
        ],
        compiler_params=pltpu.CompilerParams(vmem_limit_bytes=48 * 1024 * 1024),
        cost_estimate=pl.CostEstimate(
            flops=2 * (height + 2) * width * EMB + 20 * height * width,
            transcendentals=0,
            bytes_accessed=(width + height + 2) * EMB * 2 + height * width * 4,
        ),
    )(smooth_kernel, row_unit, col_unit, row_rec.reshape(-1, 1), col_rec.reshape(1, -1))


def gather_wide(x, group_size):
    my_index = lax.axis_index("wide")
    if group_size & (group_size - 1):
        every = lax.all_gather(x, "wide", axis=0, tiled=False)
        return every, jnp.arange(group_size, dtype=jnp.int32)
    pattern = [0]
    buf = x[None]
    bit = group_size.bit_length() - 2
    while bit >= 0:
        if bit >= 2:
            flips = [m << (bit - 1) for m in (1, 2, 3)]
            bit -= 2
        else:
            flips = [1 << bit]
            bit -= 1
        received = [
            lax.ppermute(buf, "wide", [(i, i ^ f) for i in range(group_size)]) for f in flips
        ]
        buf = jnp.concatenate([buf] + received, axis=0)
        pattern = pattern + [p ^ f for f in flips for p in pattern]
    source = jnp.asarray(pattern, dtype=jnp.int32) ^ my_index
    return buf, source


def per_device(
    frames, seg_start, seg_dest, rec_id, conv_weight, conv_bias, proj_weight, smooth_kernel
):
    group_size = lax.axis_size("wide")
    total_rows = SEG_DEV * group_size
    pooled = pool_slots(frames, seg_start, conv_weight, conv_bias)
    embedded = jnp.dot(pooled, proj_weight, precision=PRECISE, preferred_element_type=jnp.float32)
    slots = embedded.shape[0]
    meta = jnp.concatenate(
        [seg_dest.astype(jnp.float32), rec_id.astype(jnp.float32)]
    )
    if meta.shape[0] <= EMB:
        meta_rows = jnp.zeros((8, EMB), jnp.float32).at[0, : meta.shape[0]].set(meta)
    else:
        meta_rows = jnp.zeros((-(-meta.shape[0] // EMB) // 8 * 8 + 8, EMB), jnp.float32)
        meta_rows = meta_rows.reshape(-1).at[: meta.shape[0]].set(meta).reshape(-1, EMB)
    packed = jnp.concatenate([embedded, meta_rows], axis=0)
    blocks, source = gather_wide(packed, group_size)
    per_block = slots
    all_emb = blocks[:, :slots, :].reshape(group_size * slots, EMB)
    meta_all = blocks[:, slots:, :].reshape(group_size, -1)[:, : 2 * slots]
    all_dest = meta_all[:, :slots].reshape(-1).astype(jnp.int32)
    all_rec = meta_all[:, slots:].reshape(-1).astype(jnp.int32)
    slot_ids = (
        source[:, None] * per_block + jnp.arange(per_block, dtype=jnp.int32)[None, :]
    ).reshape(-1)
    slot_total = all_dest.shape[0]
    used = all_dest >= 0

    mean_sum = jnp.sum(jnp.where(used[:, None], all_emb, 0.0), axis=0)
    centred = all_emb - mean_sum / total_rows
    unit = (centred / jnp.sqrt(jnp.sum(centred * centred, axis=1, keepdims=True) + 1e-06)).astype(
        jnp.bfloat16
    )

    earlier = (slot_ids[None, :] < slot_ids[:, None]) & (all_dest[None, :] == all_dest[:, None])
    rank = jnp.sum(earlier.astype(jnp.int32), axis=1)
    position = jnp.where(used, all_dest * SEG_DEV + rank, -1)
    picks = position[None, :] == jnp.arange(total_rows, dtype=jnp.int32)[:, None]
    row_ids = jnp.arange(slot_total, dtype=jnp.int32)
    slot_of_pos = jnp.sum(jnp.where(picks, row_ids[None, :], 0), axis=1)

    if total_rows * slot_total <= ONE_HOT_LIMIT:
        selector = picks.astype(jnp.bfloat16)
        col_unit = jnp.dot(selector, unit, preferred_element_type=jnp.float32).astype(jnp.bfloat16)
        col_rec = jnp.sum(jnp.where(picks, all_rec[None, :], 0), axis=1)
    else:
        col_unit = jnp.take(unit, slot_of_pos, axis=0)
        col_rec = jnp.take(all_rec, slot_of_pos, axis=0)
    zero_unit = jnp.zeros((1, EMB), jnp.bfloat16)
    pad_unit = jnp.concatenate([zero_unit, col_unit, zero_unit], axis=0)
    pad_rec = jnp.concatenate([jnp.full((1,), -1, jnp.int32), col_rec, jnp.full((1,), -1, jnp.int32)])
    my_index = lax.axis_index("wide")
    row_unit = lax.dynamic_slice_in_dim(pad_unit, my_index * SEG_DEV, SEG_DEV + 2, 0)
    row_rec = lax.dynamic_slice_in_dim(pad_rec, my_index * SEG_DEV, SEG_DEV + 2, 0)
    return smooth_affinity(row_unit, col_unit, row_rec, col_rec, smooth_kernel)


def solution(mesh):
    in_specs = (
        P(("parts", "wide"), None),
        P(("parts", "wide")),
        P(("parts", "wide")),
        P(("parts", "wide")),
        P(),
        P(),
        P(),
        P(),
    )
    out_specs = P(("parts", "wide"), None)
    return jax.shard_map(
        per_device, mesh=mesh, in_specs=in_specs, out_specs=out_specs, check_vma=False
    )
```

```python
import functools

import jax
import jax.numpy as jnp
from jax import lax
from jax.experimental import pallas as pl
from jax.experimental.pallas import tpu as pltpu
from jax.sharding import PartitionSpec as P

FEAT = 80
CH = 1024
EMB = 192
SEGLEN = 64
SEG_DEV = 32


PRECISE = lax.Precision.HIGHEST
AFF_SCALE = 8.0
SEG_BLOCK = 8
WIN = SEGLEN + 8
CONV_ROWS = 256
ONE_HOT_LIMIT = 1 << 20


def _pool_kernel(
    starts_ref, frames_hbm, w_hbm, b_ref, out_ref, frames_ref, w_ref, x3_ref, act_ref, sem
):
    rows = frames_ref.shape[1]
    slots = out_ref.shape[0]
    frames_copy = pltpu.make_async_copy(frames_hbm, frames_ref, sem.at[0])
    w_copy = pltpu.make_async_copy(w_hbm, w_ref, sem.at[1])
    frames_copy.start()
    w_copy.start()
    frames_copy.wait()
    frames = jnp.transpose(frames_ref[...])
    x3_ref[...] = jnp.concatenate(
        [pltpu.roll(frames, 1, 0), frames, pltpu.roll(frames, rows - 1, 0)], axis=1
    )
    chunk = CONV_ROWS if rows % CONV_ROWS == 0 else rows
    w_copy.wait()

    def conv_chunk(c, carry):
        base = pl.multiple_of(c * chunk, chunk)
        preact = jnp.dot(
            x3_ref[pl.ds(base, chunk), :],
            w_ref[...],
            precision=PRECISE,
            preferred_element_type=jnp.float32,
        )
        act_ref[pl.ds(base, chunk), :] = jnp.maximum(preact + b_ref[...], 0.0)
        return carry

    lax.fori_loop(0, rows // chunk, conv_chunk, 0)
    frame_idx = lax.broadcasted_iota(jnp.int32, (WIN, CH), 0)

    def stats_block(blk, carry):
        means = []
        stds = []
        for j in range(SEG_BLOCK):
            start = starts_ref[blk * SEG_BLOCK + j]
            base = jnp.minimum((start // 8) * 8, rows - WIN)
            shift = start - base
            inside = (frame_idx >= shift) & (frame_idx < shift + SEGLEN)
            seg_act = act_ref[pl.ds(pl.multiple_of(base, 8), WIN), :]
            frame_mean = jnp.sum(jnp.where(inside, seg_act, 0.0), axis=0, keepdims=True) / SEGLEN
            deviation = jnp.where(inside, seg_act - frame_mean, 0.0)
            frame_var = jnp.sum(deviation * deviation, axis=0, keepdims=True) / SEGLEN
            means.append(frame_mean)
            stds.append(jnp.sqrt(frame_var + 1e-05))
        row0 = pl.multiple_of(blk * SEG_BLOCK, SEG_BLOCK)
        out_ref[pl.ds(row0, SEG_BLOCK), :CH] = jnp.concatenate(means, axis=0)
        out_ref[pl.ds(row0, SEG_BLOCK), CH:] = jnp.concatenate(stds, axis=0)
        return carry

    lax.fori_loop(0, slots // SEG_BLOCK, stats_block, 0)


def pool_slots(frames, seg_start, conv_weight, conv_bias):
    rows = frames.shape[0]
    slots = seg_start.shape[0]
    starts = jnp.clip(seg_start, 0, rows - SEGLEN).astype(jnp.int32)
    vmem = pltpu.MemorySpace.VMEM
    return pl.pallas_call(
        _pool_kernel,
        out_shape=jax.ShapeDtypeStruct((slots, 2 * CH), jnp.float32),
        in_specs=[
            pl.BlockSpec(memory_space=pltpu.MemorySpace.SMEM),
            pl.BlockSpec(memory_space=pl.ANY),
            pl.BlockSpec(memory_space=pl.ANY),
            pl.BlockSpec(memory_space=vmem),
        ],
        out_specs=pl.BlockSpec(memory_space=vmem),
        scratch_shapes=[
            pltpu.VMEM((FEAT, rows), jnp.float32),
            pltpu.VMEM((3 * FEAT, CH), jnp.float32),
            pltpu.VMEM((rows, 3 * FEAT), jnp.float32),
            pltpu.VMEM((rows, CH), jnp.float32),
            pltpu.SemaphoreType.DMA((2,)),
        ],
        compiler_params=pltpu.CompilerParams(vmem_limit_bytes=48 * 1024 * 1024),
        cost_estimate=pl.CostEstimate(
            flops=2 * rows * 3 * FEAT * CH * 6 + 8 * slots * WIN * CH,
            transcendentals=slots * CH,
            bytes_accessed=rows * FEAT * 4 + 3 * FEAT * CH * 4 + slots * 2 * CH * 4,
        ),
    )(
        starts,
        pltpu.with_memory_space_constraint(frames.T, pltpu.MemorySpace.HBM),
        pltpu.with_memory_space_constraint(conv_weight, pltpu.MemorySpace.HBM),
        conv_bias.reshape(1, CH),
    )


def _affinity_kernel(k_ref, row_unit_ref, col_unit_ref, row_rec_ref, col_rec_ref, out_ref, pad_ref):
    height, width = out_ref.shape
    scores = lax.dot_general(
        row_unit_ref[...],
        col_unit_ref[...],
        (((1,), (1,)), ((), ())),
        preferred_element_type=jnp.float32,
    )
    affinity = jnp.where(row_rec_ref[...] == col_rec_ref[...], 0.0, AFF_SCALE * scores)
    pad_ref[...] = jnp.zeros(pad_ref.shape, jnp.float32)
    pad_ref[0 : height + 2, 1 : width + 1] = affinity
    result = jnp.zeros((height, width), jnp.float32)
    for row_off in range(3):
        for col_off in range(3):
            result = result + k_ref[row_off, col_off] * pad_ref[
                row_off : row_off + height, col_off : col_off + width
            ]
    out_ref[...] = result


def smooth_affinity(row_unit, col_unit, row_rec, col_rec, smooth_kernel):
    height = row_unit.shape[0] - 2
    width = col_unit.shape[0]
    vmem = pltpu.MemorySpace.VMEM
    return pl.pallas_call(
        _affinity_kernel,
        out_shape=jax.ShapeDtypeStruct((height, width), jnp.float32),
        in_specs=[pl.BlockSpec(memory_space=pltpu.MemorySpace.SMEM)]
        + [pl.BlockSpec(memory_space=vmem)] * 4,
        out_specs=pl.BlockSpec(memory_space=vmem),
        scratch_shapes=[
            pltpu.VMEM((-(-(height + 2) // 8) * 8, -(-(width + 2) // 128) * 128), jnp.float32)
        ],
        compiler_params=pltpu.CompilerParams(vmem_limit_bytes=48 * 1024 * 1024),
        cost_estimate=pl.CostEstimate(
            flops=2 * (height + 2) * width * EMB + 20 * height * width,
            transcendentals=0,
            bytes_accessed=(width + height + 2) * EMB * 2 + height * width * 4,
        ),
    )(smooth_kernel, row_unit, col_unit, row_rec.reshape(-1, 1), col_rec.reshape(1, -1))


def gather_wide(x, group_size):
    my_index = lax.axis_index("wide")
    if group_size & (group_size - 1):
        every = lax.all_gather(x, "wide", axis=0, tiled=False)
        return every, jnp.arange(group_size, dtype=jnp.int32)
    pattern = [0]
    buf = x[None]
    bit = group_size.bit_length() - 2
    while bit >= 0:
        if bit >= 2:
            flips = [m << (bit - 1) for m in (1, 2, 3)]
            bit -= 2
        else:
            flips = [1 << bit]
            bit -= 1
        received = [
            lax.ppermute(buf, "wide", [(i, i ^ f) for i in range(group_size)]) for f in flips
        ]
        buf = jnp.concatenate([buf] + received, axis=0)
        pattern = pattern + [p ^ f for f in flips for p in pattern]
    source = jnp.asarray(pattern, dtype=jnp.int32) ^ my_index
    return buf, source


def per_device(
    frames, seg_start, seg_dest, rec_id, conv_weight, conv_bias, proj_weight, smooth_kernel
):
    group_size = lax.axis_size("wide")
    total_rows = SEG_DEV * group_size
    pooled = pool_slots(frames, seg_start, conv_weight, conv_bias)
    embedded = jnp.dot(pooled, proj_weight, precision=PRECISE, preferred_element_type=jnp.float32)
    slots = embedded.shape[0]
    meta = jnp.concatenate(
        [seg_dest.astype(jnp.float32), rec_id.astype(jnp.float32)]
    )
    if meta.shape[0] <= EMB:
        meta_rows = jnp.zeros((8, EMB), jnp.float32).at[0, : meta.shape[0]].set(meta)
    else:
        meta_rows = jnp.zeros((-(-meta.shape[0] // EMB) // 8 * 8 + 8, EMB), jnp.float32)
        meta_rows = meta_rows.reshape(-1).at[: meta.shape[0]].set(meta).reshape(-1, EMB)
    packed = jnp.concatenate([embedded, meta_rows], axis=0)
    blocks, source = gather_wide(packed, group_size)
    per_block = slots
    all_emb = blocks[:, :slots, :].reshape(group_size * slots, EMB)
    meta_all = blocks[:, slots:, :].reshape(group_size, -1)[:, : 2 * slots]
    all_dest = meta_all[:, :slots].reshape(-1).astype(jnp.int32)
    all_rec = meta_all[:, slots:].reshape(-1).astype(jnp.int32)
    slot_ids = (
        source[:, None] * per_block + jnp.arange(per_block, dtype=jnp.int32)[None, :]
    ).reshape(-1)
    slot_total = all_dest.shape[0]
    used = all_dest >= 0

    mean_sum = jnp.sum(jnp.where(used[:, None], all_emb, 0.0), axis=0)
    centred = all_emb - mean_sum / total_rows
    unit = (centred / jnp.sqrt(jnp.sum(centred * centred, axis=1, keepdims=True) + 1e-06)).astype(
        jnp.bfloat16
    )

    earlier = (slot_ids[None, :] < slot_ids[:, None]) & (all_dest[None, :] == all_dest[:, None])
    rank = jnp.sum(earlier.astype(jnp.int32), axis=1)
    position = jnp.where(used, all_dest * SEG_DEV + rank, -1)
    picks = position[None, :] == jnp.arange(total_rows, dtype=jnp.int32)[:, None]
    row_ids = jnp.arange(slot_total, dtype=jnp.int32)
    slot_of_pos = jnp.sum(jnp.where(picks, row_ids[None, :], 0), axis=1)

    if total_rows * slot_total <= ONE_HOT_LIMIT:
        selector = picks.astype(jnp.bfloat16)
        col_unit = jnp.dot(selector, unit, preferred_element_type=jnp.float32).astype(jnp.bfloat16)
        col_rec = jnp.sum(jnp.where(picks, all_rec[None, :], 0), axis=1)
    else:
        col_unit = jnp.take(unit, slot_of_pos, axis=0)
        col_rec = jnp.take(all_rec, slot_of_pos, axis=0)
    zero_unit = jnp.zeros((1, EMB), jnp.bfloat16)
    pad_unit = jnp.concatenate([zero_unit, col_unit, zero_unit], axis=0)
    pad_rec = jnp.concatenate([jnp.full((1,), -1, jnp.int32), col_rec, jnp.full((1,), -1, jnp.int32)])
    my_index = lax.axis_index("wide")
    row_unit = lax.dynamic_slice_in_dim(pad_unit, my_index * SEG_DEV, SEG_DEV + 2, 0)
    row_rec = lax.dynamic_slice_in_dim(pad_rec, my_index * SEG_DEV, SEG_DEV + 2, 0)
    return smooth_affinity(row_unit, col_unit, row_rec, col_rec, smooth_kernel)


def solution(mesh):
    in_specs = (
        P(("parts", "wide"), None),
        P(("parts", "wide")),
        P(("parts", "wide")),
        P(("parts", "wide")),
        P(),
        P(),
        P(),
        P(),
    )
    out_specs = P(("parts", "wide"), None)
    return jax.shard_map(
        per_device, mesh=mesh, in_specs=in_specs, out_specs=out_specs, check_vma=False
    )
```

```python
import functools

import jax
import jax.numpy as jnp
from jax import lax
from jax.experimental import pallas as pl
from jax.experimental.pallas import tpu as pltpu
from jax.sharding import PartitionSpec as P

FEAT = 80
CH = 1024
EMB = 192
SEGLEN = 64
SEG_DEV = 32


PRECISE = lax.Precision.HIGHEST
AFF_SCALE = 8.0
SEG_BLOCK = 8
WIN = SEGLEN + 8
CONV_ROWS = 256
ONE_HOT_LIMIT = 1 << 20


def _pool_kernel(
    starts_ref, frames_hbm, w_hbm, b_ref, proj_hbm, meta_ref, out_ref,
    frames_ref, w_ref, proj_ref, pooled_ref, x3_ref, act_ref, sem
):
    rows = frames_ref.shape[0]
    slots = pooled_ref.shape[0]
    frames_copy = pltpu.make_async_copy(frames_hbm, frames_ref, sem.at[0])
    w_copy = pltpu.make_async_copy(w_hbm, w_ref, sem.at[1])
    proj_copy = pltpu.make_async_copy(proj_hbm, proj_ref, sem.at[2])
    frames_copy.start()
    w_copy.start()
    proj_copy.start()
    frames_copy.wait()
    frames = frames_ref[...]
    x3_ref[...] = jnp.concatenate(
        [pltpu.roll(frames, 1, 0), frames, pltpu.roll(frames, rows - 1, 0)], axis=1
    )
    chunk = CONV_ROWS if rows % CONV_ROWS == 0 else rows
    w_copy.wait()

    def conv_chunk(c, carry):
        base = pl.multiple_of(c * chunk, chunk)
        preact = jnp.dot(
            x3_ref[pl.ds(base, chunk), :],
            w_ref[...],
            precision=PRECISE,
            preferred_element_type=jnp.float32,
        )
        act_ref[pl.ds(base, chunk), :] = jnp.maximum(preact + b_ref[...], 0.0)
        return carry

    lax.fori_loop(0, rows // chunk, conv_chunk, 0)
    frame_idx = lax.broadcasted_iota(jnp.int32, (WIN, CH), 0)

    def stats_block(blk, carry):
        means = []
        stds = []
        for j in range(SEG_BLOCK):
            start = starts_ref[blk * SEG_BLOCK + j]
            base = jnp.minimum((start // 8) * 8, rows - WIN)
            shift = start - base
            inside = (frame_idx >= shift) & (frame_idx < shift + SEGLEN)
            seg_act = act_ref[pl.ds(pl.multiple_of(base, 8), WIN), :]
            frame_mean = jnp.sum(jnp.where(inside, seg_act, 0.0), axis=0, keepdims=True) / SEGLEN
            deviation = jnp.where(inside, seg_act - frame_mean, 0.0)
            frame_var = jnp.sum(deviation * deviation, axis=0, keepdims=True) / SEGLEN
            means.append(frame_mean)
            stds.append(jnp.sqrt(frame_var + 1e-05))
        row0 = pl.multiple_of(blk * SEG_BLOCK, SEG_BLOCK)
        pooled_ref[pl.ds(row0, SEG_BLOCK), :CH] = jnp.concatenate(means, axis=0)
        pooled_ref[pl.ds(row0, SEG_BLOCK), CH:] = jnp.concatenate(stds, axis=0)
        return carry

    lax.fori_loop(0, slots // SEG_BLOCK, stats_block, 0)
    proj_copy.wait()
    out_ref[:slots, :] = jnp.dot(
        pooled_ref[...], proj_ref[...], precision=PRECISE, preferred_element_type=jnp.float32
    )
    out_ref[slots:, :] = meta_ref[...]


def embed_slots(frames, seg_start, seg_dest, rec_id, conv_weight, conv_bias, proj_weight):
    rows = frames.shape[0]
    slots = seg_start.shape[0]
    starts = jnp.clip(seg_start, 0, rows - SEGLEN).astype(jnp.int32)
    meta = jnp.concatenate([seg_dest.astype(jnp.float32), rec_id.astype(jnp.float32)])
    meta_len = -(-meta.shape[0] // EMB) * EMB
    meta_rows = jnp.pad(meta, (0, meta_len - meta.shape[0])).reshape(-1, EMB)
    meta_rows = jnp.pad(meta_rows, ((0, -(-meta_rows.shape[0] // 8) * 8 - meta_rows.shape[0]), (0, 0)))
    vmem = pltpu.MemorySpace.VMEM
    hbm = pltpu.MemorySpace.HBM
    return pl.pallas_call(
        _pool_kernel,
        out_shape=jax.ShapeDtypeStruct((slots + meta_rows.shape[0], EMB), jnp.float32),
        in_specs=[
            pl.BlockSpec(memory_space=pltpu.MemorySpace.SMEM),
            pl.BlockSpec(memory_space=pl.ANY),
            pl.BlockSpec(memory_space=pl.ANY),
            pl.BlockSpec(memory_space=vmem),
            pl.BlockSpec(memory_space=pl.ANY),
            pl.BlockSpec(memory_space=vmem),
        ],
        out_specs=pl.BlockSpec(memory_space=vmem),
        scratch_shapes=[
            pltpu.VMEM((rows, FEAT), jnp.float32),
            pltpu.VMEM((3 * FEAT, CH), jnp.float32),
            pltpu.VMEM((2 * CH, EMB), jnp.float32),
            pltpu.VMEM((slots, 2 * CH), jnp.float32),
            pltpu.VMEM((rows, 3 * FEAT), jnp.float32),
            pltpu.VMEM((rows, CH), jnp.float32),
            pltpu.SemaphoreType.DMA((3,)),
        ],
        compiler_params=pltpu.CompilerParams(vmem_limit_bytes=48 * 1024 * 1024),
        cost_estimate=pl.CostEstimate(
            flops=2 * rows * 3 * FEAT * CH * 6 + 8 * slots * WIN * CH + 2 * slots * 2 * CH * EMB * 6,
            transcendentals=slots * CH,
            bytes_accessed=rows * FEAT * 4 + 3 * FEAT * CH * 4 + 2 * CH * EMB * 4 + slots * EMB * 4,
        ),
    )(
        starts,
        frames,
        pltpu.with_memory_space_constraint(conv_weight, hbm),
        conv_bias.reshape(1, CH),
        pltpu.with_memory_space_constraint(proj_weight, hbm),
        meta_rows,
    )


def _affinity_kernel(k_ref, row_unit_ref, col_unit_ref, row_rec_ref, col_rec_ref, out_ref, pad_ref):
    height, width = out_ref.shape
    scores = lax.dot_general(
        row_unit_ref[...],
        col_unit_ref[...],
        (((1,), (1,)), ((), ())),
        preferred_element_type=jnp.float32,
    )
    affinity = jnp.where(row_rec_ref[...] == col_rec_ref[...], 0.0, AFF_SCALE * scores)
    pad_ref[...] = jnp.zeros(pad_ref.shape, jnp.float32)
    pad_ref[0 : height + 2, 1 : width + 1] = affinity
    result = jnp.zeros((height, width), jnp.float32)
    for row_off in range(3):
        for col_off in range(3):
            result = result + k_ref[row_off, col_off] * pad_ref[
                row_off : row_off + height, col_off : col_off + width
            ]
    out_ref[...] = result


def smooth_affinity(row_unit, col_unit, row_rec, col_rec, smooth_kernel):
    height = row_unit.shape[0] - 2
    width = col_unit.shape[0]
    vmem = pltpu.MemorySpace.VMEM
    return pl.pallas_call(
        _affinity_kernel,
        out_shape=jax.ShapeDtypeStruct((height, width), jnp.float32),
        in_specs=[pl.BlockSpec(memory_space=pltpu.MemorySpace.SMEM)]
        + [pl.BlockSpec(memory_space=vmem)] * 4,
        out_specs=pl.BlockSpec(memory_space=vmem),
        scratch_shapes=[
            pltpu.VMEM((-(-(height + 2) // 8) * 8, -(-(width + 2) // 128) * 128), jnp.float32)
        ],
        compiler_params=pltpu.CompilerParams(vmem_limit_bytes=48 * 1024 * 1024),
        cost_estimate=pl.CostEstimate(
            flops=2 * (height + 2) * width * EMB + 20 * height * width,
            transcendentals=0,
            bytes_accessed=(width + height + 2) * EMB * 2 + height * width * 4,
        ),
    )(smooth_kernel, row_unit, col_unit, row_rec.reshape(-1, 1), col_rec.reshape(1, -1))


def gather_wide(x, group_size):
    my_index = lax.axis_index("wide")
    if group_size & (group_size - 1):
        every = lax.all_gather(x, "wide", axis=0, tiled=False)
        return every, jnp.arange(group_size, dtype=jnp.int32)
    pattern = [0]
    buf = x[None]
    bit = group_size.bit_length() - 2
    while bit >= 0:
        if bit >= 2:
            flips = [m << (bit - 1) for m in (1, 2, 3)]
            bit -= 2
        else:
            flips = [1 << bit]
            bit -= 1
        received = [
            lax.ppermute(buf, "wide", [(i, i ^ f) for i in range(group_size)]) for f in flips
        ]
        buf = jnp.concatenate([buf] + received, axis=0)
        pattern = pattern + [p ^ f for f in flips for p in pattern]
    source = jnp.asarray(pattern, dtype=jnp.int32) ^ my_index
    return buf, source


def per_device(
    frames, seg_start, seg_dest, rec_id, conv_weight, conv_bias, proj_weight, smooth_kernel
):
    group_size = lax.axis_size("wide")
    total_rows = SEG_DEV * group_size
    packed = embed_slots(frames, seg_start, seg_dest, rec_id, conv_weight, conv_bias, proj_weight)
    slots = seg_start.shape[0]
    blocks, source = gather_wide(packed, group_size)
    per_block = slots
    all_emb = blocks[:, :slots, :].reshape(group_size * slots, EMB)
    meta_all = blocks[:, slots:, :].reshape(group_size, -1)[:, : 2 * slots]
    all_dest = meta_all[:, :slots].reshape(-1).astype(jnp.int32)
    all_rec = meta_all[:, slots:].reshape(-1).astype(jnp.int32)
    slot_ids = (
        source[:, None] * per_block + jnp.arange(per_block, dtype=jnp.int32)[None, :]
    ).reshape(-1)
    slot_total = all_dest.shape[0]
    used = all_dest >= 0

    mean_sum = jnp.sum(jnp.where(used[:, None], all_emb, 0.0), axis=0)
    centred = all_emb - mean_sum / total_rows
    unit = (centred / jnp.sqrt(jnp.sum(centred * centred, axis=1, keepdims=True) + 1e-06)).astype(
        jnp.bfloat16
    )

    earlier = (slot_ids[None, :] < slot_ids[:, None]) & (all_dest[None, :] == all_dest[:, None])
    rank = jnp.sum(earlier.astype(jnp.int32), axis=1)
    position = jnp.where(used, all_dest * SEG_DEV + rank, -1)
    picks = position[None, :] == jnp.arange(total_rows, dtype=jnp.int32)[:, None]
    row_ids = jnp.arange(slot_total, dtype=jnp.int32)
    slot_of_pos = jnp.sum(jnp.where(picks, row_ids[None, :], 0), axis=1)

    if total_rows * slot_total <= ONE_HOT_LIMIT:
        selector = picks.astype(jnp.bfloat16)
        col_unit = jnp.dot(selector, unit, preferred_element_type=jnp.float32).astype(jnp.bfloat16)
        col_rec = jnp.sum(jnp.where(picks, all_rec[None, :], 0), axis=1)
    else:
        col_unit = jnp.take(unit, slot_of_pos, axis=0)
        col_rec = jnp.take(all_rec, slot_of_pos, axis=0)
    zero_unit = jnp.zeros((1, EMB), jnp.bfloat16)
    pad_unit = jnp.concatenate([zero_unit, col_unit, zero_unit], axis=0)
    pad_rec = jnp.concatenate([jnp.full((1,), -1, jnp.int32), col_rec, jnp.full((1,), -1, jnp.int32)])
    my_index = lax.axis_index("wide")
    row_unit = lax.dynamic_slice_in_dim(pad_unit, my_index * SEG_DEV, SEG_DEV + 2, 0)
    row_rec = lax.dynamic_slice_in_dim(pad_rec, my_index * SEG_DEV, SEG_DEV + 2, 0)
    return smooth_affinity(row_unit, col_unit, row_rec, col_rec, smooth_kernel)


def solution(mesh):
    in_specs = (
        P(("parts", "wide"), None),
        P(("parts", "wide")),
        P(("parts", "wide")),
        P(("parts", "wide")),
        P(),
        P(),
        P(),
        P(),
    )
    out_specs = P(("parts", "wide"), None)
    return jax.shard_map(
        per_device, mesh=mesh, in_specs=in_specs, out_specs=out_specs, check_vma=False
    )
```

```python
import functools

import jax
import jax.numpy as jnp
from jax import lax
from jax.experimental import pallas as pl
from jax.experimental.pallas import tpu as pltpu
from jax.sharding import PartitionSpec as P

FEAT = 80
CH = 1024
EMB = 192
SEGLEN = 64
SEG_DEV = 32


PRECISE = lax.Precision.HIGHEST
AFF_SCALE = 8.0
SEG_BLOCK = 8
WIN = SEGLEN + 8
CONV_ROWS = 256
ONE_HOT_LIMIT = 1 << 20


def _pool_kernel(
    starts_ref, frames_hbm, w_hbm, b_ref, proj_hbm, meta_ref, out_ref,
    frames_ref, w_ref, proj_ref, pooled_ref, x3_ref, act_ref, sem
):
    rows = frames_ref.shape[0]
    slots = pooled_ref.shape[0]
    frames_copy = pltpu.make_async_copy(frames_hbm, frames_ref, sem.at[0])
    w_copy = pltpu.make_async_copy(w_hbm, w_ref, sem.at[1])
    proj_copy = pltpu.make_async_copy(proj_hbm, proj_ref, sem.at[2])
    frames_copy.start()
    w_copy.start()
    proj_copy.start()
    frames_copy.wait()
    frames = frames_ref[...]
    x3_ref[...] = jnp.concatenate(
        [pltpu.roll(frames, 1, 0), frames, pltpu.roll(frames, rows - 1, 0)], axis=1
    )
    chunk = CONV_ROWS if rows % CONV_ROWS == 0 else rows
    w_copy.wait()

    def conv_chunk(c, carry):
        base = pl.multiple_of(c * chunk, chunk)
        preact = jnp.dot(
            x3_ref[pl.ds(base, chunk), :],
            w_ref[...],
            precision=PRECISE,
            preferred_element_type=jnp.float32,
        )
        act_ref[pl.ds(base, chunk), :] = jnp.maximum(preact + b_ref[...], 0.0)
        return carry

    lax.fori_loop(0, rows // chunk, conv_chunk, 0)
    frame_idx = lax.broadcasted_iota(jnp.int32, (WIN, CH), 0)

    def stats_block(blk, carry):
        means = []
        stds = []
        for j in range(SEG_BLOCK):
            start = starts_ref[blk * SEG_BLOCK + j]
            base = jnp.minimum((start // 8) * 8, rows - WIN)
            shift = start - base
            inside = (frame_idx >= shift) & (frame_idx < shift + SEGLEN)
            seg_act = act_ref[pl.ds(pl.multiple_of(base, 8), WIN), :]
            frame_mean = jnp.sum(jnp.where(inside, seg_act, 0.0), axis=0, keepdims=True) / SEGLEN
            deviation = jnp.where(inside, seg_act - frame_mean, 0.0)
            frame_var = jnp.sum(deviation * deviation, axis=0, keepdims=True) / SEGLEN
            means.append(frame_mean)
            stds.append(jnp.sqrt(frame_var + 1e-05))
        row0 = pl.multiple_of(blk * SEG_BLOCK, SEG_BLOCK)
        pooled_ref[pl.ds(row0, SEG_BLOCK), :CH] = jnp.concatenate(means, axis=0)
        pooled_ref[pl.ds(row0, SEG_BLOCK), CH:] = jnp.concatenate(stds, axis=0)
        return carry

    lax.fori_loop(0, slots // SEG_BLOCK, stats_block, 0)
    proj_copy.wait()
    out_ref[:slots, :] = lax.dot_general(
        pooled_ref[...],
        proj_ref[...],
        (((1,), (1,)), ((), ())),
        precision=PRECISE,
        preferred_element_type=jnp.float32,
    )
    out_ref[slots:, :] = meta_ref[...]


def embed_slots(frames, seg_start, seg_dest, rec_id, conv_weight, conv_bias, proj_weight):
    rows = frames.shape[0]
    slots = seg_start.shape[0]
    starts = jnp.clip(seg_start, 0, rows - SEGLEN).astype(jnp.int32)
    meta = jnp.concatenate([seg_dest.astype(jnp.float32), rec_id.astype(jnp.float32)])
    meta_len = -(-meta.shape[0] // EMB) * EMB
    meta_rows = jnp.pad(meta, (0, meta_len - meta.shape[0])).reshape(-1, EMB)
    meta_rows = jnp.pad(meta_rows, ((0, -(-meta_rows.shape[0] // 8) * 8 - meta_rows.shape[0]), (0, 0)))
    vmem = pltpu.MemorySpace.VMEM
    hbm = pltpu.MemorySpace.HBM
    return pl.pallas_call(
        _pool_kernel,
        out_shape=jax.ShapeDtypeStruct((slots + meta_rows.shape[0], EMB), jnp.float32),
        in_specs=[
            pl.BlockSpec(memory_space=pltpu.MemorySpace.SMEM),
            pl.BlockSpec(memory_space=pl.ANY),
            pl.BlockSpec(memory_space=pl.ANY),
            pl.BlockSpec(memory_space=vmem),
            pl.BlockSpec(memory_space=pl.ANY),
            pl.BlockSpec(memory_space=vmem),
        ],
        out_specs=pl.BlockSpec(memory_space=vmem),
        scratch_shapes=[
            pltpu.VMEM((rows, FEAT), jnp.float32),
            pltpu.VMEM((3 * FEAT, CH), jnp.float32),
            pltpu.VMEM((EMB, 2 * CH), jnp.float32),
            pltpu.VMEM((slots, 2 * CH), jnp.float32),
            pltpu.VMEM((rows, 3 * FEAT), jnp.float32),
            pltpu.VMEM((rows, CH), jnp.float32),
            pltpu.SemaphoreType.DMA((3,)),
        ],
        compiler_params=pltpu.CompilerParams(vmem_limit_bytes=48 * 1024 * 1024),
        cost_estimate=pl.CostEstimate(
            flops=2 * rows * 3 * FEAT * CH * 6 + 8 * slots * WIN * CH + 2 * slots * 2 * CH * EMB * 6,
            transcendentals=slots * CH,
            bytes_accessed=rows * FEAT * 4 + 3 * FEAT * CH * 4 + 2 * CH * EMB * 4 + slots * EMB * 4,
        ),
    )(
        starts,
        frames,
        pltpu.with_memory_space_constraint(conv_weight, hbm),
        conv_bias.reshape(1, CH),
        pltpu.with_memory_space_constraint(proj_weight.T, hbm),
        meta_rows,
    )


def _affinity_kernel(k_ref, row_unit_ref, col_unit_ref, row_rec_ref, col_rec_ref, out_ref, pad_ref):
    height, width = out_ref.shape
    scores = lax.dot_general(
        row_unit_ref[...],
        col_unit_ref[...],
        (((1,), (1,)), ((), ())),
        preferred_element_type=jnp.float32,
    )
    affinity = jnp.where(row_rec_ref[...] == col_rec_ref[...], 0.0, AFF_SCALE * scores)
    pad_ref[...] = jnp.zeros(pad_ref.shape, jnp.float32)
    pad_ref[0 : height + 2, 1 : width + 1] = affinity
    result = jnp.zeros((height, width), jnp.float32)
    for row_off in range(3):
        for col_off in range(3):
            result = result + k_ref[row_off, col_off] * pad_ref[
                row_off : row_off + height, col_off : col_off + width
            ]
    out_ref[...] = result


def smooth_affinity(row_unit, col_unit, row_rec, col_rec, smooth_kernel):
    height = row_unit.shape[0] - 2
    width = col_unit.shape[0]
    vmem = pltpu.MemorySpace.VMEM
    return pl.pallas_call(
        _affinity_kernel,
        out_shape=jax.ShapeDtypeStruct((height, width), jnp.float32),
        in_specs=[pl.BlockSpec(memory_space=pltpu.MemorySpace.SMEM)]
        + [pl.BlockSpec(memory_space=vmem)] * 4,
        out_specs=pl.BlockSpec(memory_space=vmem),
        scratch_shapes=[
            pltpu.VMEM((-(-(height + 2) // 8) * 8, -(-(width + 2) // 128) * 128), jnp.float32)
        ],
        compiler_params=pltpu.CompilerParams(vmem_limit_bytes=48 * 1024 * 1024),
        cost_estimate=pl.CostEstimate(
            flops=2 * (height + 2) * width * EMB + 20 * height * width,
            transcendentals=0,
            bytes_accessed=(width + height + 2) * EMB * 2 + height * width * 4,
        ),
    )(smooth_kernel, row_unit, col_unit, row_rec.reshape(-1, 1), col_rec.reshape(1, -1))


def gather_wide(x, group_size):
    my_index = lax.axis_index("wide")
    if group_size & (group_size - 1):
        every = lax.all_gather(x, "wide", axis=0, tiled=False)
        return every, jnp.arange(group_size, dtype=jnp.int32)
    pattern = [0]
    buf = x[None]
    bit = group_size.bit_length() - 2
    while bit >= 0:
        if bit >= 2:
            flips = [m << (bit - 1) for m in (1, 2, 3)]
            bit -= 2
        else:
            flips = [1 << bit]
            bit -= 1
        received = [
            lax.ppermute(buf, "wide", [(i, i ^ f) for i in range(group_size)]) for f in flips
        ]
        buf = jnp.concatenate([buf] + received, axis=0)
        pattern = pattern + [p ^ f for f in flips for p in pattern]
    source = jnp.asarray(pattern, dtype=jnp.int32) ^ my_index
    return buf, source


def per_device(
    frames, seg_start, seg_dest, rec_id, conv_weight, conv_bias, proj_weight, smooth_kernel
):
    group_size = lax.axis_size("wide")
    total_rows = SEG_DEV * group_size
    packed = embed_slots(frames, seg_start, seg_dest, rec_id, conv_weight, conv_bias, proj_weight)
    slots = seg_start.shape[0]
    blocks, source = gather_wide(packed, group_size)
    per_block = slots
    all_emb = blocks[:, :slots, :].reshape(group_size * slots, EMB)
    meta_all = blocks[:, slots:, :].reshape(group_size, -1)[:, : 2 * slots]
    all_dest = meta_all[:, :slots].reshape(-1).astype(jnp.int32)
    all_rec = meta_all[:, slots:].reshape(-1).astype(jnp.int32)
    slot_ids = (
        source[:, None] * per_block + jnp.arange(per_block, dtype=jnp.int32)[None, :]
    ).reshape(-1)
    slot_total = all_dest.shape[0]
    used = all_dest >= 0

    mean_sum = jnp.sum(jnp.where(used[:, None], all_emb, 0.0), axis=0)
    centred = all_emb - mean_sum / total_rows
    unit = (centred / jnp.sqrt(jnp.sum(centred * centred, axis=1, keepdims=True) + 1e-06)).astype(
        jnp.bfloat16
    )

    earlier = (slot_ids[None, :] < slot_ids[:, None]) & (all_dest[None, :] == all_dest[:, None])
    rank = jnp.sum(earlier.astype(jnp.int32), axis=1)
    position = jnp.where(used, all_dest * SEG_DEV + rank, -1)
    picks = position[None, :] == jnp.arange(total_rows, dtype=jnp.int32)[:, None]
    row_ids = jnp.arange(slot_total, dtype=jnp.int32)
    slot_of_pos = jnp.sum(jnp.where(picks, row_ids[None, :], 0), axis=1)

    if total_rows * slot_total <= ONE_HOT_LIMIT:
        selector = picks.astype(jnp.bfloat16)
        col_unit = jnp.dot(selector, unit, preferred_element_type=jnp.float32).astype(jnp.bfloat16)
        col_rec = jnp.sum(jnp.where(picks, all_rec[None, :], 0), axis=1)
    else:
        col_unit = jnp.take(unit, slot_of_pos, axis=0)
        col_rec = jnp.take(all_rec, slot_of_pos, axis=0)
    zero_unit = jnp.zeros((1, EMB), jnp.bfloat16)
    pad_unit = jnp.concatenate([zero_unit, col_unit, zero_unit], axis=0)
    pad_rec = jnp.concatenate([jnp.full((1,), -1, jnp.int32), col_rec, jnp.full((1,), -1, jnp.int32)])
    my_index = lax.axis_index("wide")
    row_unit = lax.dynamic_slice_in_dim(pad_unit, my_index * SEG_DEV, SEG_DEV + 2, 0)
    row_rec = lax.dynamic_slice_in_dim(pad_rec, my_index * SEG_DEV, SEG_DEV + 2, 0)
    return smooth_affinity(row_unit, col_unit, row_rec, col_rec, smooth_kernel)


def solution(mesh):
    in_specs = (
        P(("parts", "wide"), None),
        P(("parts", "wide")),
        P(("parts", "wide")),
        P(("parts", "wide")),
        P(),
        P(),
        P(),
        P(),
    )
    out_specs = P(("parts", "wide"), None)
    return jax.shard_map(
        per_device, mesh=mesh, in_specs=in_specs, out_specs=out_specs, check_vma=False
    )
```

```python
import functools

import jax
import jax.numpy as jnp
from jax import lax
from jax.experimental import pallas as pl
from jax.experimental.pallas import tpu as pltpu
from jax.sharding import PartitionSpec as P

FEAT = 80
CH = 1024
EMB = 192
SEGLEN = 64
SEG_DEV = 32


PRECISE = lax.Precision.HIGHEST
AFF_SCALE = 8.0
SEG_BLOCK = 8
WIN = SEGLEN + 8
CONV_ROWS = 512
ONE_HOT_LIMIT = 1 << 20


def _pool_kernel(
    starts_ref, frames_hbm, w_hbm, b_ref, proj_hbm, meta_ref, out_ref,
    frames_ref, w_ref, proj_ref, pooled_ref, x3_ref, act_ref, sem
):
    rows = frames_ref.shape[0]
    slots = pooled_ref.shape[0]
    frames_copy = pltpu.make_async_copy(frames_hbm, frames_ref, sem.at[0])
    w_copy = pltpu.make_async_copy(w_hbm, w_ref, sem.at[1])
    proj_copy = pltpu.make_async_copy(proj_hbm, proj_ref, sem.at[2])
    frames_copy.start()
    w_copy.start()
    proj_copy.start()
    frames_copy.wait()
    frames = frames_ref[...]
    x3_ref[...] = jnp.concatenate(
        [pltpu.roll(frames, 1, 0), frames, pltpu.roll(frames, rows - 1, 0)], axis=1
    )
    chunk = CONV_ROWS if rows % CONV_ROWS == 0 else rows
    w_copy.wait()

    def conv_chunk(c, carry):
        base = pl.multiple_of(c * chunk, chunk)
        preact = jnp.dot(
            x3_ref[pl.ds(base, chunk), :],
            w_ref[...],
            precision=PRECISE,
            preferred_element_type=jnp.float32,
        )
        act_ref[pl.ds(base, chunk), :] = jnp.maximum(preact + b_ref[...], 0.0)
        return carry

    lax.fori_loop(0, rows // chunk, conv_chunk, 0)
    frame_idx = lax.broadcasted_iota(jnp.int32, (WIN, CH), 0)

    def stats_block(blk, carry):
        means = []
        stds = []
        for j in range(SEG_BLOCK):
            start = starts_ref[blk * SEG_BLOCK + j]
            base = jnp.minimum((start // 8) * 8, rows - WIN)
            shift = start - base
            inside = (frame_idx >= shift) & (frame_idx < shift + SEGLEN)
            seg_act = act_ref[pl.ds(pl.multiple_of(base, 8), WIN), :]
            frame_mean = jnp.sum(jnp.where(inside, seg_act, 0.0), axis=0, keepdims=True) / SEGLEN
            deviation = jnp.where(inside, seg_act - frame_mean, 0.0)
            frame_var = jnp.sum(deviation * deviation, axis=0, keepdims=True) / SEGLEN
            means.append(frame_mean)
            stds.append(jnp.sqrt(frame_var + 1e-05))
        row0 = pl.multiple_of(blk * SEG_BLOCK, SEG_BLOCK)
        pooled_ref[pl.ds(row0, SEG_BLOCK), :CH] = jnp.concatenate(means, axis=0)
        pooled_ref[pl.ds(row0, SEG_BLOCK), CH:] = jnp.concatenate(stds, axis=0)
        return carry

    lax.fori_loop(0, slots // SEG_BLOCK, stats_block, 0)
    proj_copy.wait()
    out_ref[:slots, :] = lax.dot_general(
        pooled_ref[...],
        proj_ref[...],
        (((1,), (1,)), ((), ())),
        precision=PRECISE,
        preferred_element_type=jnp.float32,
    )
    out_ref[slots:, :] = meta_ref[...]


def embed_slots(frames, seg_start, seg_dest, rec_id, conv_weight, conv_bias, proj_weight):
    rows = frames.shape[0]
    slots = seg_start.shape[0]
    starts = jnp.clip(seg_start, 0, rows - SEGLEN).astype(jnp.int32)
    meta = jnp.concatenate([seg_dest.astype(jnp.float32), rec_id.astype(jnp.float32)])
    meta_len = -(-meta.shape[0] // EMB) * EMB
    meta_rows = jnp.pad(meta, (0, meta_len - meta.shape[0])).reshape(-1, EMB)
    meta_rows = jnp.pad(meta_rows, ((0, -(-meta_rows.shape[0] // 8) * 8 - meta_rows.shape[0]), (0, 0)))
    vmem = pltpu.MemorySpace.VMEM
    hbm = pltpu.MemorySpace.HBM
    return pl.pallas_call(
        _pool_kernel,
        out_shape=jax.ShapeDtypeStruct((slots + meta_rows.shape[0], EMB), jnp.float32),
        in_specs=[
            pl.BlockSpec(memory_space=pltpu.MemorySpace.SMEM),
            pl.BlockSpec(memory_space=pl.ANY),
            pl.BlockSpec(memory_space=pl.ANY),
            pl.BlockSpec(memory_space=vmem),
            pl.BlockSpec(memory_space=pl.ANY),
            pl.BlockSpec(memory_space=vmem),
        ],
        out_specs=pl.BlockSpec(memory_space=vmem),
        scratch_shapes=[
            pltpu.VMEM((rows, FEAT), jnp.float32),
            pltpu.VMEM((3 * FEAT, CH), jnp.float32),
            pltpu.VMEM((EMB, 2 * CH), jnp.float32),
            pltpu.VMEM((slots, 2 * CH), jnp.float32),
            pltpu.VMEM((rows, 3 * FEAT), jnp.float32),
            pltpu.VMEM((rows, CH), jnp.float32),
            pltpu.SemaphoreType.DMA((3,)),
        ],
        compiler_params=pltpu.CompilerParams(vmem_limit_bytes=48 * 1024 * 1024),
        cost_estimate=pl.CostEstimate(
            flops=2 * rows * 3 * FEAT * CH * 6 + 8 * slots * WIN * CH + 2 * slots * 2 * CH * EMB * 6,
            transcendentals=slots * CH,
            bytes_accessed=rows * FEAT * 4 + 3 * FEAT * CH * 4 + 2 * CH * EMB * 4 + slots * EMB * 4,
        ),
    )(
        starts,
        frames,
        pltpu.with_memory_space_constraint(conv_weight, hbm),
        conv_bias.reshape(1, CH),
        pltpu.with_memory_space_constraint(proj_weight.T, hbm),
        meta_rows,
    )


def _affinity_kernel(k_ref, row_unit_ref, col_unit_ref, row_rec_ref, col_rec_ref, out_ref, pad_ref):
    height, width = out_ref.shape
    scores = lax.dot_general(
        row_unit_ref[...],
        col_unit_ref[...],
        (((1,), (1,)), ((), ())),
        preferred_element_type=jnp.float32,
    )
    affinity = jnp.where(row_rec_ref[...] == col_rec_ref[...], 0.0, AFF_SCALE * scores)
    pad_ref[...] = jnp.zeros(pad_ref.shape, jnp.float32)
    pad_ref[0 : height + 2, 1 : width + 1] = affinity
    result = jnp.zeros((height, width), jnp.float32)
    for row_off in range(3):
        for col_off in range(3):
            result = result + k_ref[row_off, col_off] * pad_ref[
                row_off : row_off + height, col_off : col_off + width
            ]
    out_ref[...] = result


def smooth_affinity(row_unit, col_unit, row_rec, col_rec, smooth_kernel):
    height = row_unit.shape[0] - 2
    width = col_unit.shape[0]
    vmem = pltpu.MemorySpace.VMEM
    return pl.pallas_call(
        _affinity_kernel,
        out_shape=jax.ShapeDtypeStruct((height, width), jnp.float32),
        in_specs=[pl.BlockSpec(memory_space=pltpu.MemorySpace.SMEM)]
        + [pl.BlockSpec(memory_space=vmem)] * 4,
        out_specs=pl.BlockSpec(memory_space=vmem),
        scratch_shapes=[
            pltpu.VMEM((-(-(height + 2) // 8) * 8, -(-(width + 2) // 128) * 128), jnp.float32)
        ],
        compiler_params=pltpu.CompilerParams(vmem_limit_bytes=48 * 1024 * 1024),
        cost_estimate=pl.CostEstimate(
            flops=2 * (height + 2) * width * EMB + 20 * height * width,
            transcendentals=0,
            bytes_accessed=(width + height + 2) * EMB * 2 + height * width * 4,
        ),
    )(smooth_kernel, row_unit, col_unit, row_rec.reshape(-1, 1), col_rec.reshape(1, -1))


def gather_wide(x, group_size):
    my_index = lax.axis_index("wide")
    if group_size & (group_size - 1):
        every = lax.all_gather(x, "wide", axis=0, tiled=False)
        return every, jnp.arange(group_size, dtype=jnp.int32)
    pattern = [0]
    buf = x[None]
    bit = group_size.bit_length() - 2
    while bit >= 0:
        if bit >= 2:
            flips = [m << (bit - 1) for m in (1, 2, 3)]
            bit -= 2
        else:
            flips = [1 << bit]
            bit -= 1
        received = [
            lax.ppermute(buf, "wide", [(i, i ^ f) for i in range(group_size)]) for f in flips
        ]
        buf = jnp.concatenate([buf] + received, axis=0)
        pattern = pattern + [p ^ f for f in flips for p in pattern]
    source = jnp.asarray(pattern, dtype=jnp.int32) ^ my_index
    return buf, source


def per_device(
    frames, seg_start, seg_dest, rec_id, conv_weight, conv_bias, proj_weight, smooth_kernel
):
    group_size = lax.axis_size("wide")
    total_rows = SEG_DEV * group_size
    packed = embed_slots(frames, seg_start, seg_dest, rec_id, conv_weight, conv_bias, proj_weight)
    slots = seg_start.shape[0]
    blocks, source = gather_wide(packed, group_size)
    per_block = slots
    all_emb = blocks[:, :slots, :].reshape(group_size * slots, EMB)
    meta_all = blocks[:, slots:, :].reshape(group_size, -1)[:, : 2 * slots]
    all_dest = meta_all[:, :slots].reshape(-1).astype(jnp.int32)
    all_rec = meta_all[:, slots:].reshape(-1).astype(jnp.int32)
    slot_ids = (
        source[:, None] * per_block + jnp.arange(per_block, dtype=jnp.int32)[None, :]
    ).reshape(-1)
    slot_total = all_dest.shape[0]
    used = all_dest >= 0

    mean_sum = jnp.sum(jnp.where(used[:, None], all_emb, 0.0), axis=0)
    centred = all_emb - mean_sum / total_rows
    unit = (centred / jnp.sqrt(jnp.sum(centred * centred, axis=1, keepdims=True) + 1e-06)).astype(
        jnp.bfloat16
    )

    earlier = (slot_ids[None, :] < slot_ids[:, None]) & (all_dest[None, :] == all_dest[:, None])
    rank = jnp.sum(earlier.astype(jnp.int32), axis=1)
    position = jnp.where(used, all_dest * SEG_DEV + rank, -1)
    picks = position[None, :] == jnp.arange(total_rows, dtype=jnp.int32)[:, None]
    row_ids = jnp.arange(slot_total, dtype=jnp.int32)
    slot_of_pos = jnp.sum(jnp.where(picks, row_ids[None, :], 0), axis=1)

    if total_rows * slot_total <= ONE_HOT_LIMIT:
        selector = picks.astype(jnp.bfloat16)
        col_unit = jnp.dot(selector, unit, preferred_element_type=jnp.float32).astype(jnp.bfloat16)
        col_rec = jnp.sum(jnp.where(picks, all_rec[None, :], 0), axis=1)
    else:
        col_unit = jnp.take(unit, slot_of_pos, axis=0)
        col_rec = jnp.take(all_rec, slot_of_pos, axis=0)
    zero_unit = jnp.zeros((1, EMB), jnp.bfloat16)
    pad_unit = jnp.concatenate([zero_unit, col_unit, zero_unit], axis=0)
    pad_rec = jnp.concatenate([jnp.full((1,), -1, jnp.int32), col_rec, jnp.full((1,), -1, jnp.int32)])
    my_index = lax.axis_index("wide")
    row_unit = lax.dynamic_slice_in_dim(pad_unit, my_index * SEG_DEV, SEG_DEV + 2, 0)
    row_rec = lax.dynamic_slice_in_dim(pad_rec, my_index * SEG_DEV, SEG_DEV + 2, 0)
    return smooth_affinity(row_unit, col_unit, row_rec, col_rec, smooth_kernel)


def solution(mesh):
    in_specs = (
        P(("parts", "wide"), None),
        P(("parts", "wide")),
        P(("parts", "wide")),
        P(("parts", "wide")),
        P(),
        P(),
        P(),
        P(),
    )
    out_specs = P(("parts", "wide"), None)
    return jax.shard_map(
        per_device, mesh=mesh, in_specs=in_specs, out_specs=out_specs, check_vma=False
    )
```

```python
import functools

import jax
import jax.numpy as jnp
from jax import lax
from jax.experimental import pallas as pl
from jax.experimental.pallas import tpu as pltpu
from jax.sharding import PartitionSpec as P

FEAT = 80
CH = 1024
EMB = 192
SEGLEN = 64
SEG_DEV = 32


PRECISE = lax.Precision.HIGHEST
AFF_SCALE = 8.0
SEG_BLOCK = 8
WIN = SEGLEN + 8
CONV_ROWS = 1024
ONE_HOT_LIMIT = 1 << 20


def _pool_kernel(
    starts_ref, frames_hbm, w_hbm, b_ref, proj_hbm, meta_ref, out_ref,
    frames_ref, w_ref, proj_ref, pooled_ref, x3_ref, act_ref, sem
):
    rows = frames_ref.shape[0]
    slots = pooled_ref.shape[0]
    frames_copy = pltpu.make_async_copy(frames_hbm, frames_ref, sem.at[0])
    w_copy = pltpu.make_async_copy(w_hbm, w_ref, sem.at[1])
    proj_copy = pltpu.make_async_copy(proj_hbm, proj_ref, sem.at[2])
    frames_copy.start()
    w_copy.start()
    proj_copy.start()
    frames_copy.wait()
    frames = frames_ref[...]
    x3_ref[...] = jnp.concatenate(
        [pltpu.roll(frames, 1, 0), frames, pltpu.roll(frames, rows - 1, 0)], axis=1
    )
    chunk = CONV_ROWS if rows % CONV_ROWS == 0 else rows
    w_copy.wait()

    def conv_chunk(c, carry):
        base = pl.multiple_of(c * chunk, chunk)
        preact = jnp.dot(
            x3_ref[pl.ds(base, chunk), :],
            w_ref[...],
            precision=PRECISE,
            preferred_element_type=jnp.float32,
        )
        act_ref[pl.ds(base, chunk), :] = jnp.maximum(preact + b_ref[...], 0.0)
        return carry

    lax.fori_loop(0, rows // chunk, conv_chunk, 0)
    frame_idx = lax.broadcasted_iota(jnp.int32, (WIN, CH), 0)

    def stats_block(blk, carry):
        means = []
        stds = []
        for j in range(SEG_BLOCK):
            start = starts_ref[blk * SEG_BLOCK + j]
            base = jnp.minimum((start // 8) * 8, rows - WIN)
            shift = start - base
            inside = (frame_idx >= shift) & (frame_idx < shift + SEGLEN)
            seg_act = act_ref[pl.ds(pl.multiple_of(base, 8), WIN), :]
            frame_mean = jnp.sum(jnp.where(inside, seg_act, 0.0), axis=0, keepdims=True) / SEGLEN
            deviation = jnp.where(inside, seg_act - frame_mean, 0.0)
            frame_var = jnp.sum(deviation * deviation, axis=0, keepdims=True) / SEGLEN
            means.append(frame_mean)
            stds.append(jnp.sqrt(frame_var + 1e-05))
        row0 = pl.multiple_of(blk * SEG_BLOCK, SEG_BLOCK)
        pooled_ref[pl.ds(row0, SEG_BLOCK), :CH] = jnp.concatenate(means, axis=0)
        pooled_ref[pl.ds(row0, SEG_BLOCK), CH:] = jnp.concatenate(stds, axis=0)
        return carry

    lax.fori_loop(0, slots // SEG_BLOCK, stats_block, 0)
    proj_copy.wait()
    out_ref[:slots, :] = lax.dot_general(
        pooled_ref[...],
        proj_ref[...],
        (((1,), (1,)), ((), ())),
        precision=PRECISE,
        preferred_element_type=jnp.float32,
    )
    out_ref[slots:, :] = meta_ref[...]


def embed_slots(frames, seg_start, seg_dest, rec_id, conv_weight, conv_bias, proj_weight):
    rows = frames.shape[0]
    slots = seg_start.shape[0]
    starts = jnp.clip(seg_start, 0, rows - SEGLEN).astype(jnp.int32)
    meta = jnp.concatenate([seg_dest.astype(jnp.float32), rec_id.astype(jnp.float32)])
    meta_len = -(-meta.shape[0] // EMB) * EMB
    meta_rows = jnp.pad(meta, (0, meta_len - meta.shape[0])).reshape(-1, EMB)
    meta_rows = jnp.pad(meta_rows, ((0, -(-meta_rows.shape[0] // 8) * 8 - meta_rows.shape[0]), (0, 0)))
    vmem = pltpu.MemorySpace.VMEM
    hbm = pltpu.MemorySpace.HBM
    return pl.pallas_call(
        _pool_kernel,
        out_shape=jax.ShapeDtypeStruct((slots + meta_rows.shape[0], EMB), jnp.float32),
        in_specs=[
            pl.BlockSpec(memory_space=pltpu.MemorySpace.SMEM),
            pl.BlockSpec(memory_space=pl.ANY),
            pl.BlockSpec(memory_space=pl.ANY),
            pl.BlockSpec(memory_space=vmem),
            pl.BlockSpec(memory_space=pl.ANY),
            pl.BlockSpec(memory_space=vmem),
        ],
        out_specs=pl.BlockSpec(memory_space=vmem),
        scratch_shapes=[
            pltpu.VMEM((rows, FEAT), jnp.float32),
            pltpu.VMEM((3 * FEAT, CH), jnp.float32),
            pltpu.VMEM((EMB, 2 * CH), jnp.float32),
            pltpu.VMEM((slots, 2 * CH), jnp.float32),
            pltpu.VMEM((rows, 3 * FEAT), jnp.float32),
            pltpu.VMEM((rows, CH), jnp.float32),
            pltpu.SemaphoreType.DMA((3,)),
        ],
        compiler_params=pltpu.CompilerParams(vmem_limit_bytes=48 * 1024 * 1024),
        cost_estimate=pl.CostEstimate(
            flops=2 * rows * 3 * FEAT * CH * 6 + 8 * slots * WIN * CH + 2 * slots * 2 * CH * EMB * 6,
            transcendentals=slots * CH,
            bytes_accessed=rows * FEAT * 4 + 3 * FEAT * CH * 4 + 2 * CH * EMB * 4 + slots * EMB * 4,
        ),
    )(
        starts,
        frames,
        pltpu.with_memory_space_constraint(conv_weight, hbm),
        conv_bias.reshape(1, CH),
        pltpu.with_memory_space_constraint(proj_weight.T, hbm),
        meta_rows,
    )


def _affinity_kernel(k_ref, row_unit_ref, col_unit_ref, row_rec_ref, col_rec_ref, out_ref, pad_ref):
    height, width = out_ref.shape
    scores = lax.dot_general(
        row_unit_ref[...],
        col_unit_ref[...],
        (((1,), (1,)), ((), ())),
        preferred_element_type=jnp.float32,
    )
    affinity = jnp.where(row_rec_ref[...] == col_rec_ref[...], 0.0, AFF_SCALE * scores)
    pad_ref[...] = jnp.zeros(pad_ref.shape, jnp.float32)
    pad_ref[0 : height + 2, 1 : width + 1] = affinity
    result = jnp.zeros((height, width), jnp.float32)
    for row_off in range(3):
        for col_off in range(3):
            result = result + k_ref[row_off, col_off] * pad_ref[
                row_off : row_off + height, col_off : col_off + width
            ]
    out_ref[...] = result


def smooth_affinity(row_unit, col_unit, row_rec, col_rec, smooth_kernel):
    height = row_unit.shape[0] - 2
    width = col_unit.shape[0]
    vmem = pltpu.MemorySpace.VMEM
    return pl.pallas_call(
        _affinity_kernel,
        out_shape=jax.ShapeDtypeStruct((height, width), jnp.float32),
        in_specs=[pl.BlockSpec(memory_space=pltpu.MemorySpace.SMEM)]
        + [pl.BlockSpec(memory_space=vmem)] * 4,
        out_specs=pl.BlockSpec(memory_space=vmem),
        scratch_shapes=[
            pltpu.VMEM((-(-(height + 2) // 8) * 8, -(-(width + 2) // 128) * 128), jnp.float32)
        ],
        compiler_params=pltpu.CompilerParams(vmem_limit_bytes=48 * 1024 * 1024),
        cost_estimate=pl.CostEstimate(
            flops=2 * (height + 2) * width * EMB + 20 * height * width,
            transcendentals=0,
            bytes_accessed=(width + height + 2) * EMB * 2 + height * width * 4,
        ),
    )(smooth_kernel, row_unit, col_unit, row_rec.reshape(-1, 1), col_rec.reshape(1, -1))


def gather_wide(x, group_size):
    my_index = lax.axis_index("wide")
    if group_size & (group_size - 1):
        every = lax.all_gather(x, "wide", axis=0, tiled=False)
        return every, jnp.arange(group_size, dtype=jnp.int32)
    pattern = [0]
    buf = x[None]
    bit = group_size.bit_length() - 2
    while bit >= 0:
        if bit >= 2:
            flips = [m << (bit - 1) for m in (1, 2, 3)]
            bit -= 2
        else:
            flips = [1 << bit]
            bit -= 1
        received = [
            lax.ppermute(buf, "wide", [(i, i ^ f) for i in range(group_size)]) for f in flips
        ]
        buf = jnp.concatenate([buf] + received, axis=0)
        pattern = pattern + [p ^ f for f in flips for p in pattern]
    source = jnp.asarray(pattern, dtype=jnp.int32) ^ my_index
    return buf, source


def per_device(
    frames, seg_start, seg_dest, rec_id, conv_weight, conv_bias, proj_weight, smooth_kernel
):
    group_size = lax.axis_size("wide")
    total_rows = SEG_DEV * group_size
    packed = embed_slots(frames, seg_start, seg_dest, rec_id, conv_weight, conv_bias, proj_weight)
    slots = seg_start.shape[0]
    blocks, source = gather_wide(packed, group_size)
    per_block = slots
    all_emb = blocks[:, :slots, :].reshape(group_size * slots, EMB)
    meta_all = blocks[:, slots:, :].reshape(group_size, -1)[:, : 2 * slots]
    all_dest = meta_all[:, :slots].reshape(-1).astype(jnp.int32)
    all_rec = meta_all[:, slots:].reshape(-1).astype(jnp.int32)
    slot_ids = (
        source[:, None] * per_block + jnp.arange(per_block, dtype=jnp.int32)[None, :]
    ).reshape(-1)
    slot_total = all_dest.shape[0]
    used = all_dest >= 0

    mean_sum = jnp.sum(jnp.where(used[:, None], all_emb, 0.0), axis=0)
    centred = all_emb - mean_sum / total_rows
    unit = (centred / jnp.sqrt(jnp.sum(centred * centred, axis=1, keepdims=True) + 1e-06)).astype(
        jnp.bfloat16
    )

    earlier = (slot_ids[None, :] < slot_ids[:, None]) & (all_dest[None, :] == all_dest[:, None])
    rank = jnp.sum(earlier.astype(jnp.int32), axis=1)
    position = jnp.where(used, all_dest * SEG_DEV + rank, -1)
    picks = position[None, :] == jnp.arange(total_rows, dtype=jnp.int32)[:, None]
    row_ids = jnp.arange(slot_total, dtype=jnp.int32)
    slot_of_pos = jnp.sum(jnp.where(picks, row_ids[None, :], 0), axis=1)

    if total_rows * slot_total <= ONE_HOT_LIMIT:
        selector = picks.astype(jnp.bfloat16)
        col_unit = jnp.dot(selector, unit, preferred_element_type=jnp.float32).astype(jnp.bfloat16)
        col_rec = jnp.sum(jnp.where(picks, all_rec[None, :], 0), axis=1)
    else:
        col_unit = jnp.take(unit, slot_of_pos, axis=0)
        col_rec = jnp.take(all_rec, slot_of_pos, axis=0)
    zero_unit = jnp.zeros((1, EMB), jnp.bfloat16)
    pad_unit = jnp.concatenate([zero_unit, col_unit, zero_unit], axis=0)
    pad_rec = jnp.concatenate([jnp.full((1,), -1, jnp.int32), col_rec, jnp.full((1,), -1, jnp.int32)])
    my_index = lax.axis_index("wide")
    row_unit = lax.dynamic_slice_in_dim(pad_unit, my_index * SEG_DEV, SEG_DEV + 2, 0)
    row_rec = lax.dynamic_slice_in_dim(pad_rec, my_index * SEG_DEV, SEG_DEV + 2, 0)
    return smooth_affinity(row_unit, col_unit, row_rec, col_rec, smooth_kernel)


def solution(mesh):
    in_specs = (
        P(("parts", "wide"), None),
        P(("parts", "wide")),
        P(("parts", "wide")),
        P(("parts", "wide")),
        P(),
        P(),
        P(),
        P(),
    )
    out_specs = P(("parts", "wide"), None)
    return jax.shard_map(
        per_device, mesh=mesh, in_specs=in_specs, out_specs=out_specs, check_vma=False
    )
```

```python
import functools

import jax
import jax.numpy as jnp
from jax import lax
from jax.experimental import pallas as pl
from jax.experimental.pallas import tpu as pltpu
from jax.sharding import PartitionSpec as P

FEAT = 80
CH = 1024
EMB = 192
SEGLEN = 64
SEG_DEV = 32


PRECISE = lax.Precision.HIGHEST
AFF_SCALE = 8.0
SEG_BLOCK = 8
WIN = SEGLEN + 8
CONV_ROWS = 2048
ONE_HOT_LIMIT = 1 << 20


def _pool_kernel(
    starts_ref, frames_hbm, w_hbm, b_ref, proj_hbm, meta_ref, out_ref,
    frames_ref, w_ref, proj_ref, pooled_ref, x3_ref, act_ref, sem
):
    rows = frames_ref.shape[0]
    slots = pooled_ref.shape[0]
    frames_copy = pltpu.make_async_copy(frames_hbm, frames_ref, sem.at[0])
    w_copy = pltpu.make_async_copy(w_hbm, w_ref, sem.at[1])
    proj_copy = pltpu.make_async_copy(proj_hbm, proj_ref, sem.at[2])
    frames_copy.start()
    w_copy.start()
    proj_copy.start()
    frames_copy.wait()
    frames = frames_ref[...]
    x3_ref[...] = jnp.concatenate(
        [pltpu.roll(frames, 1, 0), frames, pltpu.roll(frames, rows - 1, 0)], axis=1
    )
    chunk = CONV_ROWS if rows % CONV_ROWS == 0 else rows
    w_copy.wait()

    def conv_chunk(c, carry):
        base = pl.multiple_of(c * chunk, chunk)
        preact = jnp.dot(
            x3_ref[pl.ds(base, chunk), :],
            w_ref[...],
            precision=PRECISE,
            preferred_element_type=jnp.float32,
        )
        act_ref[pl.ds(base, chunk), :] = jnp.maximum(preact + b_ref[...], 0.0)
        return carry

    lax.fori_loop(0, rows // chunk, conv_chunk, 0)
    frame_idx = lax.broadcasted_iota(jnp.int32, (WIN, CH), 0)

    def stats_block(blk, carry):
        means = []
        stds = []
        for j in range(SEG_BLOCK):
            start = starts_ref[blk * SEG_BLOCK + j]
            base = jnp.minimum((start // 8) * 8, rows - WIN)
            shift = start - base
            inside = (frame_idx >= shift) & (frame_idx < shift + SEGLEN)
            seg_act = act_ref[pl.ds(pl.multiple_of(base, 8), WIN), :]
            frame_mean = jnp.sum(jnp.where(inside, seg_act, 0.0), axis=0, keepdims=True) / SEGLEN
            deviation = jnp.where(inside, seg_act - frame_mean, 0.0)
            frame_var = jnp.sum(deviation * deviation, axis=0, keepdims=True) / SEGLEN
            means.append(frame_mean)
            stds.append(jnp.sqrt(frame_var + 1e-05))
        row0 = pl.multiple_of(blk * SEG_BLOCK, SEG_BLOCK)
        pooled_ref[pl.ds(row0, SEG_BLOCK), :CH] = jnp.concatenate(means, axis=0)
        pooled_ref[pl.ds(row0, SEG_BLOCK), CH:] = jnp.concatenate(stds, axis=0)
        return carry

    lax.fori_loop(0, slots // SEG_BLOCK, stats_block, 0)
    proj_copy.wait()
    out_ref[:slots, :] = lax.dot_general(
        pooled_ref[...],
        proj_ref[...],
        (((1,), (1,)), ((), ())),
        precision=PRECISE,
        preferred_element_type=jnp.float32,
    )
    out_ref[slots:, :] = meta_ref[...]


def embed_slots(frames, seg_start, seg_dest, rec_id, conv_weight, conv_bias, proj_weight):
    rows = frames.shape[0]
    slots = seg_start.shape[0]
    starts = jnp.clip(seg_start, 0, rows - SEGLEN).astype(jnp.int32)
    meta = jnp.concatenate([seg_dest.astype(jnp.float32), rec_id.astype(jnp.float32)])
    meta_len = -(-meta.shape[0] // EMB) * EMB
    meta_rows = jnp.pad(meta, (0, meta_len - meta.shape[0])).reshape(-1, EMB)
    meta_rows = jnp.pad(meta_rows, ((0, -(-meta_rows.shape[0] // 8) * 8 - meta_rows.shape[0]), (0, 0)))
    vmem = pltpu.MemorySpace.VMEM
    hbm = pltpu.MemorySpace.HBM
    return pl.pallas_call(
        _pool_kernel,
        out_shape=jax.ShapeDtypeStruct((slots + meta_rows.shape[0], EMB), jnp.float32),
        in_specs=[
            pl.BlockSpec(memory_space=pltpu.MemorySpace.SMEM),
            pl.BlockSpec(memory_space=pl.ANY),
            pl.BlockSpec(memory_space=pl.ANY),
            pl.BlockSpec(memory_space=vmem),
            pl.BlockSpec(memory_space=pl.ANY),
            pl.BlockSpec(memory_space=vmem),
        ],
        out_specs=pl.BlockSpec(memory_space=vmem),
        scratch_shapes=[
            pltpu.VMEM((rows, FEAT), jnp.float32),
            pltpu.VMEM((3 * FEAT, CH), jnp.float32),
            pltpu.VMEM((EMB, 2 * CH), jnp.float32),
            pltpu.VMEM((slots, 2 * CH), jnp.float32),
            pltpu.VMEM((rows, 3 * FEAT), jnp.float32),
            pltpu.VMEM((rows, CH), jnp.float32),
            pltpu.SemaphoreType.DMA((3,)),
        ],
        compiler_params=pltpu.CompilerParams(vmem_limit_bytes=48 * 1024 * 1024),
        cost_estimate=pl.CostEstimate(
            flops=2 * rows * 3 * FEAT * CH * 6 + 8 * slots * WIN * CH + 2 * slots * 2 * CH * EMB * 6,
            transcendentals=slots * CH,
            bytes_accessed=rows * FEAT * 4 + 3 * FEAT * CH * 4 + 2 * CH * EMB * 4 + slots * EMB * 4,
        ),
    )(
        starts,
        frames,
        pltpu.with_memory_space_constraint(conv_weight, hbm),
        conv_bias.reshape(1, CH),
        pltpu.with_memory_space_constraint(proj_weight.T, hbm),
        meta_rows,
    )


def _affinity_kernel(k_ref, row_unit_ref, col_unit_ref, row_rec_ref, col_rec_ref, out_ref, pad_ref):
    height, width = out_ref.shape
    scores = lax.dot_general(
        row_unit_ref[...],
        col_unit_ref[...],
        (((1,), (1,)), ((), ())),
        preferred_element_type=jnp.float32,
    )
    affinity = jnp.where(row_rec_ref[...] == col_rec_ref[...], 0.0, AFF_SCALE * scores)
    pad_ref[...] = jnp.zeros(pad_ref.shape, jnp.float32)
    pad_ref[0 : height + 2, 1 : width + 1] = affinity
    result = jnp.zeros((height, width), jnp.float32)
    for row_off in range(3):
        for col_off in range(3):
            result = result + k_ref[row_off, col_off] * pad_ref[
                row_off : row_off + height, col_off : col_off + width
            ]
    out_ref[...] = result


def smooth_affinity(row_unit, col_unit, row_rec, col_rec, smooth_kernel):
    height = row_unit.shape[0] - 2
    width = col_unit.shape[0]
    vmem = pltpu.MemorySpace.VMEM
    return pl.pallas_call(
        _affinity_kernel,
        out_shape=jax.ShapeDtypeStruct((height, width), jnp.float32),
        in_specs=[pl.BlockSpec(memory_space=pltpu.MemorySpace.SMEM)]
        + [pl.BlockSpec(memory_space=vmem)] * 4,
        out_specs=pl.BlockSpec(memory_space=vmem),
        scratch_shapes=[
            pltpu.VMEM((-(-(height + 2) // 8) * 8, -(-(width + 2) // 128) * 128), jnp.float32)
        ],
        compiler_params=pltpu.CompilerParams(vmem_limit_bytes=48 * 1024 * 1024),
        cost_estimate=pl.CostEstimate(
            flops=2 * (height + 2) * width * EMB + 20 * height * width,
            transcendentals=0,
            bytes_accessed=(width + height + 2) * EMB * 2 + height * width * 4,
        ),
    )(smooth_kernel, row_unit, col_unit, row_rec.reshape(-1, 1), col_rec.reshape(1, -1))


def gather_wide(x, group_size):
    my_index = lax.axis_index("wide")
    if group_size & (group_size - 1):
        every = lax.all_gather(x, "wide", axis=0, tiled=False)
        return every, jnp.arange(group_size, dtype=jnp.int32)
    pattern = [0]
    buf = x[None]
    bit = group_size.bit_length() - 2
    while bit >= 0:
        if bit >= 2:
            flips = [m << (bit - 1) for m in (1, 2, 3)]
            bit -= 2
        else:
            flips = [1 << bit]
            bit -= 1
        received = [
            lax.ppermute(buf, "wide", [(i, i ^ f) for i in range(group_size)]) for f in flips
        ]
        buf = jnp.concatenate([buf] + received, axis=0)
        pattern = pattern + [p ^ f for f in flips for p in pattern]
    source = jnp.asarray(pattern, dtype=jnp.int32) ^ my_index
    return buf, source


def per_device(
    frames, seg_start, seg_dest, rec_id, conv_weight, conv_bias, proj_weight, smooth_kernel
):
    group_size = lax.axis_size("wide")
    total_rows = SEG_DEV * group_size
    packed = embed_slots(frames, seg_start, seg_dest, rec_id, conv_weight, conv_bias, proj_weight)
    slots = seg_start.shape[0]
    blocks, source = gather_wide(packed, group_size)
    per_block = slots
    all_emb = blocks[:, :slots, :].reshape(group_size * slots, EMB)
    meta_all = blocks[:, slots:, :].reshape(group_size, -1)[:, : 2 * slots]
    all_dest = meta_all[:, :slots].reshape(-1).astype(jnp.int32)
    all_rec = meta_all[:, slots:].reshape(-1).astype(jnp.int32)
    slot_ids = (
        source[:, None] * per_block + jnp.arange(per_block, dtype=jnp.int32)[None, :]
    ).reshape(-1)
    slot_total = all_dest.shape[0]
    used = all_dest >= 0

    mean_sum = jnp.sum(jnp.where(used[:, None], all_emb, 0.0), axis=0)
    centred = all_emb - mean_sum / total_rows
    unit = (centred / jnp.sqrt(jnp.sum(centred * centred, axis=1, keepdims=True) + 1e-06)).astype(
        jnp.bfloat16
    )

    earlier = (slot_ids[None, :] < slot_ids[:, None]) & (all_dest[None, :] == all_dest[:, None])
    rank = jnp.sum(earlier.astype(jnp.int32), axis=1)
    position = jnp.where(used, all_dest * SEG_DEV + rank, -1)
    picks = position[None, :] == jnp.arange(total_rows, dtype=jnp.int32)[:, None]
    row_ids = jnp.arange(slot_total, dtype=jnp.int32)
    slot_of_pos = jnp.sum(jnp.where(picks, row_ids[None, :], 0), axis=1)

    if total_rows * slot_total <= ONE_HOT_LIMIT:
        selector = picks.astype(jnp.bfloat16)
        col_unit = jnp.dot(selector, unit, preferred_element_type=jnp.float32).astype(jnp.bfloat16)
        col_rec = jnp.sum(jnp.where(picks, all_rec[None, :], 0), axis=1)
    else:
        col_unit = jnp.take(unit, slot_of_pos, axis=0)
        col_rec = jnp.take(all_rec, slot_of_pos, axis=0)
    zero_unit = jnp.zeros((1, EMB), jnp.bfloat16)
    pad_unit = jnp.concatenate([zero_unit, col_unit, zero_unit], axis=0)
    pad_rec = jnp.concatenate([jnp.full((1,), -1, jnp.int32), col_rec, jnp.full((1,), -1, jnp.int32)])
    my_index = lax.axis_index("wide")
    row_unit = lax.dynamic_slice_in_dim(pad_unit, my_index * SEG_DEV, SEG_DEV + 2, 0)
    row_rec = lax.dynamic_slice_in_dim(pad_rec, my_index * SEG_DEV, SEG_DEV + 2, 0)
    return smooth_affinity(row_unit, col_unit, row_rec, col_rec, smooth_kernel)


def solution(mesh):
    in_specs = (
        P(("parts", "wide"), None),
        P(("parts", "wide")),
        P(("parts", "wide")),
        P(("parts", "wide")),
        P(),
        P(),
        P(),
        P(),
    )
    out_specs = P(("parts", "wide"), None)
    return jax.shard_map(
        per_device, mesh=mesh, in_specs=in_specs, out_specs=out_specs, check_vma=False
    )
```

```python
import functools

import jax
import jax.numpy as jnp
from jax import lax
from jax.experimental import pallas as pl
from jax.experimental.pallas import tpu as pltpu
from jax.sharding import PartitionSpec as P

FEAT = 80
CH = 1024
EMB = 192
SEGLEN = 64
SEG_DEV = 32


PRECISE = lax.Precision.HIGHEST
AFF_SCALE = 8.0
SEG_BLOCK = 16
WIN = SEGLEN + 8
CONV_ROWS = 1024
ONE_HOT_LIMIT = 1 << 20


def _pool_kernel(
    starts_ref, frames_hbm, w_hbm, b_ref, proj_hbm, meta_ref, out_ref,
    frames_ref, w_ref, proj_ref, pooled_ref, x3_ref, act_ref, sem
):
    rows = frames_ref.shape[0]
    slots = pooled_ref.shape[0]
    frames_copy = pltpu.make_async_copy(frames_hbm, frames_ref, sem.at[0])
    w_copy = pltpu.make_async_copy(w_hbm, w_ref, sem.at[1])
    proj_copy = pltpu.make_async_copy(proj_hbm, proj_ref, sem.at[2])
    frames_copy.start()
    w_copy.start()
    proj_copy.start()
    frames_copy.wait()
    frames = frames_ref[...]
    x3_ref[...] = jnp.concatenate(
        [pltpu.roll(frames, 1, 0), frames, pltpu.roll(frames, rows - 1, 0)], axis=1
    )
    chunk = CONV_ROWS if rows % CONV_ROWS == 0 else rows
    w_copy.wait()

    def conv_chunk(c, carry):
        base = pl.multiple_of(c * chunk, chunk)
        preact = jnp.dot(
            x3_ref[pl.ds(base, chunk), :],
            w_ref[...],
            precision=PRECISE,
            preferred_element_type=jnp.float32,
        )
        act_ref[pl.ds(base, chunk), :] = jnp.maximum(preact + b_ref[...], 0.0)
        return carry

    lax.fori_loop(0, rows // chunk, conv_chunk, 0)
    frame_idx = lax.broadcasted_iota(jnp.int32, (WIN, CH), 0)

    def stats_block(blk, carry):
        means = []
        stds = []
        for j in range(SEG_BLOCK):
            start = starts_ref[blk * SEG_BLOCK + j]
            base = jnp.minimum((start // 8) * 8, rows - WIN)
            shift = start - base
            inside = (frame_idx >= shift) & (frame_idx < shift + SEGLEN)
            seg_act = act_ref[pl.ds(pl.multiple_of(base, 8), WIN), :]
            frame_mean = jnp.sum(jnp.where(inside, seg_act, 0.0), axis=0, keepdims=True) / SEGLEN
            deviation = jnp.where(inside, seg_act - frame_mean, 0.0)
            frame_var = jnp.sum(deviation * deviation, axis=0, keepdims=True) / SEGLEN
            means.append(frame_mean)
            stds.append(jnp.sqrt(frame_var + 1e-05))
        row0 = pl.multiple_of(blk * SEG_BLOCK, SEG_BLOCK)
        pooled_ref[pl.ds(row0, SEG_BLOCK), :CH] = jnp.concatenate(means, axis=0)
        pooled_ref[pl.ds(row0, SEG_BLOCK), CH:] = jnp.concatenate(stds, axis=0)
        return carry

    lax.fori_loop(0, slots // SEG_BLOCK, stats_block, 0)
    proj_copy.wait()
    out_ref[:slots, :] = lax.dot_general(
        pooled_ref[...],
        proj_ref[...],
        (((1,), (1,)), ((), ())),
        precision=PRECISE,
        preferred_element_type=jnp.float32,
    )
    out_ref[slots:, :] = meta_ref[...]


def embed_slots(frames, seg_start, seg_dest, rec_id, conv_weight, conv_bias, proj_weight):
    rows = frames.shape[0]
    slots = seg_start.shape[0]
    starts = jnp.clip(seg_start, 0, rows - SEGLEN).astype(jnp.int32)
    meta = jnp.concatenate([seg_dest.astype(jnp.float32), rec_id.astype(jnp.float32)])
    meta_len = -(-meta.shape[0] // EMB) * EMB
    meta_rows = jnp.pad(meta, (0, meta_len - meta.shape[0])).reshape(-1, EMB)
    meta_rows = jnp.pad(meta_rows, ((0, -(-meta_rows.shape[0] // 8) * 8 - meta_rows.shape[0]), (0, 0)))
    vmem = pltpu.MemorySpace.VMEM
    hbm = pltpu.MemorySpace.HBM
    return pl.pallas_call(
        _pool_kernel,
        out_shape=jax.ShapeDtypeStruct((slots + meta_rows.shape[0], EMB), jnp.float32),
        in_specs=[
            pl.BlockSpec(memory_space=pltpu.MemorySpace.SMEM),
            pl.BlockSpec(memory_space=pl.ANY),
            pl.BlockSpec(memory_space=pl.ANY),
            pl.BlockSpec(memory_space=vmem),
            pl.BlockSpec(memory_space=pl.ANY),
            pl.BlockSpec(memory_space=vmem),
        ],
        out_specs=pl.BlockSpec(memory_space=vmem),
        scratch_shapes=[
            pltpu.VMEM((rows, FEAT), jnp.float32),
            pltpu.VMEM((3 * FEAT, CH), jnp.float32),
            pltpu.VMEM((EMB, 2 * CH), jnp.float32),
            pltpu.VMEM((slots, 2 * CH), jnp.float32),
            pltpu.VMEM((rows, 3 * FEAT), jnp.float32),
            pltpu.VMEM((rows, CH), jnp.float32),
            pltpu.SemaphoreType.DMA((3,)),
        ],
        compiler_params=pltpu.CompilerParams(vmem_limit_bytes=48 * 1024 * 1024),
        cost_estimate=pl.CostEstimate(
            flops=2 * rows * 3 * FEAT * CH * 6 + 8 * slots * WIN * CH + 2 * slots * 2 * CH * EMB * 6,
            transcendentals=slots * CH,
            bytes_accessed=rows * FEAT * 4 + 3 * FEAT * CH * 4 + 2 * CH * EMB * 4 + slots * EMB * 4,
        ),
    )(
        starts,
        frames,
        pltpu.with_memory_space_constraint(conv_weight, hbm),
        conv_bias.reshape(1, CH),
        pltpu.with_memory_space_constraint(proj_weight.T, hbm),
        meta_rows,
    )


def _affinity_kernel(k_ref, row_unit_ref, col_unit_ref, row_rec_ref, col_rec_ref, out_ref, pad_ref):
    height, width = out_ref.shape
    scores = lax.dot_general(
        row_unit_ref[...],
        col_unit_ref[...],
        (((1,), (1,)), ((), ())),
        preferred_element_type=jnp.float32,
    )
    affinity = jnp.where(row_rec_ref[...] == col_rec_ref[...], 0.0, AFF_SCALE * scores)
    pad_ref[...] = jnp.zeros(pad_ref.shape, jnp.float32)
    pad_ref[0 : height + 2, 1 : width + 1] = affinity
    result = jnp.zeros((height, width), jnp.float32)
    for row_off in range(3):
        for col_off in range(3):
            result = result + k_ref[row_off, col_off] * pad_ref[
                row_off : row_off + height, col_off : col_off + width
            ]
    out_ref[...] = result


def smooth_affinity(row_unit, col_unit, row_rec, col_rec, smooth_kernel):
    height = row_unit.shape[0] - 2
    width = col_unit.shape[0]
    vmem = pltpu.MemorySpace.VMEM
    return pl.pallas_call(
        _affinity_kernel,
        out_shape=jax.ShapeDtypeStruct((height, width), jnp.float32),
        in_specs=[pl.BlockSpec(memory_space=pltpu.MemorySpace.SMEM)]
        + [pl.BlockSpec(memory_space=vmem)] * 4,
        out_specs=pl.BlockSpec(memory_space=vmem),
        scratch_shapes=[
            pltpu.VMEM((-(-(height + 2) // 8) * 8, -(-(width + 2) // 128) * 128), jnp.float32)
        ],
        compiler_params=pltpu.CompilerParams(vmem_limit_bytes=48 * 1024 * 1024),
        cost_estimate=pl.CostEstimate(
            flops=2 * (height + 2) * width * EMB + 20 * height * width,
            transcendentals=0,
            bytes_accessed=(width + height + 2) * EMB * 2 + height * width * 4,
        ),
    )(smooth_kernel, row_unit, col_unit, row_rec.reshape(-1, 1), col_rec.reshape(1, -1))


def gather_wide(x, group_size):
    my_index = lax.axis_index("wide")
    if group_size & (group_size - 1):
        every = lax.all_gather(x, "wide", axis=0, tiled=False)
        return every, jnp.arange(group_size, dtype=jnp.int32)
    pattern = [0]
    buf = x[None]
    bit = group_size.bit_length() - 2
    while bit >= 0:
        if bit >= 2:
            flips = [m << (bit - 1) for m in (1, 2, 3)]
            bit -= 2
        else:
            flips = [1 << bit]
            bit -= 1
        received = [
            lax.ppermute(buf, "wide", [(i, i ^ f) for i in range(group_size)]) for f in flips
        ]
        buf = jnp.concatenate([buf] + received, axis=0)
        pattern = pattern + [p ^ f for f in flips for p in pattern]
    source = jnp.asarray(pattern, dtype=jnp.int32) ^ my_index
    return buf, source


def per_device(
    frames, seg_start, seg_dest, rec_id, conv_weight, conv_bias, proj_weight, smooth_kernel
):
    group_size = lax.axis_size("wide")
    total_rows = SEG_DEV * group_size
    packed = embed_slots(frames, seg_start, seg_dest, rec_id, conv_weight, conv_bias, proj_weight)
    slots = seg_start.shape[0]
    blocks, source = gather_wide(packed, group_size)
    per_block = slots
    all_emb = blocks[:, :slots, :].reshape(group_size * slots, EMB)
    meta_all = blocks[:, slots:, :].reshape(group_size, -1)[:, : 2 * slots]
    all_dest = meta_all[:, :slots].reshape(-1).astype(jnp.int32)
    all_rec = meta_all[:, slots:].reshape(-1).astype(jnp.int32)
    slot_ids = (
        source[:, None] * per_block + jnp.arange(per_block, dtype=jnp.int32)[None, :]
    ).reshape(-1)
    slot_total = all_dest.shape[0]
    used = all_dest >= 0

    mean_sum = jnp.sum(jnp.where(used[:, None], all_emb, 0.0), axis=0)
    centred = all_emb - mean_sum / total_rows
    unit = (centred / jnp.sqrt(jnp.sum(centred * centred, axis=1, keepdims=True) + 1e-06)).astype(
        jnp.bfloat16
    )

    earlier = (slot_ids[None, :] < slot_ids[:, None]) & (all_dest[None, :] == all_dest[:, None])
    rank = jnp.sum(earlier.astype(jnp.int32), axis=1)
    position = jnp.where(used, all_dest * SEG_DEV + rank, -1)
    picks = position[None, :] == jnp.arange(total_rows, dtype=jnp.int32)[:, None]
    row_ids = jnp.arange(slot_total, dtype=jnp.int32)
    slot_of_pos = jnp.sum(jnp.where(picks, row_ids[None, :], 0), axis=1)

    if total_rows * slot_total <= ONE_HOT_LIMIT:
        selector = picks.astype(jnp.bfloat16)
        col_unit = jnp.dot(selector, unit, preferred_element_type=jnp.float32).astype(jnp.bfloat16)
        col_rec = jnp.sum(jnp.where(picks, all_rec[None, :], 0), axis=1)
    else:
        col_unit = jnp.take(unit, slot_of_pos, axis=0)
        col_rec = jnp.take(all_rec, slot_of_pos, axis=0)
    zero_unit = jnp.zeros((1, EMB), jnp.bfloat16)
    pad_unit = jnp.concatenate([zero_unit, col_unit, zero_unit], axis=0)
    pad_rec = jnp.concatenate([jnp.full((1,), -1, jnp.int32), col_rec, jnp.full((1,), -1, jnp.int32)])
    my_index = lax.axis_index("wide")
    row_unit = lax.dynamic_slice_in_dim(pad_unit, my_index * SEG_DEV, SEG_DEV + 2, 0)
    row_rec = lax.dynamic_slice_in_dim(pad_rec, my_index * SEG_DEV, SEG_DEV + 2, 0)
    return smooth_affinity(row_unit, col_unit, row_rec, col_rec, smooth_kernel)


def solution(mesh):
    in_specs = (
        P(("parts", "wide"), None),
        P(("parts", "wide")),
        P(("parts", "wide")),
        P(("parts", "wide")),
        P(),
        P(),
        P(),
        P(),
    )
    out_specs = P(("parts", "wide"), None)
    return jax.shard_map(
        per_device, mesh=mesh, in_specs=in_specs, out_specs=out_specs, check_vma=False
    )
```

```python
import functools

import jax
import jax.numpy as jnp
from jax import lax
from jax.experimental import pallas as pl
from jax.experimental.pallas import tpu as pltpu
from jax.sharding import PartitionSpec as P

FEAT = 80
CH = 1024
EMB = 192
SEGLEN = 64
SEG_DEV = 32


PRECISE = lax.Precision.HIGHEST
AFF_SCALE = 8.0
SEG_BLOCK = 8
WIN = SEGLEN + 8
CONV_ROWS = 1024
ONE_HOT_LIMIT = 1 << 20


def _pool_kernel(
    starts_ref, frames_hbm, w_hbm, b_ref, proj_hbm, meta_ref, out_ref,
    frames_ref, w_ref, proj_ref, pooled_ref, x3_ref, act_ref, sem
):
    rows = frames_ref.shape[0]
    slots = pooled_ref.shape[0]
    frames_copy = pltpu.make_async_copy(frames_hbm, frames_ref, sem.at[0])
    w_copy = pltpu.make_async_copy(w_hbm, w_ref, sem.at[1])
    proj_copy = pltpu.make_async_copy(proj_hbm, proj_ref, sem.at[2])
    frames_copy.start()
    w_copy.start()
    proj_copy.start()
    frames_copy.wait()
    frames = frames_ref[...]
    x3_ref[...] = jnp.concatenate(
        [pltpu.roll(frames, 1, 0), frames, pltpu.roll(frames, rows - 1, 0)], axis=1
    )
    chunk = CONV_ROWS if rows % CONV_ROWS == 0 else rows
    w_copy.wait()

    def conv_chunk(c, carry):
        base = pl.multiple_of(c * chunk, chunk)
        preact = jnp.dot(
            x3_ref[pl.ds(base, chunk), :],
            w_ref[...],
            precision=PRECISE,
            preferred_element_type=jnp.float32,
        )
        act_ref[pl.ds(base, chunk), :] = jnp.maximum(preact + b_ref[...], 0.0)
        return carry

    lax.fori_loop(0, rows // chunk, conv_chunk, 0)
    frame_idx = lax.broadcasted_iota(jnp.int32, (WIN, CH), 0)

    def stats_block(blk, carry):
        means = []
        stds = []
        for j in range(SEG_BLOCK):
            start = jnp.clip(starts_ref[blk * SEG_BLOCK + j], 0, rows - SEGLEN)
            base = jnp.minimum((start // 8) * 8, rows - WIN)
            shift = start - base
            inside = (frame_idx >= shift) & (frame_idx < shift + SEGLEN)
            seg_act = act_ref[pl.ds(pl.multiple_of(base, 8), WIN), :]
            frame_mean = jnp.sum(jnp.where(inside, seg_act, 0.0), axis=0, keepdims=True) / SEGLEN
            deviation = jnp.where(inside, seg_act - frame_mean, 0.0)
            frame_var = jnp.sum(deviation * deviation, axis=0, keepdims=True) / SEGLEN
            means.append(frame_mean)
            stds.append(jnp.sqrt(frame_var + 1e-05))
        row0 = pl.multiple_of(blk * SEG_BLOCK, SEG_BLOCK)
        pooled_ref[pl.ds(row0, SEG_BLOCK), :CH] = jnp.concatenate(means, axis=0)
        pooled_ref[pl.ds(row0, SEG_BLOCK), CH:] = jnp.concatenate(stds, axis=0)
        return carry

    lax.fori_loop(0, slots // SEG_BLOCK, stats_block, 0)
    proj_copy.wait()
    out_ref[:slots, :] = lax.dot_general(
        pooled_ref[...],
        proj_ref[...],
        (((1,), (1,)), ((), ())),
        precision=PRECISE,
        preferred_element_type=jnp.float32,
    )
    out_ref[slots:, :] = meta_ref[...]


def embed_slots(frames, seg_start, seg_dest, rec_id, conv_weight, conv_bias, proj_weight):
    rows = frames.shape[0]
    slots = seg_start.shape[0]
    starts = seg_start.astype(jnp.int32)
    meta = jnp.concatenate([seg_dest.astype(jnp.float32), rec_id.astype(jnp.float32)])
    meta_len = -(-meta.shape[0] // EMB) * EMB
    meta_rows = jnp.pad(meta, (0, meta_len - meta.shape[0])).reshape(-1, EMB)
    meta_rows = jnp.pad(meta_rows, ((0, -(-meta_rows.shape[0] // 8) * 8 - meta_rows.shape[0]), (0, 0)))
    vmem = pltpu.MemorySpace.VMEM
    hbm = pltpu.MemorySpace.HBM
    return pl.pallas_call(
        _pool_kernel,
        out_shape=jax.ShapeDtypeStruct((slots + meta_rows.shape[0], EMB), jnp.float32),
        in_specs=[
            pl.BlockSpec(memory_space=pltpu.MemorySpace.SMEM),
            pl.BlockSpec(memory_space=pl.ANY),
            pl.BlockSpec(memory_space=pl.ANY),
            pl.BlockSpec(memory_space=vmem),
            pl.BlockSpec(memory_space=pl.ANY),
            pl.BlockSpec(memory_space=vmem),
        ],
        out_specs=pl.BlockSpec(memory_space=vmem),
        scratch_shapes=[
            pltpu.VMEM((rows, FEAT), jnp.float32),
            pltpu.VMEM((3 * FEAT, CH), jnp.float32),
            pltpu.VMEM((EMB, 2 * CH), jnp.float32),
            pltpu.VMEM((slots, 2 * CH), jnp.float32),
            pltpu.VMEM((rows, 3 * FEAT), jnp.float32),
            pltpu.VMEM((rows, CH), jnp.float32),
            pltpu.SemaphoreType.DMA((3,)),
        ],
        compiler_params=pltpu.CompilerParams(vmem_limit_bytes=48 * 1024 * 1024),
        cost_estimate=pl.CostEstimate(
            flops=2 * rows * 3 * FEAT * CH * 6 + 8 * slots * WIN * CH + 2 * slots * 2 * CH * EMB * 6,
            transcendentals=slots * CH,
            bytes_accessed=rows * FEAT * 4 + 3 * FEAT * CH * 4 + 2 * CH * EMB * 4 + slots * EMB * 4,
        ),
    )(
        starts,
        frames,
        pltpu.with_memory_space_constraint(conv_weight, hbm),
        conv_bias.reshape(1, CH),
        pltpu.with_memory_space_constraint(proj_weight.T, hbm),
        meta_rows,
    )


def _affinity_kernel(k_ref, row_unit_ref, col_unit_ref, row_rec_ref, col_rec_ref, out_ref, pad_ref):
    height, width = out_ref.shape
    scores = lax.dot_general(
        row_unit_ref[...],
        col_unit_ref[...],
        (((1,), (1,)), ((), ())),
        preferred_element_type=jnp.float32,
    )
    affinity = jnp.where(row_rec_ref[...] == col_rec_ref[...], 0.0, AFF_SCALE * scores)
    pad_ref[...] = jnp.zeros(pad_ref.shape, jnp.float32)
    pad_ref[0 : height + 2, 1 : width + 1] = affinity
    result = jnp.zeros((height, width), jnp.float32)
    for row_off in range(3):
        for col_off in range(3):
            result = result + k_ref[row_off, col_off] * pad_ref[
                row_off : row_off + height, col_off : col_off + width
            ]
    out_ref[...] = result


def smooth_affinity(row_unit, col_unit, row_rec, col_rec, smooth_kernel):
    height = row_unit.shape[0] - 2
    width = col_unit.shape[0]
    vmem = pltpu.MemorySpace.VMEM
    return pl.pallas_call(
        _affinity_kernel,
        out_shape=jax.ShapeDtypeStruct((height, width), jnp.float32),
        in_specs=[pl.BlockSpec(memory_space=pltpu.MemorySpace.SMEM)]
        + [pl.BlockSpec(memory_space=vmem)] * 4,
        out_specs=pl.BlockSpec(memory_space=vmem),
        scratch_shapes=[
            pltpu.VMEM((-(-(height + 2) // 8) * 8, -(-(width + 2) // 128) * 128), jnp.float32)
        ],
        compiler_params=pltpu.CompilerParams(vmem_limit_bytes=48 * 1024 * 1024),
        cost_estimate=pl.CostEstimate(
            flops=2 * (height + 2) * width * EMB + 20 * height * width,
            transcendentals=0,
            bytes_accessed=(width + height + 2) * EMB * 2 + height * width * 4,
        ),
    )(smooth_kernel, row_unit, col_unit, row_rec.reshape(-1, 1), col_rec.reshape(1, -1))


def gather_wide(x, group_size):
    my_index = lax.axis_index("wide")
    if group_size & (group_size - 1):
        every = lax.all_gather(x, "wide", axis=0, tiled=False)
        return every, jnp.arange(group_size, dtype=jnp.int32)
    pattern = [0]
    buf = x[None]
    bit = group_size.bit_length() - 2
    while bit >= 0:
        if bit >= 2:
            flips = [m << (bit - 1) for m in (1, 2, 3)]
            bit -= 2
        else:
            flips = [1 << bit]
            bit -= 1
        received = [
            lax.ppermute(buf, "wide", [(i, i ^ f) for i in range(group_size)]) for f in flips
        ]
        buf = jnp.concatenate([buf] + received, axis=0)
        pattern = pattern + [p ^ f for f in flips for p in pattern]
    source = jnp.asarray(pattern, dtype=jnp.int32) ^ my_index
    return buf, source


def per_device(
    frames, seg_start, seg_dest, rec_id, conv_weight, conv_bias, proj_weight, smooth_kernel
):
    group_size = lax.axis_size("wide")
    total_rows = SEG_DEV * group_size
    packed = embed_slots(frames, seg_start, seg_dest, rec_id, conv_weight, conv_bias, proj_weight)
    slots = seg_start.shape[0]
    blocks, source = gather_wide(packed, group_size)
    per_block = slots
    all_emb = blocks[:, :slots, :].reshape(group_size * slots, EMB)
    meta_all = blocks[:, slots:, :].reshape(group_size, -1)[:, : 2 * slots]
    all_dest = meta_all[:, :slots].reshape(-1).astype(jnp.int32)
    all_rec = meta_all[:, slots:].reshape(-1).astype(jnp.int32)
    slot_ids = (
        source[:, None] * per_block + jnp.arange(per_block, dtype=jnp.int32)[None, :]
    ).reshape(-1)
    slot_total = all_dest.shape[0]
    used = all_dest >= 0

    mean_sum = jnp.sum(jnp.where(used[:, None], all_emb, 0.0), axis=0)
    centred = all_emb - mean_sum / total_rows
    unit = (centred / jnp.sqrt(jnp.sum(centred * centred, axis=1, keepdims=True) + 1e-06)).astype(
        jnp.bfloat16
    )

    earlier = (slot_ids[None, :] < slot_ids[:, None]) & (all_dest[None, :] == all_dest[:, None])
    rank = jnp.sum(earlier.astype(jnp.int32), axis=1)
    position = jnp.where(used, all_dest * SEG_DEV + rank, -1)
    picks = position[None, :] == jnp.arange(total_rows, dtype=jnp.int32)[:, None]
    row_ids = jnp.arange(slot_total, dtype=jnp.int32)
    slot_of_pos = jnp.sum(jnp.where(picks, row_ids[None, :], 0), axis=1)

    if total_rows * slot_total <= ONE_HOT_LIMIT:
        selector = picks.astype(jnp.bfloat16)
        col_unit = jnp.dot(selector, unit, preferred_element_type=jnp.float32).astype(jnp.bfloat16)
        col_rec = jnp.sum(jnp.where(picks, all_rec[None, :], 0), axis=1)
    else:
        col_unit = jnp.take(unit, slot_of_pos, axis=0)
        col_rec = jnp.take(all_rec, slot_of_pos, axis=0)
    zero_unit = jnp.zeros((1, EMB), jnp.bfloat16)
    pad_unit = jnp.concatenate([zero_unit, col_unit, zero_unit], axis=0)
    pad_rec = jnp.concatenate([jnp.full((1,), -1, jnp.int32), col_rec, jnp.full((1,), -1, jnp.int32)])
    my_index = lax.axis_index("wide")
    row_unit = lax.dynamic_slice_in_dim(pad_unit, my_index * SEG_DEV, SEG_DEV + 2, 0)
    row_rec = lax.dynamic_slice_in_dim(pad_rec, my_index * SEG_DEV, SEG_DEV + 2, 0)
    return smooth_affinity(row_unit, col_unit, row_rec, col_rec, smooth_kernel)


def solution(mesh):
    in_specs = (
        P(("parts", "wide"), None),
        P(("parts", "wide")),
        P(("parts", "wide")),
        P(("parts", "wide")),
        P(),
        P(),
        P(),
        P(),
    )
    out_specs = P(("parts", "wide"), None)
    return jax.shard_map(
        per_device, mesh=mesh, in_specs=in_specs, out_specs=out_specs, check_vma=False
    )
```

```python
import functools

import jax
import jax.numpy as jnp
from jax import lax
from jax.experimental import pallas as pl
from jax.experimental.pallas import tpu as pltpu
from jax.sharding import PartitionSpec as P

FEAT = 80
CH = 1024
EMB = 192
SEGLEN = 64
SEG_DEV = 32


PRECISE = lax.Precision.HIGHEST
AFF_SCALE = 8.0
SEG_BLOCK = 8
WIN = SEGLEN + 8
CONV_ROWS = 1024
ONE_HOT_LIMIT = 1 << 20


def _pool_kernel(
    starts_ref, frames_hbm, w_hbm, b_ref, proj_hbm, meta_ref, out_ref,
    frames_ref, w_ref, proj_ref, pooled_ref, x3_ref, act_ref, sem
):
    rows = frames_ref.shape[0]
    slots = pooled_ref.shape[0]
    frames_copy = pltpu.make_async_copy(frames_hbm, frames_ref, sem.at[0])
    w_copy = pltpu.make_async_copy(w_hbm, w_ref, sem.at[1])
    proj_copy = pltpu.make_async_copy(proj_hbm, proj_ref, sem.at[2])
    frames_copy.start()
    w_copy.start()
    proj_copy.start()
    frames_copy.wait()
    frames = frames_ref[...]
    x3_ref[...] = jnp.concatenate(
        [pltpu.roll(frames, 1, 0), frames, pltpu.roll(frames, rows - 1, 0)], axis=1
    )
    chunk = CONV_ROWS if rows % CONV_ROWS == 0 else rows
    w_copy.wait()

    def conv_chunk(c, carry):
        base = pl.multiple_of(c * chunk, chunk)
        preact = jnp.dot(
            x3_ref[pl.ds(base, chunk), :],
            w_ref[...],
            precision=PRECISE,
            preferred_element_type=jnp.float32,
        )
        act_ref[pl.ds(base, chunk), :] = jnp.maximum(preact + b_ref[...], 0.0)
        return carry

    lax.fori_loop(0, rows // chunk, conv_chunk, 0)
    frame_idx = lax.broadcasted_iota(jnp.int32, (WIN, CH), 0)

    def stats_block(blk, carry):
        means = []
        stds = []
        for j in range(SEG_BLOCK):
            start = jnp.clip(starts_ref[blk * SEG_BLOCK + j], 0, rows - SEGLEN)
            base = jnp.minimum((start // 8) * 8, rows - WIN)
            shift = start - base
            inside = (frame_idx >= shift) & (frame_idx < shift + SEGLEN)
            seg_act = act_ref[pl.ds(pl.multiple_of(base, 8), WIN), :]
            frame_mean = jnp.sum(jnp.where(inside, seg_act, 0.0), axis=0, keepdims=True) / SEGLEN
            deviation = jnp.where(inside, seg_act - frame_mean, 0.0)
            frame_var = jnp.sum(deviation * deviation, axis=0, keepdims=True) / SEGLEN
            means.append(frame_mean)
            stds.append(jnp.sqrt(frame_var + 1e-05))
        row0 = pl.multiple_of(blk * SEG_BLOCK, SEG_BLOCK)
        pooled_ref[pl.ds(row0, SEG_BLOCK), :CH] = jnp.concatenate(means, axis=0)
        pooled_ref[pl.ds(row0, SEG_BLOCK), CH:] = jnp.concatenate(stds, axis=0)
        return carry

    lax.fori_loop(0, slots // SEG_BLOCK, stats_block, 0)
    proj_copy.wait()
    out_ref[:slots, :] = lax.dot_general(
        pooled_ref[...],
        proj_ref[...],
        (((1,), (1,)), ((), ())),
        precision=PRECISE,
        preferred_element_type=jnp.float32,
    )
    out_ref[slots:, :] = meta_ref[...]


def embed_slots(frames, seg_start, seg_dest, rec_id, conv_weight, conv_bias, proj_weight):
    rows = frames.shape[0]
    slots = seg_start.shape[0]
    starts = seg_start.astype(jnp.int32)
    meta = jnp.concatenate([seg_dest.astype(jnp.float32), rec_id.astype(jnp.float32)])
    meta_len = -(-meta.shape[0] // EMB) * EMB
    meta_rows = jnp.pad(meta, (0, meta_len - meta.shape[0])).reshape(-1, EMB)
    meta_rows = jnp.pad(meta_rows, ((0, -(-meta_rows.shape[0] // 8) * 8 - meta_rows.shape[0]), (0, 0)))
    vmem = pltpu.MemorySpace.VMEM
    hbm = pltpu.MemorySpace.HBM
    return pl.pallas_call(
        _pool_kernel,
        out_shape=jax.ShapeDtypeStruct((slots + meta_rows.shape[0], EMB), jnp.float32),
        in_specs=[
            pl.BlockSpec(memory_space=pltpu.MemorySpace.SMEM),
            pl.BlockSpec(memory_space=pl.ANY),
            pl.BlockSpec(memory_space=pl.ANY),
            pl.BlockSpec(memory_space=vmem),
            pl.BlockSpec(memory_space=pl.ANY),
            pl.BlockSpec(memory_space=vmem),
        ],
        out_specs=pl.BlockSpec(memory_space=vmem),
        scratch_shapes=[
            pltpu.VMEM((rows, FEAT), jnp.float32),
            pltpu.VMEM((3 * FEAT, CH), jnp.float32),
            pltpu.VMEM((EMB, 2 * CH), jnp.float32),
            pltpu.VMEM((slots, 2 * CH), jnp.float32),
            pltpu.VMEM((rows, 3 * FEAT), jnp.float32),
            pltpu.VMEM((rows, CH), jnp.float32),
            pltpu.SemaphoreType.DMA((3,)),
        ],
        compiler_params=pltpu.CompilerParams(vmem_limit_bytes=48 * 1024 * 1024),
        cost_estimate=pl.CostEstimate(
            flops=2 * rows * 3 * FEAT * CH * 6 + 8 * slots * WIN * CH + 2 * slots * 2 * CH * EMB * 6,
            transcendentals=slots * CH,
            bytes_accessed=rows * FEAT * 4 + 3 * FEAT * CH * 4 + 2 * CH * EMB * 4 + slots * EMB * 4,
        ),
    )(
        starts,
        frames,
        pltpu.with_memory_space_constraint(conv_weight, hbm),
        conv_bias.reshape(1, CH),
        pltpu.with_memory_space_constraint(proj_weight.T, hbm),
        meta_rows,
    )


def _affinity_kernel(k_ref, row_unit_ref, col_unit_ref, row_rec_ref, col_rec_ref, out_ref, pad_ref):
    height, width = out_ref.shape
    scores = lax.dot_general(
        row_unit_ref[...],
        col_unit_ref[...],
        (((1,), (1,)), ((), ())),
        preferred_element_type=jnp.float32,
    )
    affinity = jnp.where(row_rec_ref[...] == col_rec_ref[...], 0.0, AFF_SCALE * scores)
    pad_ref[...] = jnp.zeros(pad_ref.shape, jnp.float32)
    pad_ref[0 : height + 2, 1 : width + 1] = affinity
    result = jnp.zeros((height, width), jnp.float32)
    for row_off in range(3):
        for col_off in range(3):
            result = result + k_ref[row_off, col_off] * pad_ref[
                row_off : row_off + height, col_off : col_off + width
            ]
    out_ref[...] = result


def smooth_affinity(row_unit, col_unit, row_rec, col_rec, smooth_kernel):
    height = row_unit.shape[0] - 2
    width = col_unit.shape[0]
    vmem = pltpu.MemorySpace.VMEM
    return pl.pallas_call(
        _affinity_kernel,
        out_shape=jax.ShapeDtypeStruct((height, width), jnp.float32),
        in_specs=[pl.BlockSpec(memory_space=pltpu.MemorySpace.SMEM)]
        + [pl.BlockSpec(memory_space=vmem)] * 4,
        out_specs=pl.BlockSpec(memory_space=vmem),
        scratch_shapes=[
            pltpu.VMEM((-(-(height + 2) // 8) * 8, -(-(width + 2) // 128) * 128), jnp.float32)
        ],
        compiler_params=pltpu.CompilerParams(vmem_limit_bytes=48 * 1024 * 1024),
        cost_estimate=pl.CostEstimate(
            flops=2 * (height + 2) * width * EMB + 20 * height * width,
            transcendentals=0,
            bytes_accessed=(width + height + 2) * EMB * 2 + height * width * 4,
        ),
    )(smooth_kernel, row_unit, col_unit, row_rec.reshape(-1, 1), col_rec.reshape(1, -1))


def gather_wide(x, group_size):
    my_index = lax.axis_index("wide")
    if group_size & (group_size - 1):
        every = lax.all_gather(x, "wide", axis=0, tiled=False)
        return every, jnp.arange(group_size, dtype=jnp.int32)
    pattern = [0]
    buf = x[None]
    bit = group_size.bit_length() - 2
    while bit >= 0:
        if bit >= 2:
            flips = [m << (bit - 1) for m in (3, 2, 1)]
            bit -= 2
        else:
            flips = [1 << bit]
            bit -= 1
        received = [
            lax.ppermute(buf, "wide", [(i, i ^ f) for i in range(group_size)]) for f in flips
        ]
        buf = jnp.concatenate([buf] + received, axis=0)
        pattern = pattern + [p ^ f for f in flips for p in pattern]
    source = jnp.asarray(pattern, dtype=jnp.int32) ^ my_index
    return buf, source


def per_device(
    frames, seg_start, seg_dest, rec_id, conv_weight, conv_bias, proj_weight, smooth_kernel
):
    group_size = lax.axis_size("wide")
    total_rows = SEG_DEV * group_size
    packed = embed_slots(frames, seg_start, seg_dest, rec_id, conv_weight, conv_bias, proj_weight)
    slots = seg_start.shape[0]
    blocks, source = gather_wide(packed, group_size)
    per_block = slots
    all_emb = blocks[:, :slots, :].reshape(group_size * slots, EMB)
    meta_all = blocks[:, slots:, :].reshape(group_size, -1)[:, : 2 * slots]
    all_dest = meta_all[:, :slots].reshape(-1).astype(jnp.int32)
    all_rec = meta_all[:, slots:].reshape(-1).astype(jnp.int32)
    slot_ids = (
        source[:, None] * per_block + jnp.arange(per_block, dtype=jnp.int32)[None, :]
    ).reshape(-1)
    slot_total = all_dest.shape[0]
    used = all_dest >= 0

    mean_sum = jnp.sum(jnp.where(used[:, None], all_emb, 0.0), axis=0)
    centred = all_emb - mean_sum / total_rows
    unit = (centred / jnp.sqrt(jnp.sum(centred * centred, axis=1, keepdims=True) + 1e-06)).astype(
        jnp.bfloat16
    )

    earlier = (slot_ids[None, :] < slot_ids[:, None]) & (all_dest[None, :] == all_dest[:, None])
    rank = jnp.sum(earlier.astype(jnp.int32), axis=1)
    position = jnp.where(used, all_dest * SEG_DEV + rank, -1)
    picks = position[None, :] == jnp.arange(total_rows, dtype=jnp.int32)[:, None]
    row_ids = jnp.arange(slot_total, dtype=jnp.int32)
    slot_of_pos = jnp.sum(jnp.where(picks, row_ids[None, :], 0), axis=1)

    if total_rows * slot_total <= ONE_HOT_LIMIT:
        selector = picks.astype(jnp.bfloat16)
        col_unit = jnp.dot(selector, unit, preferred_element_type=jnp.float32).astype(jnp.bfloat16)
        col_rec = jnp.sum(jnp.where(picks, all_rec[None, :], 0), axis=1)
    else:
        col_unit = jnp.take(unit, slot_of_pos, axis=0)
        col_rec = jnp.take(all_rec, slot_of_pos, axis=0)
    zero_unit = jnp.zeros((1, EMB), jnp.bfloat16)
    pad_unit = jnp.concatenate([zero_unit, col_unit, zero_unit], axis=0)
    pad_rec = jnp.concatenate([jnp.full((1,), -1, jnp.int32), col_rec, jnp.full((1,), -1, jnp.int32)])
    my_index = lax.axis_index("wide")
    row_unit = lax.dynamic_slice_in_dim(pad_unit, my_index * SEG_DEV, SEG_DEV + 2, 0)
    row_rec = lax.dynamic_slice_in_dim(pad_rec, my_index * SEG_DEV, SEG_DEV + 2, 0)
    return smooth_affinity(row_unit, col_unit, row_rec, col_rec, smooth_kernel)


def solution(mesh):
    in_specs = (
        P(("parts", "wide"), None),
        P(("parts", "wide")),
        P(("parts", "wide")),
        P(("parts", "wide")),
        P(),
        P(),
        P(),
        P(),
    )
    out_specs = P(("parts", "wide"), None)
    return jax.shard_map(
        per_device, mesh=mesh, in_specs=in_specs, out_specs=out_specs, check_vma=False
    )
```
